32 devices in a mesh: parts: 2 (over x), rows: 2 (over core), cols: 8 (over z, y).
Axes of the slice: x: 2, y: 2, z: 4, core: 2. Of those that a mesh axis runs over, the one named last changes fastest.
Arguments:
- src_feat: float32 [32, 131072], P(None, ('parts', 'rows', 'cols')), parts along dimension 1, may hold values from -0.75 to 0.75
- tgt_feat: float32 [32, 16384], P(None, ('parts', 'cols')), parts along dimension 1, may hold values from -0.75 to 0.75
- tgt_pot: float32 [16384], P(('parts', 'cols')), parts along dimension 0, may hold values from -25 to 25
- log_src: float32 [131072], P(('parts', 'rows', 'cols')), parts along dimension 0, may hold values from -3 to 3
- log_tgt: float32 [16384], P(('parts', 'cols')), parts along dimension 0, may hold values from -3 to 3
- pairs: int32 [512, 24], P(('parts', 'rows', 'cols')), parts along dimension 0, may hold values from 0 to 31, as said below
- counts: int32 [512], P(('parts', 'rows', 'cols')), parts along dimension 0, may hold values from 1 to 24, as said below
Outputs:
- src_pot: float32 [131072], P(('parts', 'rows', 'cols')), parts along dimension 0
- new_tgt_pot: float32 [16384], P(('parts', 'cols')), parts along dimension 0
The draws below stay inside these ranges and needn't reach their ends.
There are 2 independent parts, one for each index of `parts`. The reference program is written for one: setup_inputs(seed, part) draws one part's arguments, and reference() takes and returns one part's arrays. A program takes and returns all parts, laid end to end along the dimension named above; each array names one. Nothing has to cross between parts.
Inputs may be any that keep to these rules, and one draw needn't show every extreme that they name: `pairs`: each row names 24 different target blocks, and every target block is the first entry of some row. `counts`: row 0 uses all 24 entries and row 1 only one.
All inputs are finite; a program needn't handle non-finite values.
Results may differ from the reference program's by a relative error of at most 0.0003.
Values sent between devices are 32-bit elements; how exact they have to be, the bound alone decides.
No kernel may reach another device: no remote copies, remote signals or barrier semaphores. Data moves between devices by JAX's collectives and lax.ppermute only.
A program may use at most 128 MiB of HBM per device.

```python
import jax
import jax.numpy as jnp
from jax import lax

D = 32
BLK = 256
PAIRS = 24
RB_DEV = 16
NSB = 256
NS = 65536
NT = 8192
TBLK = 32


def draw_pairs(key, part):
    first_key, rest_key = jax.random.split(key)
    order = jax.random.permutation(first_key, TBLK).astype(jnp.int32)
    first = order[jnp.arange(NSB, dtype=jnp.int32) % TBLK]
    raw = jax.random.randint(rest_key, (NSB, TBLK - 1), 0, 1 << 20)
    ranked = raw * TBLK + jnp.arange(TBLK - 1, dtype=jnp.int32)[None, :]
    picked = lax.top_k(ranked, PAIRS - 1)[1].astype(jnp.int32) + 1
    rest = (first[:, None] + picked) % TBLK
    return jnp.concatenate([first[:, None], rest], axis=1).astype(jnp.int32)


def draw_counts(key, part):
    floor_key, row_key = jax.random.split(key)
    floor = jax.random.randint(floor_key, (NSB // RB_DEV,), 1, PAIRS + 1)
    floor = jnp.repeat(floor, RB_DEV)
    raw = jax.random.randint(row_key, (NSB,), 0, 1 << 20)
    picked = floor + raw % (PAIRS + 1 - floor)
    picked = picked.at[0].set(PAIRS).at[1].set(1)
    return picked.astype(jnp.int32)


def draw_tgt_pot(key, part):
    base_key = jax.random.fold_in(key, 0)
    values = jnp.clip(0.3 * jax.random.normal(base_key, (NT,), jnp.float32), -1.8, 1.8)
    return values.astype(jnp.float32)


def shard_levels(stream_key, shape, pieces, low, high):
    level = 1.0
    for dim, parts in pieces:
        steps = jax.random.uniform(jax.random.fold_in(jax.random.fold_in(stream_key, 6), dim), (parts,), jnp.float32, low / len(pieces), high / len(pieces))
        level = level * jnp.repeat(jnp.exp(steps), shape[dim] // parts).reshape((-1,) + (1,) * (len(shape) - 1 - dim))
    return level


def noise(rng, shape, spread, most, pieces=(), kind=jnp.bfloat16):
    array = spread * jax.random.normal(rng, shape, jnp.float32)
    if pieces:
        array = array * shard_levels(rng, shape, pieces, -0.22, 0.18)
    return jnp.clip(array, -most, most).astype(kind)


def setup_inputs(seed: int = 0, part: int = 0) -> dict:
    splits = jax.random.split(jax.random.key(seed), 8)
    own_keys = jax.random.split(jax.random.fold_in(splits[7], part), 8)
    return {
        "src_feat": noise(own_keys[0], (D, NS), 0.125, 0.75, ((1, 16),), jnp.float32),
        "tgt_feat": noise(own_keys[1], (D, NT), 0.125, 0.75, ((1, 8),), jnp.float32),
        "tgt_pot": draw_tgt_pot(jax.random.fold_in(jax.random.fold_in(splits[7], part), 71), part),
        "log_src": jnp.clip(jax.random.uniform(own_keys[3], (NS,), jnp.float32, -3.0, 3.0) * shard_levels(own_keys[3], (NS,), ((0, 16),), -0.4, 0.0), -3.0, 3.0),
        "log_tgt": jnp.clip(jax.random.uniform(own_keys[4], (NT,), jnp.float32, -3.0, 3.0) * shard_levels(own_keys[4], (NT,), ((0, 8),), -0.4, 0.0), -3.0, 3.0),
        "pairs": draw_pairs(jax.random.fold_in(jax.random.fold_in(splits[7], part), 71), part),
        "counts": draw_counts(jax.random.fold_in(jax.random.fold_in(splits[7], part), 71), part),
    }


epsilon = 0.1
NEG = -1.0e30


def block_terms(src_feat, tgt_feat, tgt_pot, log_src, log_tgt, pairs, counts, index):
    start = (index * BLK).astype(jnp.int32)
    xs = lax.dynamic_slice_in_dim(src_feat, start, BLK, 1)
    weights = lax.dynamic_slice_in_dim(log_src, start, BLK, 0)
    ids = pairs[index]
    cols = (ids[:, None] * BLK + jnp.arange(BLK, dtype=jnp.int32)[None, :]).reshape(-1)
    ys = jnp.take(tgt_feat, cols, axis=1)
    xnorm = jnp.sum(xs * xs, axis=0)
    ynorm = jnp.sum(ys * ys, axis=0)
    cross = jnp.dot(xs.T, ys, precision=lax.Precision.HIGHEST, preferred_element_type=jnp.float32)
    cost = xnorm[:, None] + ynorm[None, :] - 2.0 * cross
    active = jnp.repeat(jnp.arange(PAIRS, dtype=jnp.int32) < counts[index], BLK)
    row_scores = jnp.where(active[None, :], jnp.take(log_tgt, cols)[None, :] + (jnp.take(tgt_pot, cols)[None, :] - cost) / epsilon, NEG)
    row_top = jnp.max(row_scores, axis=1)
    fpot = -epsilon * (row_top + jnp.log(jnp.sum(jnp.exp(row_scores - row_top[:, None]), axis=1)))
    col_scores = jnp.where(active[None, :], weights[:, None] + (fpot[:, None] - cost) / epsilon, NEG)
    col_top = jnp.max(col_scores, axis=0)
    col_sum = jnp.where(active, jnp.sum(jnp.exp(col_scores - col_top[None, :]), axis=0), 0.0)
    return fpot, col_top.reshape(PAIRS, BLK), col_sum.reshape(PAIRS, BLK)


def reference(src_feat, tgt_feat, tgt_pot, log_src, log_tgt, pairs, counts):
    def one_block(index):
        return block_terms(src_feat, tgt_feat, tgt_pot, log_src, log_tgt, pairs, counts, index)

    fpot, col_top, col_sum = lax.map(one_block, jnp.arange(NSB, dtype=jnp.int32))
    flat_ids = pairs.reshape(-1)
    tops = col_top.reshape(-1, BLK)
    sums = col_sum.reshape(-1, BLK)
    highest = jnp.full((TBLK, BLK), NEG, jnp.float32).at[flat_ids].max(tops)
    total = jnp.zeros((TBLK, BLK), jnp.float32).at[flat_ids].add(sums * jnp.exp(tops - highest[flat_ids]))
    gpot = -epsilon * (highest + jnp.log(total))
    return fpot.reshape(-1), gpot.reshape(-1)
```

```python
import functools

import jax
import jax.numpy as jnp
from jax import lax
from jax.experimental import pallas as pl
from jax.experimental.pallas import tpu as pltpu
from jax.sharding import PartitionSpec as P

BLK = 256
KP = 256
LANE = 128

epsilon = 0.1
NEG = -1e30
LOG2E = 1.4426950408889634
LN2 = 0.6931471805599453


def split3(v):
    first = lax.reduce_precision(v, exponent_bits=8, mantissa_bits=7)
    rest = v - first
    second = lax.reduce_precision(rest, exponent_bits=8, mantissa_bits=7)
    third = rest - second
    return (first.astype(jnp.bfloat16), second.astype(jnp.bfloat16),
            third.astype(jnp.bfloat16))


def split3_kernel(v):
    first = v.astype(jnp.bfloat16)
    rest = v - first.astype(jnp.float32)
    second = rest.astype(jnp.bfloat16)
    third = (rest - second.astype(jnp.float32)).astype(jnp.bfloat16)
    return first, second, third


def build_table(d, blocks_ref, tab_ref):
    scale = 2.0 * LOG2E / epsilon
    slot_row = lax.broadcasted_iota(jnp.int32, (16, BLK), 0)
    used = 6 * d + 16

    def one(tb, carry):
        blk = blocks_ref[tb]
        y = blk[0:d, :]
        yn = jnp.sum(y * y, axis=0, keepdims=True)
        tp = blk[d:d + 1, :]
        lt = blk[d + 1:d + 2, :]
        acol = (lt + (tp - yn) / epsilon) * LOG2E
        ccol = (-yn / epsilon) * LOG2E
        y1, y2, y3 = split3_kernel(y * scale)
        for k, piece in enumerate([y1, y2, y1, y3, y2, y1]):
            tab_ref[tb, k * d:(k + 1) * d, :] = piece
        slot = jnp.zeros((16, BLK), jnp.float32)
        pieces = list(split3_kernel(acol)) + list(split3_kernel(ccol))
        for k, piece in enumerate(pieces):
            slot = jnp.where(slot_row == k, piece.astype(jnp.float32), slot)
        slot = jnp.where((slot_row >= 6) & (slot_row < 9), 1.0, slot)
        tab_ref[tb, 6 * d:used, :] = slot.astype(jnp.bfloat16)
        tab_ref[tb, used:KP, :] = jnp.zeros((KP - used, BLK), jnp.bfloat16)
        return carry

    lax.fori_loop(0, tab_ref.shape[0], one, 0)


def sinkhorn_kernel(npairs, d, pairs_ref, counts_ref, xt_ref, xn_ref, ls_ref, expand_ref, sel_ref,
                    blocks_ref, fpot_ref, gtop_ref, gsum_ref, sbuf, xr_ref, xc_ref, acc_ref, tab_ref):
    b = pl.program_id(0)

    @pl.when(b == 0)
    def _init():
        gtop_ref[...] = jnp.full(gtop_ref.shape, NEG, jnp.float32)
        gsum_ref[...] = jnp.zeros(gsum_ref.shape, jnp.float32)
        build_table(d, blocks_ref, tab_ref)

    cnt = counts_ref[b]
    base = b * npairs
    x1, x2, x3 = split3_kernel(xt_ref[...])
    xa = (jnp.dot(x1, expand_ref[0], preferred_element_type=jnp.float32)
          + jnp.dot(x2, expand_ref[1], preferred_element_type=jnp.float32)
          + jnp.dot(x3, expand_ref[2], preferred_element_type=jnp.float32))
    sel = sel_ref[...]
    xr_ref[...] = (xa + sel[0:1, :]).astype(jnp.bfloat16)
    acc_ref[...] = jnp.full(acc_ref.shape, NEG, jnp.float32)

    def pairs_of(body):
        def two(k, carry):
            body([2 * k, 2 * k + 1])
            return carry

        lax.fori_loop(0, cnt // 2, two, 0)

        @pl.when(cnt % 2 == 1)
        def _last():
            body([cnt - 1])

    def row_max(ts):
        best = None
        for t in ts:
            s = jnp.dot(xr_ref[...], tab_ref[pairs_ref[base + t]], preferred_element_type=jnp.float32)
            sbuf[t] = s
            half = jnp.maximum(s[:, :LANE], s[:, LANE:])
            best = half if best is None else jnp.maximum(best, half)
        acc_ref[...] = jnp.maximum(acc_ref[...], best)

    pairs_of(row_max)
    m = jnp.max(acc_ref[...], axis=1, keepdims=True)
    acc_ref[...] = jnp.zeros(acc_ref.shape, jnp.float32)

    def row_sum(ts):
        total = None
        for t in ts:
            e = jnp.exp2(sbuf[t] - m)
            part = e[:, :LANE] + e[:, LANE:]
            total = part if total is None else total + part
        acc_ref[...] = acc_ref[...] + total

    pairs_of(row_sum)
    lse = m + jnp.log2(jnp.sum(acc_ref[...], axis=1, keepdims=True))
    fpot_ref[...] = xn_ref[...] - (epsilon * LN2) * lse
    p1, p2, p3 = split3_kernel(ls_ref[...] * LOG2E - lse)
    xc_ref[...] = (xa + sel[1:2, :] + p1.astype(jnp.float32) * sel[2:3, :]
                   + p2.astype(jnp.float32) * sel[3:4, :]
                   + p3.astype(jnp.float32) * sel[4:5, :]).astype(jnp.bfloat16)

    def col_pass(ts):
        for t in ts:
            tb = pairs_ref[base + t]
            u = jnp.dot(xc_ref[...], tab_ref[tb], preferred_element_type=jnp.float32)
            sbuf[t] = u
            cm = jnp.max(u, axis=0, keepdims=True)
            cs = jnp.sum(jnp.exp2(sbuf[t] - cm), axis=0, keepdims=True)
            old = gtop_ref[tb]
            new = jnp.maximum(old, cm)
            gsum_ref[tb] = gsum_ref[tb] * jnp.exp2(old - new) + cs * jnp.exp2(cm - new)
            gtop_ref[tb] = new

    pairs_of(col_pass)


def merge(tops, sums, axis):
    top = jnp.max(tops, axis=axis, keepdims=True)
    total = jnp.sum(sums * jnp.exp2(tops - top), axis=axis, keepdims=True)
    return top, total


def on_device(src_feat, tgt_feat, tgt_pot, log_src, log_tgt, pairs, counts):
    d = src_feat.shape[0]
    ns = src_feat.shape[1]
    nrb = ns // BLK
    npairs = pairs.shape[1]
    own_targets = tgt_feat.shape[1]
    ncols = lax.axis_size("cols")

    packed = jnp.concatenate([tgt_feat, tgt_pot[None, :], log_tgt[None, :]], axis=0)
    rowsp = packed.shape[0]
    spread = jnp.broadcast_to(packed[None], (ncols, rowsp, own_targets))
    gathered = lax.all_to_all(spread, "cols", 0, 0, tiled=True)
    nt = ncols * own_targets
    tblocks = nt // BLK
    blocks = jnp.transpose(
        gathered.reshape(ncols, rowsp, own_targets // BLK, BLK), (0, 2, 1, 3)).reshape(tblocks, rowsp, BLK)

    col = jnp.arange(KP, dtype=jnp.int32)[None, :]
    comp = jnp.arange(d, dtype=jnp.int32)[:, None]
    def place(starts):
        hit = jnp.zeros((d, KP), bool)
        for s in starts:
            hit = hit | (col == comp + s)
        return hit.astype(jnp.bfloat16)
    expand = jnp.stack([place([0, d, 3 * d]), place([2 * d, 4 * d]), place([5 * d])])
    k0 = 6 * d
    sel = jnp.stack([
        ((col[0] >= k0) & (col[0] < k0 + 3)),
        ((col[0] >= k0 + 3) & (col[0] < k0 + 6)),
        col[0] == k0 + 6, col[0] == k0 + 7, col[0] == k0 + 8,
        col[0] < 0, col[0] < 0, col[0] < 0,
    ]).astype(jnp.float32)

    xt = jnp.transpose(src_feat)
    xn = jnp.sum(src_feat * src_feat, axis=0)[:, None]
    ls = log_src[:, None]

    grid_spec = pltpu.PrefetchScalarGridSpec(
        num_scalar_prefetch=2,
        grid=(nrb,),
        in_specs=[
            pl.BlockSpec((BLK, d), lambda b, pr, ct: (b, 0)),
            pl.BlockSpec((BLK, 1), lambda b, pr, ct: (b, 0)),
            pl.BlockSpec((BLK, 1), lambda b, pr, ct: (b, 0)),
            pl.BlockSpec((3, d, KP), lambda b, pr, ct: (0, 0, 0)),
            pl.BlockSpec((8, KP), lambda b, pr, ct: (0, 0)),
            pl.BlockSpec((tblocks, rowsp, BLK), lambda b, pr, ct: (0, 0, 0)),
        ],
        out_specs=[
            pl.BlockSpec((BLK, 1), lambda b, pr, ct: (b, 0)),
            pl.BlockSpec((tblocks, 1, BLK), lambda b, pr, ct: (0, 0, 0)),
            pl.BlockSpec((tblocks, 1, BLK), lambda b, pr, ct: (0, 0, 0)),
        ],
        scratch_shapes=[pltpu.VMEM((npairs, BLK, BLK), jnp.float32),
                        pltpu.VMEM((BLK, KP), jnp.bfloat16),
                        pltpu.VMEM((BLK, KP), jnp.bfloat16),
                        pltpu.VMEM((BLK, LANE), jnp.float32),
                        pltpu.VMEM((tblocks, KP, BLK), jnp.bfloat16)],
    )
    fpot, gtop, gsum = pl.pallas_call(
        functools.partial(sinkhorn_kernel, npairs, d),
        grid_spec=grid_spec,
        out_shape=[
            jax.ShapeDtypeStruct((ns, 1), jnp.float32),
            jax.ShapeDtypeStruct((tblocks, 1, BLK), jnp.float32),
            jax.ShapeDtypeStruct((tblocks, 1, BLK), jnp.float32),
        ],
        compiler_params=pltpu.CompilerParams(
            dimension_semantics=("arbitrary",), vmem_limit_bytes=100 * 1024 * 1024),
    )(pairs.reshape(-1), counts, xt, xn, ls, expand, sel, blocks)

    src_pot = fpot.reshape(-1)
    parts = jnp.stack([gtop.reshape(ncols, own_targets), gsum.reshape(ncols, own_targets)], axis=1)
    mine = lax.all_to_all(parts, "cols", 0, 0, tiled=True)
    top, total = merge(mine[:, 0, :], mine[:, 1, :], 0)
    both = lax.all_gather(jnp.concatenate([top, total], axis=0), "rows")
    top, total = merge(both[:, 0, :], both[:, 1, :], 0)
    new_tgt_pot = (-epsilon * LN2) * (top[0] + jnp.log2(total[0]))
    return (src_pot, new_tgt_pot)


def solution(mesh):
    placed = (
        P(None, ("parts", "rows", "cols")),
        P(None, ("parts", "cols")),
        P(("parts", "cols")),
        P(("parts", "rows", "cols")),
        P(("parts", "cols")),
        P(("parts", "rows", "cols"), None),
        P(("parts", "rows", "cols")),
    )
    return jax.shard_map(
        on_device,
        mesh=mesh,
        in_specs=placed,
        out_specs=(P(("parts", "rows", "cols")), P(("parts", "cols"))),
        check_vma=False,
    )
```

```python
import functools

import jax
import jax.numpy as jnp
from jax import lax
from jax.experimental import pallas as pl
from jax.experimental.pallas import tpu as pltpu
from jax.sharding import PartitionSpec as P

BLK = 256
KP = 256
LANE = 128

epsilon = 0.1
NEG = -1e30
LOG2E = 1.4426950408889634
LN2 = 0.6931471805599453


def split3(v):
    first = lax.reduce_precision(v, exponent_bits=8, mantissa_bits=7)
    rest = v - first
    second = lax.reduce_precision(rest, exponent_bits=8, mantissa_bits=7)
    third = rest - second
    return (first.astype(jnp.bfloat16), second.astype(jnp.bfloat16),
            third.astype(jnp.bfloat16))


def split3_kernel(v):
    first = v.astype(jnp.bfloat16)
    rest = v - first.astype(jnp.float32)
    second = rest.astype(jnp.bfloat16)
    third = (rest - second.astype(jnp.float32)).astype(jnp.bfloat16)
    return first, second, third


def build_table(d, blocks_ref, tab_ref):
    scale = 2.0 * LOG2E / epsilon
    slot_row = lax.broadcasted_iota(jnp.int32, (16, BLK), 0)
    used = 6 * d + 16

    def one(tb, carry):
        blk = blocks_ref[tb]
        y = blk[0:d, :]
        yn = jnp.sum(y * y, axis=0, keepdims=True)
        tp = blk[d:d + 1, :]
        lt = blk[d + 1:d + 2, :]
        acol = (lt + (tp - yn) / epsilon) * LOG2E
        ccol = (-yn / epsilon) * LOG2E
        y1, y2, y3 = split3_kernel(y * scale)
        for k, piece in enumerate([y1, y2, y1, y3, y2, y1]):
            tab_ref[tb, k * d:(k + 1) * d, :] = piece
        slot = jnp.zeros((16, BLK), jnp.float32)
        pieces = list(split3_kernel(acol)) + list(split3_kernel(ccol))
        for k, piece in enumerate(pieces):
            slot = jnp.where(slot_row == k, piece.astype(jnp.float32), slot)
        slot = jnp.where((slot_row >= 6) & (slot_row < 9), 1.0, slot)
        tab_ref[tb, 6 * d:used, :] = slot.astype(jnp.bfloat16)
        tab_ref[tb, used:KP, :] = jnp.zeros((KP - used, BLK), jnp.bfloat16)
        return carry

    lax.fori_loop(0, tab_ref.shape[0], one, 0)


def sinkhorn_kernel(npairs, d, pairs_ref, counts_ref, xt_ref, xn_ref, ls_ref, expand_ref, sel_ref,
                    blocks_ref, fpot_ref, gtop_ref, gsum_ref, sbuf, xr_ref, xc_ref, acc_ref, tab_ref):
    b = pl.program_id(0)

    @pl.when(b == 0)
    def _init():
        gtop_ref[...] = jnp.full(gtop_ref.shape, NEG, jnp.float32)
        gsum_ref[...] = jnp.zeros(gsum_ref.shape, jnp.float32)
        build_table(d, blocks_ref, tab_ref)

    cnt = counts_ref[b]
    base = b * npairs
    x1, x2, x3 = split3_kernel(xt_ref[...])
    xa = (jnp.dot(x1, expand_ref[0], preferred_element_type=jnp.float32)
          + jnp.dot(x2, expand_ref[1], preferred_element_type=jnp.float32)
          + jnp.dot(x3, expand_ref[2], preferred_element_type=jnp.float32))
    sel = sel_ref[...]
    xr_ref[...] = (xa + sel[0:1, :]).astype(jnp.bfloat16)
    acc_ref[0] = jnp.full((BLK, LANE), NEG, jnp.float32)
    acc_ref[1] = jnp.zeros((BLK, LANE), jnp.float32)

    def pairs_of(body):
        def two(k, carry):
            body([2 * k, 2 * k + 1])
            return carry

        lax.fori_loop(0, cnt // 2, two, 0)

        @pl.when(cnt % 2 == 1)
        def _last():
            body([cnt - 1])

    def row_pass(ts):
        halves = []
        for t in ts:
            s = jnp.dot(xr_ref[...], tab_ref[pairs_ref[base + t]], preferred_element_type=jnp.float32)
            halves += [s[:, :LANE], s[:, LANE:]]
        old = acc_ref[0]
        new = old
        for h in halves:
            new = jnp.maximum(new, h)
        total = acc_ref[1] * jnp.exp2(old - new)
        for h in halves:
            total = total + jnp.exp2(h - new)
        acc_ref[0] = new
        acc_ref[1] = total

    pairs_of(row_pass)
    lane_top = acc_ref[0]
    m = jnp.max(lane_top, axis=1, keepdims=True)
    lane_sum = acc_ref[1] * jnp.exp2(lane_top - m)
    lse = m + jnp.log2(jnp.sum(lane_sum, axis=1, keepdims=True))
    fpot_ref[...] = xn_ref[...] - (epsilon * LN2) * lse
    p1, p2, p3 = split3_kernel(ls_ref[...] * LOG2E - lse)
    xc_ref[...] = (xa + sel[1:2, :] + p1.astype(jnp.float32) * sel[2:3, :]
                   + p2.astype(jnp.float32) * sel[3:4, :]
                   + p3.astype(jnp.float32) * sel[4:5, :]).astype(jnp.bfloat16)

    def col_pass(ts):
        for slot, t in enumerate(ts):
            tb = pairs_ref[base + t]
            u = jnp.dot(xc_ref[...], tab_ref[tb], preferred_element_type=jnp.float32)
            sbuf[slot] = u
            cm = jnp.max(u, axis=0, keepdims=True)
            cs = jnp.sum(jnp.exp2(sbuf[slot] - cm), axis=0, keepdims=True)
            old = gtop_ref[tb]
            new = jnp.maximum(old, cm)
            gsum_ref[tb] = gsum_ref[tb] * jnp.exp2(old - new) + cs * jnp.exp2(cm - new)
            gtop_ref[tb] = new

    pairs_of(col_pass)


def merge(tops, sums, axis):
    top = jnp.max(tops, axis=axis, keepdims=True)
    total = jnp.sum(sums * jnp.exp2(tops - top), axis=axis, keepdims=True)
    return top, total


def on_device(src_feat, tgt_feat, tgt_pot, log_src, log_tgt, pairs, counts):
    d = src_feat.shape[0]
    ns = src_feat.shape[1]
    nrb = ns // BLK
    npairs = pairs.shape[1]
    own_targets = tgt_feat.shape[1]
    ncols = lax.axis_size("cols")

    packed = jnp.concatenate([tgt_feat, tgt_pot[None, :], log_tgt[None, :]], axis=0)
    rowsp = packed.shape[0]
    spread = jnp.broadcast_to(packed[None], (ncols, rowsp, own_targets))
    gathered = lax.all_to_all(spread, "cols", 0, 0, tiled=True)
    nt = ncols * own_targets
    tblocks = nt // BLK
    blocks = jnp.transpose(
        gathered.reshape(ncols, rowsp, own_targets // BLK, BLK), (0, 2, 1, 3)).reshape(tblocks, rowsp, BLK)

    col = jnp.arange(KP, dtype=jnp.int32)[None, :]
    comp = jnp.arange(d, dtype=jnp.int32)[:, None]
    def place(starts):
        hit = jnp.zeros((d, KP), bool)
        for s in starts:
            hit = hit | (col == comp + s)
        return hit.astype(jnp.bfloat16)
    expand = jnp.stack([place([0, d, 3 * d]), place([2 * d, 4 * d]), place([5 * d])])
    k0 = 6 * d
    sel = jnp.stack([
        ((col[0] >= k0) & (col[0] < k0 + 3)),
        ((col[0] >= k0 + 3) & (col[0] < k0 + 6)),
        col[0] == k0 + 6, col[0] == k0 + 7, col[0] == k0 + 8,
        col[0] < 0, col[0] < 0, col[0] < 0,
    ]).astype(jnp.float32)

    xt = jnp.transpose(src_feat)
    xn = jnp.sum(src_feat * src_feat, axis=0)[:, None]
    ls = log_src[:, None]

    grid_spec = pltpu.PrefetchScalarGridSpec(
        num_scalar_prefetch=2,
        grid=(nrb,),
        in_specs=[
            pl.BlockSpec((BLK, d), lambda b, pr, ct: (b, 0)),
            pl.BlockSpec((BLK, 1), lambda b, pr, ct: (b, 0)),
            pl.BlockSpec((BLK, 1), lambda b, pr, ct: (b, 0)),
            pl.BlockSpec((3, d, KP), lambda b, pr, ct: (0, 0, 0)),
            pl.BlockSpec((8, KP), lambda b, pr, ct: (0, 0)),
            pl.BlockSpec((tblocks, rowsp, BLK), lambda b, pr, ct: (0, 0, 0)),
        ],
        out_specs=[
            pl.BlockSpec((BLK, 1), lambda b, pr, ct: (b, 0)),
            pl.BlockSpec((tblocks, 1, BLK), lambda b, pr, ct: (0, 0, 0)),
            pl.BlockSpec((tblocks, 1, BLK), lambda b, pr, ct: (0, 0, 0)),
        ],
        scratch_shapes=[pltpu.VMEM((2, BLK, BLK), jnp.float32),
                        pltpu.VMEM((BLK, KP), jnp.bfloat16),
                        pltpu.VMEM((BLK, KP), jnp.bfloat16),
                        pltpu.VMEM((2, BLK, LANE), jnp.float32),
                        pltpu.VMEM((tblocks, KP, BLK), jnp.bfloat16)],
    )
    fpot, gtop, gsum = pl.pallas_call(
        functools.partial(sinkhorn_kernel, npairs, d),
        grid_spec=grid_spec,
        out_shape=[
            jax.ShapeDtypeStruct((ns, 1), jnp.float32),
            jax.ShapeDtypeStruct((tblocks, 1, BLK), jnp.float32),
            jax.ShapeDtypeStruct((tblocks, 1, BLK), jnp.float32),
        ],
        compiler_params=pltpu.CompilerParams(
            dimension_semantics=("arbitrary",), vmem_limit_bytes=100 * 1024 * 1024),
    )(pairs.reshape(-1), counts, xt, xn, ls, expand, sel, blocks)

    src_pot = fpot.reshape(-1)
    parts = jnp.stack([gtop.reshape(ncols, own_targets), gsum.reshape(ncols, own_targets)], axis=1)
    mine = lax.all_to_all(parts, "cols", 0, 0, tiled=True)
    top, total = merge(mine[:, 0, :], mine[:, 1, :], 0)
    both = lax.all_gather(jnp.concatenate([top, total], axis=0), "rows")
    top, total = merge(both[:, 0, :], both[:, 1, :], 0)
    new_tgt_pot = (-epsilon * LN2) * (top[0] + jnp.log2(total[0]))
    return (src_pot, new_tgt_pot)


def solution(mesh):
    placed = (
        P(None, ("parts", "rows", "cols")),
        P(None, ("parts", "cols")),
        P(("parts", "cols")),
        P(("parts", "rows", "cols")),
        P(("parts", "cols")),
        P(("parts", "rows", "cols"), None),
        P(("parts", "rows", "cols")),
    )
    return jax.shard_map(
        on_device,
        mesh=mesh,
        in_specs=placed,
        out_specs=(P(("parts", "rows", "cols")), P(("parts", "cols"))),
        check_vma=False,
    )
```

```python
import functools

import jax
import jax.numpy as jnp
from jax import lax
from jax.experimental import pallas as pl
from jax.experimental.pallas import tpu as pltpu
from jax.sharding import PartitionSpec as P

BLK = 256
KP = 256
LANE = 128

epsilon = 0.1
NEG = -1e30
LOG2E = 1.4426950408889634
LN2 = 0.6931471805599453


def split3(v):
    first = lax.reduce_precision(v, exponent_bits=8, mantissa_bits=7)
    rest = v - first
    second = lax.reduce_precision(rest, exponent_bits=8, mantissa_bits=7)
    third = rest - second
    return (first.astype(jnp.bfloat16), second.astype(jnp.bfloat16),
            third.astype(jnp.bfloat16))


def split3_kernel(v):
    first = v.astype(jnp.bfloat16)
    rest = v - first.astype(jnp.float32)
    second = rest.astype(jnp.bfloat16)
    third = (rest - second.astype(jnp.float32)).astype(jnp.bfloat16)
    return first, second, third


def build_table(d, blocks_ref, tab_ref):
    scale = 2.0 * LOG2E / epsilon
    slot_row = lax.broadcasted_iota(jnp.int32, (16, BLK), 0)
    used = 6 * d + 16

    def one(tb, carry):
        blk = blocks_ref[tb]
        y = blk[0:d, :]
        yn = jnp.sum(y * y, axis=0, keepdims=True)
        tp = blk[d:d + 1, :]
        lt = blk[d + 1:d + 2, :]
        acol = (lt + (tp - yn) / epsilon) * LOG2E
        ccol = (-yn / epsilon) * LOG2E
        y1, y2, y3 = split3_kernel(y * scale)
        for k, piece in enumerate([y1, y2, y1, y3, y2, y1]):
            tab_ref[tb, k * d:(k + 1) * d, :] = piece
        slot = jnp.zeros((16, BLK), jnp.float32)
        pieces = list(split3_kernel(acol)) + list(split3_kernel(ccol))
        for k, piece in enumerate(pieces):
            slot = jnp.where(slot_row == k, piece.astype(jnp.float32), slot)
        slot = jnp.where((slot_row >= 6) & (slot_row < 9), 1.0, slot)
        tab_ref[tb, 6 * d:used, :] = slot.astype(jnp.bfloat16)
        tab_ref[tb, used:KP, :] = jnp.zeros((KP - used, BLK), jnp.bfloat16)
        return carry

    lax.fori_loop(0, tab_ref.shape[0], one, 0)


def sinkhorn_kernel(npairs, d, pairs_ref, counts_ref, xt_ref, xn_ref, ls_ref, expand_ref, sel_ref,
                    blocks_ref, fpot_ref, gtop_ref, gsum_ref, sbuf, xr_ref, xc_ref, acc_ref, tab_ref):
    b = pl.program_id(0)

    @pl.when(b == 0)
    def _init():
        gtop_ref[...] = jnp.full(gtop_ref.shape, NEG, jnp.float32)
        gsum_ref[...] = jnp.zeros(gsum_ref.shape, jnp.float32)
        build_table(d, blocks_ref, tab_ref)

    cnt = counts_ref[b]
    base = b * npairs
    x1, x2, x3 = split3_kernel(xt_ref[...])
    xa = (jnp.dot(x1, expand_ref[0], preferred_element_type=jnp.float32)
          + jnp.dot(x2, expand_ref[1], preferred_element_type=jnp.float32)
          + jnp.dot(x3, expand_ref[2], preferred_element_type=jnp.float32))
    sel = sel_ref[...]
    xr_ref[...] = (xa + sel[0:1, :]).astype(jnp.bfloat16)
    acc_ref[0] = jnp.full((BLK, LANE), NEG, jnp.float32)
    acc_ref[1] = jnp.zeros((BLK, LANE), jnp.float32)

    def pairs_of(body):
        def two(k, carry):
            body([2 * k, 2 * k + 1])
            return carry

        lax.fori_loop(0, cnt // 2, two, 0)

        @pl.when(cnt % 2 == 1)
        def _last():
            body([cnt - 1])

    def row_pass(ts):
        halves = []
        for t in ts:
            s = jnp.dot(xr_ref[...], tab_ref[pairs_ref[base + t]], preferred_element_type=jnp.float32)
            halves += [s[:, :LANE], s[:, LANE:]]
        old = acc_ref[0]
        new = old
        for h in halves:
            new = jnp.maximum(new, h)
        total = acc_ref[1] * jnp.exp2(old - new)
        for h in halves:
            total = total + jnp.exp2(h - new)
        acc_ref[0] = new
        acc_ref[1] = total

    pairs_of(row_pass)
    lane_top = acc_ref[0]
    m = jnp.max(lane_top, axis=1, keepdims=True)
    lane_sum = acc_ref[1] * jnp.exp2(lane_top - m)
    lse = m + jnp.log2(jnp.sum(lane_sum, axis=1, keepdims=True))
    fpot_ref[...] = xn_ref[...] - (epsilon * LN2) * lse
    p1, p2, p3 = split3_kernel(ls_ref[...] * LOG2E - lse)
    xc_ref[...] = (xa + sel[1:2, :] + p1.astype(jnp.float32) * sel[2:3, :]
                   + p2.astype(jnp.float32) * sel[3:4, :]
                   + p3.astype(jnp.float32) * sel[4:5, :]).astype(jnp.bfloat16)

    def col_pass(ts):
        for slot, t in enumerate(ts):
            tb = pairs_ref[base + t]
            u = jnp.dot(xc_ref[...], tab_ref[tb], preferred_element_type=jnp.float32)
            sbuf[slot] = u
            cm = jnp.max(u, axis=0, keepdims=True)
            cs = jnp.sum(jnp.exp2(sbuf[slot] - cm), axis=0, keepdims=True)
            old = gtop_ref[tb]
            new = jnp.maximum(old, cm)
            gsum_ref[tb] = gsum_ref[tb] * jnp.exp2(old - new) + cs * jnp.exp2(cm - new)
            gtop_ref[tb] = new

    pairs_of(col_pass)


def merge(tops, sums, axis):
    top = jnp.max(tops, axis=axis, keepdims=True)
    total = jnp.sum(sums * jnp.exp2(tops - top), axis=axis, keepdims=True)
    return top, total


def on_device(src_feat, tgt_feat, tgt_pot, log_src, log_tgt, pairs, counts):
    d = src_feat.shape[0]
    ns = src_feat.shape[1]
    nrb = ns // BLK
    npairs = pairs.shape[1]
    own_targets = tgt_feat.shape[1]
    ncols = lax.axis_size("cols")

    packed = jnp.concatenate([tgt_feat, tgt_pot[None, :], log_tgt[None, :]], axis=0)
    rowsp = packed.shape[0]
    nrows = lax.axis_size("rows")
    share = rowsp // nrows
    mine = lax.dynamic_slice_in_dim(packed, lax.axis_index("rows") * share, share, 0)
    spread = jnp.broadcast_to(mine[None], (ncols, share, own_targets))
    halves = lax.all_to_all(spread, "cols", 0, 0, tiled=True)
    gathered = lax.all_gather(halves, "rows", axis=1, tiled=True)
    nt = ncols * own_targets
    tblocks = nt // BLK
    blocks = jnp.transpose(
        gathered.reshape(ncols, rowsp, own_targets // BLK, BLK), (0, 2, 1, 3)).reshape(tblocks, rowsp, BLK)

    col = jnp.arange(KP, dtype=jnp.int32)[None, :]
    comp = jnp.arange(d, dtype=jnp.int32)[:, None]
    def place(starts):
        hit = jnp.zeros((d, KP), bool)
        for s in starts:
            hit = hit | (col == comp + s)
        return hit.astype(jnp.bfloat16)
    expand = jnp.stack([place([0, d, 3 * d]), place([2 * d, 4 * d]), place([5 * d])])
    k0 = 6 * d
    sel = jnp.stack([
        ((col[0] >= k0) & (col[0] < k0 + 3)),
        ((col[0] >= k0 + 3) & (col[0] < k0 + 6)),
        col[0] == k0 + 6, col[0] == k0 + 7, col[0] == k0 + 8,
        col[0] < 0, col[0] < 0, col[0] < 0,
    ]).astype(jnp.float32)

    xt = jnp.transpose(src_feat)
    xn = jnp.sum(src_feat * src_feat, axis=0)[:, None]
    ls = log_src[:, None]

    grid_spec = pltpu.PrefetchScalarGridSpec(
        num_scalar_prefetch=2,
        grid=(nrb,),
        in_specs=[
            pl.BlockSpec((BLK, d), lambda b, pr, ct: (b, 0)),
            pl.BlockSpec((BLK, 1), lambda b, pr, ct: (b, 0)),
            pl.BlockSpec((BLK, 1), lambda b, pr, ct: (b, 0)),
            pl.BlockSpec((3, d, KP), lambda b, pr, ct: (0, 0, 0)),
            pl.BlockSpec((8, KP), lambda b, pr, ct: (0, 0)),
            pl.BlockSpec((tblocks, rowsp, BLK), lambda b, pr, ct: (0, 0, 0)),
        ],
        out_specs=[
            pl.BlockSpec((BLK, 1), lambda b, pr, ct: (b, 0)),
            pl.BlockSpec((tblocks, 1, BLK), lambda b, pr, ct: (0, 0, 0)),
            pl.BlockSpec((tblocks, 1, BLK), lambda b, pr, ct: (0, 0, 0)),
        ],
        scratch_shapes=[pltpu.VMEM((2, BLK, BLK), jnp.float32),
                        pltpu.VMEM((BLK, KP), jnp.bfloat16),
                        pltpu.VMEM((BLK, KP), jnp.bfloat16),
                        pltpu.VMEM((2, BLK, LANE), jnp.float32),
                        pltpu.VMEM((tblocks, KP, BLK), jnp.bfloat16)],
    )
    fpot, gtop, gsum = pl.pallas_call(
        functools.partial(sinkhorn_kernel, npairs, d),
        grid_spec=grid_spec,
        out_shape=[
            jax.ShapeDtypeStruct((ns, 1), jnp.float32),
            jax.ShapeDtypeStruct((tblocks, 1, BLK), jnp.float32),
            jax.ShapeDtypeStruct((tblocks, 1, BLK), jnp.float32),
        ],
        compiler_params=pltpu.CompilerParams(
            dimension_semantics=("arbitrary",), vmem_limit_bytes=100 * 1024 * 1024),
    )(pairs.reshape(-1), counts, xt, xn, ls, expand, sel, blocks)

    src_pot = fpot.reshape(-1)
    parts = jnp.stack([gtop.reshape(ncols, own_targets), gsum.reshape(ncols, own_targets)], axis=1)
    mine = lax.all_to_all(parts, "cols", 0, 0, tiled=True)
    top, total = merge(mine[:, 0, :], mine[:, 1, :], 0)
    both = lax.all_gather(jnp.concatenate([top, total], axis=0), "rows")
    top, total = merge(both[:, 0, :], both[:, 1, :], 0)
    new_tgt_pot = (-epsilon * LN2) * (top[0] + jnp.log2(total[0]))
    return (src_pot, new_tgt_pot)


def solution(mesh):
    placed = (
        P(None, ("parts", "rows", "cols")),
        P(None, ("parts", "cols")),
        P(("parts", "cols")),
        P(("parts", "rows", "cols")),
        P(("parts", "cols")),
        P(("parts", "rows", "cols"), None),
        P(("parts", "rows", "cols")),
    )
    return jax.shard_map(
        on_device,
        mesh=mesh,
        in_specs=placed,
        out_specs=(P(("parts", "rows", "cols")), P(("parts", "cols"))),
        check_vma=False,
    )
```

```python
import functools

import jax
import jax.numpy as jnp
from jax import lax
from jax.experimental import pallas as pl
from jax.experimental.pallas import tpu as pltpu
from jax.sharding import PartitionSpec as P

BLK = 256
KP = 256
LANE = 128

epsilon = 0.1
NEG = -1e30
LOG2E = 1.4426950408889634
LN2 = 0.6931471805599453


def split3(v):
    first = lax.reduce_precision(v, exponent_bits=8, mantissa_bits=7)
    rest = v - first
    second = lax.reduce_precision(rest, exponent_bits=8, mantissa_bits=7)
    third = rest - second
    return (first.astype(jnp.bfloat16), second.astype(jnp.bfloat16),
            third.astype(jnp.bfloat16))


def split3_kernel(v):
    first = v.astype(jnp.bfloat16)
    rest = v - first.astype(jnp.float32)
    second = rest.astype(jnp.bfloat16)
    third = (rest - second.astype(jnp.float32)).astype(jnp.bfloat16)
    return first, second, third


def build_table(d, blocks_ref, tab_ref):
    scale = 2.0 * LOG2E / epsilon
    slot_row = lax.broadcasted_iota(jnp.int32, (16, BLK), 0)
    used = 6 * d + 16

    def one(tb, carry):
        blk = blocks_ref[tb]
        y = blk[0:d, :]
        yn = jnp.sum(y * y, axis=0, keepdims=True)
        tp = blk[d:d + 1, :]
        lt = blk[d + 1:d + 2, :]
        acol = (lt + (tp - yn) / epsilon) * LOG2E
        ccol = (-yn / epsilon) * LOG2E
        y1, y2, y3 = split3_kernel(y * scale)
        for k, piece in enumerate([y1, y2, y1, y3, y2, y1]):
            tab_ref[tb, k * d:(k + 1) * d, :] = piece
        slot = jnp.zeros((16, BLK), jnp.float32)
        pieces = list(split3_kernel(acol)) + list(split3_kernel(ccol))
        for k, piece in enumerate(pieces):
            slot = jnp.where(slot_row == k, piece.astype(jnp.float32), slot)
        slot = jnp.where((slot_row >= 6) & (slot_row < 9), 1.0, slot)
        tab_ref[tb, 6 * d:used, :] = slot.astype(jnp.bfloat16)
        tab_ref[tb, used:KP, :] = jnp.zeros((KP - used, BLK), jnp.bfloat16)
        return carry

    lax.fori_loop(0, tab_ref.shape[0], one, 0)


def sinkhorn_kernel(npairs, d, pairs_ref, counts_ref, xt_ref, xn_ref, ls_ref, expand_ref, sel_ref,
                    blocks_ref, fpot_ref, gtop_ref, gsum_ref, sbuf, xr_ref, xc_ref, acc_ref, tab_ref):
    b = pl.program_id(0)

    @pl.when(b == 0)
    def _init():
        gtop_ref[...] = jnp.full(gtop_ref.shape, NEG, jnp.float32)
        gsum_ref[...] = jnp.zeros(gsum_ref.shape, jnp.float32)
        build_table(d, blocks_ref, tab_ref)

    cnt = counts_ref[b]
    base = b * npairs
    x1, x2, x3 = split3_kernel(xt_ref[...])
    xa = (jnp.dot(x1, expand_ref[0], preferred_element_type=jnp.float32)
          + jnp.dot(x2, expand_ref[1], preferred_element_type=jnp.float32)
          + jnp.dot(x3, expand_ref[2], preferred_element_type=jnp.float32))
    sel = sel_ref[...]
    xr_ref[...] = (xa + sel[0:1, :]).astype(jnp.bfloat16)
    acc_ref[0] = jnp.full((BLK, LANE), NEG, jnp.float32)
    acc_ref[1] = jnp.zeros((BLK, LANE), jnp.float32)

    def pairs_of(body):
        def two(k, carry):
            body([2 * k, 2 * k + 1])
            return carry

        lax.fori_loop(0, cnt // 2, two, 0)

        @pl.when(cnt % 2 == 1)
        def _last():
            body([cnt - 1])

    def row_pass(ts):
        halves = []
        for t in ts:
            s = jnp.dot(xr_ref[...], tab_ref[pairs_ref[base + t]], preferred_element_type=jnp.float32)
            halves += [s[:, :LANE], s[:, LANE:]]
        old = acc_ref[0]
        new = old
        for h in halves:
            new = jnp.maximum(new, h)
        total = acc_ref[1] * jnp.exp2(old - new)
        for h in halves:
            total = total + jnp.exp2(h - new)
        acc_ref[0] = new
        acc_ref[1] = total

    pairs_of(row_pass)
    lane_top = acc_ref[0]
    m = jnp.max(lane_top, axis=1, keepdims=True)
    lane_sum = acc_ref[1] * jnp.exp2(lane_top - m)
    lse = m + jnp.log2(jnp.sum(lane_sum, axis=1, keepdims=True))
    fpot_ref[...] = xn_ref[...] - (epsilon * LN2) * lse
    p1, p2, p3 = split3_kernel(ls_ref[...] * LOG2E - lse)
    xc_ref[...] = (xa + sel[1:2, :] + p1.astype(jnp.float32) * sel[2:3, :]
                   + p2.astype(jnp.float32) * sel[3:4, :]
                   + p3.astype(jnp.float32) * sel[4:5, :]).astype(jnp.bfloat16)

    def col_pass(ts):
        for slot, t in enumerate(ts):
            tb = pairs_ref[base + t]
            u = jnp.dot(xc_ref[...], tab_ref[tb], preferred_element_type=jnp.float32)
            sbuf[slot] = u
            cm = jnp.max(u, axis=0, keepdims=True)
            cs = jnp.sum(jnp.exp2(sbuf[slot] - cm), axis=0, keepdims=True)
            old = gtop_ref[tb]
            new = jnp.maximum(old, cm)
            gsum_ref[tb] = gsum_ref[tb] * jnp.exp2(old - new) + cs * jnp.exp2(cm - new)
            gtop_ref[tb] = new

    pairs_of(col_pass)


def merge(tops, sums, axis):
    top = jnp.max(tops, axis=axis, keepdims=True)
    total = jnp.sum(sums * jnp.exp2(tops - top), axis=axis, keepdims=True)
    return top, total


def on_device(src_feat, tgt_feat, tgt_pot, log_src, log_tgt, pairs, counts):
    d = src_feat.shape[0]
    ns = src_feat.shape[1]
    nrb = ns // BLK
    npairs = pairs.shape[1]
    own_targets = tgt_feat.shape[1]
    ncols = lax.axis_size("cols")

    packed = jnp.concatenate([tgt_feat, tgt_pot[None, :], log_tgt[None, :]], axis=0)
    rowsp = packed.shape[0]
    nrows = lax.axis_size("rows")
    share = rowsp // nrows
    mine = lax.dynamic_slice_in_dim(packed, lax.axis_index("rows") * share, share, 0)
    spread = jnp.broadcast_to(mine[None], (ncols, share, own_targets))
    halves = lax.all_to_all(spread, "cols", 0, 0, tiled=True)
    other = lax.ppermute(halves, "rows", [(0, 1), (1, 0)])
    first = lax.axis_index("rows") == 0
    gathered = jnp.concatenate(
        [jnp.where(first, halves, other), jnp.where(first, other, halves)], axis=1)
    nt = ncols * own_targets
    tblocks = nt // BLK
    blocks = jnp.transpose(
        gathered.reshape(ncols, rowsp, own_targets // BLK, BLK), (0, 2, 1, 3)).reshape(tblocks, rowsp, BLK)

    col = jnp.arange(KP, dtype=jnp.int32)[None, :]
    comp = jnp.arange(d, dtype=jnp.int32)[:, None]
    def place(starts):
        hit = jnp.zeros((d, KP), bool)
        for s in starts:
            hit = hit | (col == comp + s)
        return hit.astype(jnp.bfloat16)
    expand = jnp.stack([place([0, d, 3 * d]), place([2 * d, 4 * d]), place([5 * d])])
    k0 = 6 * d
    sel = jnp.stack([
        ((col[0] >= k0) & (col[0] < k0 + 3)),
        ((col[0] >= k0 + 3) & (col[0] < k0 + 6)),
        col[0] == k0 + 6, col[0] == k0 + 7, col[0] == k0 + 8,
        col[0] < 0, col[0] < 0, col[0] < 0,
    ]).astype(jnp.float32)

    xt = jnp.transpose(src_feat)
    xn = jnp.sum(src_feat * src_feat, axis=0)[:, None]
    ls = log_src[:, None]

    grid_spec = pltpu.PrefetchScalarGridSpec(
        num_scalar_prefetch=2,
        grid=(nrb,),
        in_specs=[
            pl.BlockSpec((BLK, d), lambda b, pr, ct: (b, 0)),
            pl.BlockSpec((BLK, 1), lambda b, pr, ct: (b, 0)),
            pl.BlockSpec((BLK, 1), lambda b, pr, ct: (b, 0)),
            pl.BlockSpec((3, d, KP), lambda b, pr, ct: (0, 0, 0)),
            pl.BlockSpec((8, KP), lambda b, pr, ct: (0, 0)),
            pl.BlockSpec((tblocks, rowsp, BLK), lambda b, pr, ct: (0, 0, 0)),
        ],
        out_specs=[
            pl.BlockSpec((BLK, 1), lambda b, pr, ct: (b, 0)),
            pl.BlockSpec((tblocks, 1, BLK), lambda b, pr, ct: (0, 0, 0)),
            pl.BlockSpec((tblocks, 1, BLK), lambda b, pr, ct: (0, 0, 0)),
        ],
        scratch_shapes=[pltpu.VMEM((2, BLK, BLK), jnp.float32),
                        pltpu.VMEM((BLK, KP), jnp.bfloat16),
                        pltpu.VMEM((BLK, KP), jnp.bfloat16),
                        pltpu.VMEM((2, BLK, LANE), jnp.float32),
                        pltpu.VMEM((tblocks, KP, BLK), jnp.bfloat16)],
    )
    fpot, gtop, gsum = pl.pallas_call(
        functools.partial(sinkhorn_kernel, npairs, d),
        grid_spec=grid_spec,
        out_shape=[
            jax.ShapeDtypeStruct((ns, 1), jnp.float32),
            jax.ShapeDtypeStruct((tblocks, 1, BLK), jnp.float32),
            jax.ShapeDtypeStruct((tblocks, 1, BLK), jnp.float32),
        ],
        compiler_params=pltpu.CompilerParams(
            dimension_semantics=("arbitrary",), vmem_limit_bytes=100 * 1024 * 1024),
    )(pairs.reshape(-1), counts, xt, xn, ls, expand, sel, blocks)

    src_pot = fpot.reshape(-1)
    parts = jnp.stack([gtop.reshape(ncols, own_targets), gsum.reshape(ncols, own_targets)], axis=1)
    mine = lax.all_to_all(parts, "cols", 0, 0, tiled=True)
    top, total = merge(mine[:, 0, :], mine[:, 1, :], 0)
    here = jnp.concatenate([top, total], axis=0)
    there = lax.ppermute(here, "rows", [(0, 1), (1, 0)])
    both = jnp.stack([jnp.where(first, here, there), jnp.where(first, there, here)])
    top, total = merge(both[:, 0, :], both[:, 1, :], 0)
    new_tgt_pot = (-epsilon * LN2) * (top[0] + jnp.log2(total[0]))
    return (src_pot, new_tgt_pot)


def solution(mesh):
    placed = (
        P(None, ("parts", "rows", "cols")),
        P(None, ("parts", "cols")),
        P(("parts", "cols")),
        P(("parts", "rows", "cols")),
        P(("parts", "cols")),
        P(("parts", "rows", "cols"), None),
        P(("parts", "rows", "cols")),
    )
    return jax.shard_map(
        on_device,
        mesh=mesh,
        in_specs=placed,
        out_specs=(P(("parts", "rows", "cols")), P(("parts", "cols"))),
        check_vma=False,
    )
```

```python
import functools

import jax
import jax.numpy as jnp
from jax import lax
from jax.experimental import pallas as pl
from jax.experimental.pallas import tpu as pltpu
from jax.sharding import PartitionSpec as P

BLK = 256
KP = 256
LANE = 128

epsilon = 0.1
NEG = -1e30
LOG2E = 1.4426950408889634
LN2 = 0.6931471805599453


def split3(v):
    first = lax.reduce_precision(v, exponent_bits=8, mantissa_bits=7)
    rest = v - first
    second = lax.reduce_precision(rest, exponent_bits=8, mantissa_bits=7)
    third = rest - second
    return (first.astype(jnp.bfloat16), second.astype(jnp.bfloat16),
            third.astype(jnp.bfloat16))


def split3_kernel(v):
    first = v.astype(jnp.bfloat16)
    rest = v - first.astype(jnp.float32)
    second = rest.astype(jnp.bfloat16)
    third = (rest - second.astype(jnp.float32)).astype(jnp.bfloat16)
    return first, second, third


def build_table(d, blocks_ref, tab_ref):
    scale = 2.0 * LOG2E / epsilon
    slot_row = lax.broadcasted_iota(jnp.int32, (16, BLK), 0)
    used = 6 * d + 16

    def one(tb, carry):
        blk = blocks_ref[tb]
        y = blk[0:d, :]
        yn = jnp.sum(y * y, axis=0, keepdims=True)
        tp = blk[d:d + 1, :]
        lt = blk[d + 1:d + 2, :]
        acol = (lt + (tp - yn) / epsilon) * LOG2E
        ccol = (-yn / epsilon) * LOG2E
        y1, y2, y3 = split3_kernel(y * scale)
        for k, piece in enumerate([y1, y2, y1, y3, y2, y1]):
            tab_ref[tb, k * d:(k + 1) * d, :] = piece
        slot = jnp.zeros((16, BLK), jnp.float32)
        pieces = list(split3_kernel(acol)) + list(split3_kernel(ccol))
        for k, piece in enumerate(pieces):
            slot = jnp.where(slot_row == k, piece.astype(jnp.float32), slot)
        slot = jnp.where((slot_row >= 6) & (slot_row < 9), 1.0, slot)
        tab_ref[tb, 6 * d:used, :] = slot.astype(jnp.bfloat16)
        tab_ref[tb, used:KP, :] = jnp.zeros((KP - used, BLK), jnp.bfloat16)
        return carry

    lax.fori_loop(0, tab_ref.shape[0], one, 0)


def sinkhorn_kernel(npairs, d, pairs_ref, counts_ref, xt_ref, xn_ref, ls_ref, expand_ref, sel_ref,
                    blocks_ref, fpot_ref, gtop_ref, gsum_ref, sbuf, xr_ref, xc_ref, acc_ref, tab_ref):
    b = pl.program_id(0)

    @pl.when(b == 0)
    def _init():
        gtop_ref[...] = jnp.full(gtop_ref.shape, NEG, jnp.float32)
        gsum_ref[...] = jnp.zeros(gsum_ref.shape, jnp.float32)
        build_table(d, blocks_ref, tab_ref)

    cnt = counts_ref[b]
    base = b * npairs
    x1, x2, x3 = split3_kernel(xt_ref[...])
    xa = (jnp.dot(x1, expand_ref[0], preferred_element_type=jnp.float32)
          + jnp.dot(x2, expand_ref[1], preferred_element_type=jnp.float32)
          + jnp.dot(x3, expand_ref[2], preferred_element_type=jnp.float32))
    sel = sel_ref[...]
    xr_ref[...] = (xa + sel[0:1, :]).astype(jnp.bfloat16)
    acc_ref[0] = jnp.full((BLK, LANE), NEG, jnp.float32)
    acc_ref[1] = jnp.zeros((BLK, LANE), jnp.float32)

    def pairs_of(body):
        def two(k, carry):
            body([2 * k, 2 * k + 1])
            return carry

        lax.fori_loop(0, cnt // 2, two, 0)

        @pl.when(cnt % 2 == 1)
        def _last():
            body([cnt - 1])

    def quads_of(body):
        def four(k, carry):
            body([4 * k + i for i in range(4)])
            return carry

        lax.fori_loop(0, cnt // 4, four, 0)
        done = cnt - cnt % 4

        @pl.when(cnt % 4 >= 2)
        def _pair():
            body([done, done + 1])

        @pl.when(cnt % 2 == 1)
        def _last():
            body([cnt - 1])

    def row_pass(ts):
        halves = []
        for t in ts:
            s = jnp.dot(xr_ref[...], tab_ref[pairs_ref[base + t]], preferred_element_type=jnp.float32)
            halves += [s[:, :LANE], s[:, LANE:]]
        old = acc_ref[0]
        new = old
        for h in halves:
            new = jnp.maximum(new, h)
        total = acc_ref[1] * jnp.exp2(old - new)
        for h in halves:
            total = total + jnp.exp2(h - new)
        acc_ref[0] = new
        acc_ref[1] = total

    pairs_of(row_pass)
    lane_top = acc_ref[0]
    m = jnp.max(lane_top, axis=1, keepdims=True)
    lane_sum = acc_ref[1] * jnp.exp2(lane_top - m)
    lse = m + jnp.log2(jnp.sum(lane_sum, axis=1, keepdims=True))
    fpot_ref[...] = xn_ref[...] - (epsilon * LN2) * lse
    p1, p2, p3 = split3_kernel(ls_ref[...] * LOG2E - lse)
    xc_ref[...] = (xa + sel[1:2, :] + p1.astype(jnp.float32) * sel[2:3, :]
                   + p2.astype(jnp.float32) * sel[3:4, :]
                   + p3.astype(jnp.float32) * sel[4:5, :]).astype(jnp.bfloat16)

    def col_pass(ts):
        for slot, t in enumerate(ts):
            tb = pairs_ref[base + t]
            u = jnp.dot(xc_ref[...], tab_ref[tb], preferred_element_type=jnp.float32)
            sbuf[slot] = u
            cm = jnp.max(u, axis=0, keepdims=True)
            cs = jnp.sum(jnp.exp2(sbuf[slot] - cm), axis=0, keepdims=True)
            old = gtop_ref[tb]
            new = jnp.maximum(old, cm)
            gsum_ref[tb] = gsum_ref[tb] * jnp.exp2(old - new) + cs * jnp.exp2(cm - new)
            gtop_ref[tb] = new

    quads_of(col_pass)


def merge(tops, sums, axis):
    top = jnp.max(tops, axis=axis, keepdims=True)
    total = jnp.sum(sums * jnp.exp2(tops - top), axis=axis, keepdims=True)
    return top, total


def on_device(src_feat, tgt_feat, tgt_pot, log_src, log_tgt, pairs, counts):
    d = src_feat.shape[0]
    ns = src_feat.shape[1]
    nrb = ns // BLK
    npairs = pairs.shape[1]
    own_targets = tgt_feat.shape[1]
    ncols = lax.axis_size("cols")

    packed = jnp.concatenate([tgt_feat, tgt_pot[None, :], log_tgt[None, :]], axis=0)
    rowsp = packed.shape[0]
    nrows = lax.axis_size("rows")
    share = rowsp // nrows
    mine = lax.dynamic_slice_in_dim(packed, lax.axis_index("rows") * share, share, 0)
    spread = jnp.broadcast_to(mine[None], (ncols, share, own_targets))
    halves = lax.all_to_all(spread, "cols", 0, 0, tiled=True)
    other = lax.ppermute(halves, "rows", [(0, 1), (1, 0)])
    first = lax.axis_index("rows") == 0
    gathered = jnp.concatenate(
        [jnp.where(first, halves, other), jnp.where(first, other, halves)], axis=1)
    nt = ncols * own_targets
    tblocks = nt // BLK
    blocks = jnp.transpose(
        gathered.reshape(ncols, rowsp, own_targets // BLK, BLK), (0, 2, 1, 3)).reshape(tblocks, rowsp, BLK)

    col = jnp.arange(KP, dtype=jnp.int32)[None, :]
    comp = jnp.arange(d, dtype=jnp.int32)[:, None]
    def place(starts):
        hit = jnp.zeros((d, KP), bool)
        for s in starts:
            hit = hit | (col == comp + s)
        return hit.astype(jnp.bfloat16)
    expand = jnp.stack([place([0, d, 3 * d]), place([2 * d, 4 * d]), place([5 * d])])
    k0 = 6 * d
    sel = jnp.stack([
        ((col[0] >= k0) & (col[0] < k0 + 3)),
        ((col[0] >= k0 + 3) & (col[0] < k0 + 6)),
        col[0] == k0 + 6, col[0] == k0 + 7, col[0] == k0 + 8,
        col[0] < 0, col[0] < 0, col[0] < 0,
    ]).astype(jnp.float32)

    xt = jnp.transpose(src_feat)
    xn = jnp.sum(src_feat * src_feat, axis=0)[:, None]
    ls = log_src[:, None]

    grid_spec = pltpu.PrefetchScalarGridSpec(
        num_scalar_prefetch=2,
        grid=(nrb,),
        in_specs=[
            pl.BlockSpec((BLK, d), lambda b, pr, ct: (b, 0)),
            pl.BlockSpec((BLK, 1), lambda b, pr, ct: (b, 0)),
            pl.BlockSpec((BLK, 1), lambda b, pr, ct: (b, 0)),
            pl.BlockSpec((3, d, KP), lambda b, pr, ct: (0, 0, 0)),
            pl.BlockSpec((8, KP), lambda b, pr, ct: (0, 0)),
            pl.BlockSpec((tblocks, rowsp, BLK), lambda b, pr, ct: (0, 0, 0)),
        ],
        out_specs=[
            pl.BlockSpec((BLK, 1), lambda b, pr, ct: (b, 0)),
            pl.BlockSpec((tblocks, 1, BLK), lambda b, pr, ct: (0, 0, 0)),
            pl.BlockSpec((tblocks, 1, BLK), lambda b, pr, ct: (0, 0, 0)),
        ],
        scratch_shapes=[pltpu.VMEM((4, BLK, BLK), jnp.float32),
                        pltpu.VMEM((BLK, KP), jnp.bfloat16),
                        pltpu.VMEM((BLK, KP), jnp.bfloat16),
                        pltpu.VMEM((2, BLK, LANE), jnp.float32),
                        pltpu.VMEM((tblocks, KP, BLK), jnp.bfloat16)],
    )
    fpot, gtop, gsum = pl.pallas_call(
        functools.partial(sinkhorn_kernel, npairs, d),
        grid_spec=grid_spec,
        out_shape=[
            jax.ShapeDtypeStruct((ns, 1), jnp.float32),
            jax.ShapeDtypeStruct((tblocks, 1, BLK), jnp.float32),
            jax.ShapeDtypeStruct((tblocks, 1, BLK), jnp.float32),
        ],
        compiler_params=pltpu.CompilerParams(
            dimension_semantics=("arbitrary",), vmem_limit_bytes=100 * 1024 * 1024),
    )(pairs.reshape(-1), counts, xt, xn, ls, expand, sel, blocks)

    src_pot = fpot.reshape(-1)
    parts = jnp.stack([gtop.reshape(ncols, own_targets), gsum.reshape(ncols, own_targets)], axis=1)
    mine = lax.all_to_all(parts, "cols", 0, 0, tiled=True)
    top, total = merge(mine[:, 0, :], mine[:, 1, :], 0)
    here = jnp.concatenate([top, total], axis=0)
    there = lax.ppermute(here, "rows", [(0, 1), (1, 0)])
    both = jnp.stack([jnp.where(first, here, there), jnp.where(first, there, here)])
    top, total = merge(both[:, 0, :], both[:, 1, :], 0)
    new_tgt_pot = (-epsilon * LN2) * (top[0] + jnp.log2(total[0]))
    return (src_pot, new_tgt_pot)


def solution(mesh):
    placed = (
        P(None, ("parts", "rows", "cols")),
        P(None, ("parts", "cols")),
        P(("parts", "cols")),
        P(("parts", "rows", "cols")),
        P(("parts", "cols")),
        P(("parts", "rows", "cols"), None),
        P(("parts", "rows", "cols")),
    )
    return jax.shard_map(
        on_device,
        mesh=mesh,
        in_specs=placed,
        out_specs=(P(("parts", "rows", "cols")), P(("parts", "cols"))),
        check_vma=False,
    )
```

```python
import functools

import jax
import jax.numpy as jnp
from jax import lax
from jax.experimental import pallas as pl
from jax.experimental.pallas import tpu as pltpu
from jax.sharding import PartitionSpec as P

BLK = 256
KP = 128
LANE = 128

epsilon = 0.1
NEG = -1e30
LOG2E = 1.4426950408889634
LN2 = 0.6931471805599453


def split3(v):
    first = lax.reduce_precision(v, exponent_bits=8, mantissa_bits=7)
    rest = v - first
    second = lax.reduce_precision(rest, exponent_bits=8, mantissa_bits=7)
    third = rest - second
    return (first.astype(jnp.bfloat16), second.astype(jnp.bfloat16),
            third.astype(jnp.bfloat16))


def split3_kernel(v):
    first = v.astype(jnp.bfloat16)
    rest = v - first.astype(jnp.float32)
    second = rest.astype(jnp.bfloat16)
    third = (rest - second.astype(jnp.float32)).astype(jnp.bfloat16)
    return first, second, third


def build_table(d, blocks_ref, tab_ref):
    scale = 2.0 * LOG2E / epsilon
    slot_row = lax.broadcasted_iota(jnp.int32, (16, BLK), 0)
    used = 3 * d + 16

    def one(tb, carry):
        blk = blocks_ref[tb]
        y = blk[0:d, :]
        yn = jnp.sum(y * y, axis=0, keepdims=True)
        tp = blk[d:d + 1, :]
        lt = blk[d + 1:d + 2, :]
        acol = (lt + (tp - yn) / epsilon) * LOG2E
        ccol = (-yn / epsilon) * LOG2E
        y1, y2, y3 = split3_kernel(y * scale)
        for k, piece in enumerate([y1, y2, y1]):
            tab_ref[tb, k * d:(k + 1) * d, :] = piece
        slot = jnp.zeros((16, BLK), jnp.float32)
        pieces = list(split3_kernel(acol)) + list(split3_kernel(ccol))
        for k, piece in enumerate(pieces):
            slot = jnp.where(slot_row == k, piece.astype(jnp.float32), slot)
        slot = jnp.where((slot_row >= 6) & (slot_row < 9), 1.0, slot)
        tab_ref[tb, 3 * d:used, :] = slot.astype(jnp.bfloat16)
        tab_ref[tb, used:KP, :] = jnp.zeros((KP - used, BLK), jnp.bfloat16)
        return carry

    lax.fori_loop(0, tab_ref.shape[0], one, 0)


def sinkhorn_kernel(npairs, d, pairs_ref, counts_ref, xt_ref, xn_ref, ls_ref, expand_ref, sel_ref,
                    blocks_ref, fpot_ref, gtop_ref, gsum_ref, sbuf, xr_ref, xc_ref, acc_ref, tab_ref):
    b = pl.program_id(0)

    @pl.when(b == 0)
    def _init():
        gtop_ref[...] = jnp.full(gtop_ref.shape, NEG, jnp.float32)
        gsum_ref[...] = jnp.zeros(gsum_ref.shape, jnp.float32)
        build_table(d, blocks_ref, tab_ref)

    cnt = counts_ref[b]
    base = b * npairs
    x1, x2, x3 = split3_kernel(xt_ref[...])
    xa = (jnp.dot(x1, expand_ref[0], preferred_element_type=jnp.float32)
          + jnp.dot(x2, expand_ref[1], preferred_element_type=jnp.float32)
          + jnp.dot(x3, expand_ref[2], preferred_element_type=jnp.float32))
    sel = sel_ref[...]
    xr_ref[...] = (xa + sel[0:1, :]).astype(jnp.bfloat16)
    acc_ref[0] = jnp.full((BLK, LANE), NEG, jnp.float32)
    acc_ref[1] = jnp.zeros((BLK, LANE), jnp.float32)

    def pairs_of(body):
        def two(k, carry):
            body([2 * k, 2 * k + 1])
            return carry

        lax.fori_loop(0, cnt // 2, two, 0)

        @pl.when(cnt % 2 == 1)
        def _last():
            body([cnt - 1])

    def quads_of(body):
        def four(k, carry):
            body([4 * k + i for i in range(4)])
            return carry

        lax.fori_loop(0, cnt // 4, four, 0)
        done = cnt - cnt % 4

        @pl.when(cnt % 4 >= 2)
        def _pair():
            body([done, done + 1])

        @pl.when(cnt % 2 == 1)
        def _last():
            body([cnt - 1])

    def row_pass(ts):
        halves = []
        for t in ts:
            s = jnp.dot(xr_ref[...], tab_ref[pairs_ref[base + t]], preferred_element_type=jnp.float32)
            halves += [s[:, :LANE], s[:, LANE:]]
        old = acc_ref[0]
        new = old
        for h in halves:
            new = jnp.maximum(new, h)
        total = acc_ref[1] * jnp.exp2(old - new)
        for h in halves:
            total = total + jnp.exp2(h - new)
        acc_ref[0] = new
        acc_ref[1] = total

    pairs_of(row_pass)
    lane_top = acc_ref[0]
    m = jnp.max(lane_top, axis=1, keepdims=True)
    lane_sum = acc_ref[1] * jnp.exp2(lane_top - m)
    lse = m + jnp.log2(jnp.sum(lane_sum, axis=1, keepdims=True))
    fpot_ref[...] = xn_ref[...] - (epsilon * LN2) * lse
    p1, p2, p3 = split3_kernel(ls_ref[...] * LOG2E - lse)
    xc_ref[...] = (xa + sel[1:2, :] + p1.astype(jnp.float32) * sel[2:3, :]
                   + p2.astype(jnp.float32) * sel[3:4, :]
                   + p3.astype(jnp.float32) * sel[4:5, :]).astype(jnp.bfloat16)

    def col_pass(ts):
        for slot, t in enumerate(ts):
            tb = pairs_ref[base + t]
            u = jnp.dot(xc_ref[...], tab_ref[tb], preferred_element_type=jnp.float32)
            sbuf[slot] = u
            cm = jnp.max(u, axis=0, keepdims=True)
            cs = jnp.sum(jnp.exp2(sbuf[slot] - cm), axis=0, keepdims=True)
            old = gtop_ref[tb]
            new = jnp.maximum(old, cm)
            gsum_ref[tb] = gsum_ref[tb] * jnp.exp2(old - new) + cs * jnp.exp2(cm - new)
            gtop_ref[tb] = new

    quads_of(col_pass)


def merge(tops, sums, axis):
    top = jnp.max(tops, axis=axis, keepdims=True)
    total = jnp.sum(sums * jnp.exp2(tops - top), axis=axis, keepdims=True)
    return top, total


def on_device(src_feat, tgt_feat, tgt_pot, log_src, log_tgt, pairs, counts):
    d = src_feat.shape[0]
    ns = src_feat.shape[1]
    nrb = ns // BLK
    npairs = pairs.shape[1]
    own_targets = tgt_feat.shape[1]
    ncols = lax.axis_size("cols")

    packed = jnp.concatenate([tgt_feat, tgt_pot[None, :], log_tgt[None, :]], axis=0)
    rowsp = packed.shape[0]
    nrows = lax.axis_size("rows")
    share = rowsp // nrows
    mine = lax.dynamic_slice_in_dim(packed, lax.axis_index("rows") * share, share, 0)
    spread = jnp.broadcast_to(mine[None], (ncols, share, own_targets))
    halves = lax.all_to_all(spread, "cols", 0, 0, tiled=True)
    other = lax.ppermute(halves, "rows", [(0, 1), (1, 0)])
    first = lax.axis_index("rows") == 0
    gathered = jnp.concatenate(
        [jnp.where(first, halves, other), jnp.where(first, other, halves)], axis=1)
    nt = ncols * own_targets
    tblocks = nt // BLK
    blocks = jnp.transpose(
        gathered.reshape(ncols, rowsp, own_targets // BLK, BLK), (0, 2, 1, 3)).reshape(tblocks, rowsp, BLK)

    col = jnp.arange(KP, dtype=jnp.int32)[None, :]
    comp = jnp.arange(d, dtype=jnp.int32)[:, None]
    def place(starts):
        hit = jnp.zeros((d, KP), bool)
        for s in starts:
            hit = hit | (col == comp + s)
        return hit.astype(jnp.bfloat16)
    expand = jnp.stack([place([0, d]), place([2 * d]), place([])])
    k0 = 3 * d
    sel = jnp.stack([
        ((col[0] >= k0) & (col[0] < k0 + 3)),
        ((col[0] >= k0 + 3) & (col[0] < k0 + 6)),
        col[0] == k0 + 6, col[0] == k0 + 7, col[0] == k0 + 8,
        col[0] < 0, col[0] < 0, col[0] < 0,
    ]).astype(jnp.float32)

    xt = jnp.transpose(src_feat)
    xn = jnp.sum(src_feat * src_feat, axis=0)[:, None]
    ls = log_src[:, None]

    grid_spec = pltpu.PrefetchScalarGridSpec(
        num_scalar_prefetch=2,
        grid=(nrb,),
        in_specs=[
            pl.BlockSpec((BLK, d), lambda b, pr, ct: (b, 0)),
            pl.BlockSpec((BLK, 1), lambda b, pr, ct: (b, 0)),
            pl.BlockSpec((BLK, 1), lambda b, pr, ct: (b, 0)),
            pl.BlockSpec((3, d, KP), lambda b, pr, ct: (0, 0, 0)),
            pl.BlockSpec((8, KP), lambda b, pr, ct: (0, 0)),
            pl.BlockSpec((tblocks, rowsp, BLK), lambda b, pr, ct: (0, 0, 0)),
        ],
        out_specs=[
            pl.BlockSpec((BLK, 1), lambda b, pr, ct: (b, 0)),
            pl.BlockSpec((tblocks, 1, BLK), lambda b, pr, ct: (0, 0, 0)),
            pl.BlockSpec((tblocks, 1, BLK), lambda b, pr, ct: (0, 0, 0)),
        ],
        scratch_shapes=[pltpu.VMEM((4, BLK, BLK), jnp.float32),
                        pltpu.VMEM((BLK, KP), jnp.bfloat16),
                        pltpu.VMEM((BLK, KP), jnp.bfloat16),
                        pltpu.VMEM((2, BLK, LANE), jnp.float32),
                        pltpu.VMEM((tblocks, KP, BLK), jnp.bfloat16)],
    )
    fpot, gtop, gsum = pl.pallas_call(
        functools.partial(sinkhorn_kernel, npairs, d),
        grid_spec=grid_spec,
        out_shape=[
            jax.ShapeDtypeStruct((ns, 1), jnp.float32),
            jax.ShapeDtypeStruct((tblocks, 1, BLK), jnp.float32),
            jax.ShapeDtypeStruct((tblocks, 1, BLK), jnp.float32),
        ],
        compiler_params=pltpu.CompilerParams(
            dimension_semantics=("arbitrary",), vmem_limit_bytes=100 * 1024 * 1024),
    )(pairs.reshape(-1), counts, xt, xn, ls, expand, sel, blocks)

    src_pot = fpot.reshape(-1)
    parts = jnp.stack([gtop.reshape(ncols, own_targets), gsum.reshape(ncols, own_targets)], axis=1)
    mine = lax.all_to_all(parts, "cols", 0, 0, tiled=True)
    top, total = merge(mine[:, 0, :], mine[:, 1, :], 0)
    here = jnp.concatenate([top, total], axis=0)
    there = lax.ppermute(here, "rows", [(0, 1), (1, 0)])
    both = jnp.stack([jnp.where(first, here, there), jnp.where(first, there, here)])
    top, total = merge(both[:, 0, :], both[:, 1, :], 0)
    new_tgt_pot = (-epsilon * LN2) * (top[0] + jnp.log2(total[0]))
    return (src_pot, new_tgt_pot)


def solution(mesh):
    placed = (
        P(None, ("parts", "rows", "cols")),
        P(None, ("parts", "cols")),
        P(("parts", "cols")),
        P(("parts", "rows", "cols")),
        P(("parts", "cols")),
        P(("parts", "rows", "cols"), None),
        P(("parts", "rows", "cols")),
    )
    return jax.shard_map(
        on_device,
        mesh=mesh,
        in_specs=placed,
        out_specs=(P(("parts", "rows", "cols")), P(("parts", "cols"))),
        check_vma=False,
    )
```

```python
import functools

import jax
import jax.numpy as jnp
from jax import lax
from jax.experimental import pallas as pl
from jax.experimental.pallas import tpu as pltpu
from jax.sharding import PartitionSpec as P

BLK = 256
KP = 128
LANE = 128

epsilon = 0.1
NEG = -1e30
LOG2E = 1.4426950408889634
LN2 = 0.6931471805599453


def split3(v):
    first = lax.reduce_precision(v, exponent_bits=8, mantissa_bits=7)
    rest = v - first
    second = lax.reduce_precision(rest, exponent_bits=8, mantissa_bits=7)
    third = rest - second
    return (first.astype(jnp.bfloat16), second.astype(jnp.bfloat16),
            third.astype(jnp.bfloat16))


def split3_kernel(v):
    first = v.astype(jnp.bfloat16)
    rest = v - first.astype(jnp.float32)
    second = rest.astype(jnp.bfloat16)
    third = (rest - second.astype(jnp.float32)).astype(jnp.bfloat16)
    return first, second, third


def build_table(d, blocks_ref, tab_ref):
    scale = 2.0 * LOG2E / epsilon
    slot_row = lax.broadcasted_iota(jnp.int32, (16, BLK), 0)
    used = 3 * d + 16

    def one(tb, carry):
        blk = blocks_ref[tb]
        y = blk[0:d, :]
        yn = jnp.sum(y * y, axis=0, keepdims=True)
        tp = blk[d:d + 1, :]
        lt = blk[d + 1:d + 2, :]
        acol = (lt + (tp - yn) / epsilon) * LOG2E
        ccol = (-yn / epsilon) * LOG2E
        y1, y2, y3 = split3_kernel(y * scale)
        for k, piece in enumerate([y1, y2, y1]):
            tab_ref[tb, k * d:(k + 1) * d, :] = piece
        slot = jnp.zeros((16, BLK), jnp.float32)
        pieces = list(split3_kernel(acol)) + list(split3_kernel(ccol))
        for k, piece in enumerate(pieces):
            slot = jnp.where(slot_row == k, piece.astype(jnp.float32), slot)
        slot = jnp.where((slot_row >= 6) & (slot_row < 9), 1.0, slot)
        tab_ref[tb, 3 * d:used, :] = slot.astype(jnp.bfloat16)
        tab_ref[tb, used:KP, :] = jnp.zeros((KP - used, BLK), jnp.bfloat16)
        return carry

    lax.fori_loop(0, tab_ref.shape[0], one, 0)


def sinkhorn_kernel(npairs, d, pairs_ref, counts_ref, xt_ref, xn_ref, ls_ref, expand_ref, sel_ref,
                    blocks_ref, fpot_ref, gtop_ref, gsum_ref, sbuf, xr_ref, xc_ref, acc_ref, tab_ref):
    b = pl.program_id(0)

    @pl.when(b == 0)
    def _init():
        gtop_ref[...] = jnp.full(gtop_ref.shape, NEG, jnp.float32)
        gsum_ref[...] = jnp.zeros(gsum_ref.shape, jnp.float32)
        build_table(d, blocks_ref, tab_ref)

    cnt = counts_ref[b]
    base = b * npairs
    x1, x2, x3 = split3_kernel(xt_ref[...])
    xa = (jnp.dot(x1, expand_ref[0], preferred_element_type=jnp.float32)
          + jnp.dot(x2, expand_ref[1], preferred_element_type=jnp.float32)
          + jnp.dot(x3, expand_ref[2], preferred_element_type=jnp.float32))
    sel = sel_ref[...]
    xr_ref[...] = (xa + sel[0:1, :]).astype(jnp.bfloat16)
    acc_ref[0] = jnp.full((BLK, LANE), NEG, jnp.float32)
    acc_ref[1] = jnp.zeros((BLK, LANE), jnp.float32)

    def pairs_of(body):
        def two(k, carry):
            body([2 * k, 2 * k + 1])
            return carry

        lax.fori_loop(0, cnt // 2, two, 0)

        @pl.when(cnt % 2 == 1)
        def _last():
            body([cnt - 1])

    def quads_of(body):
        def four(k, carry):
            body([4 * k + i for i in range(4)])
            return carry

        lax.fori_loop(0, cnt // 4, four, 0)
        done = cnt - cnt % 4

        @pl.when(cnt % 4 >= 2)
        def _pair():
            body([done, done + 1])

        @pl.when(cnt % 2 == 1)
        def _last():
            body([cnt - 1])

    def row_pass(ts):
        halves = []
        for t in ts:
            s = jnp.dot(xr_ref[...], tab_ref[pairs_ref[base + t]], preferred_element_type=jnp.float32)
            halves += [s[:, :LANE], s[:, LANE:]]
        old = acc_ref[0]
        new = old
        for h in halves:
            new = jnp.maximum(new, h)
        total = acc_ref[1] * jnp.exp2(old - new)
        for h in halves:
            total = total + jnp.exp2(h - new)
        acc_ref[0] = new
        acc_ref[1] = total

    pairs_of(row_pass)
    lane_top = acc_ref[0]
    m = jnp.max(lane_top, axis=1, keepdims=True)
    lane_sum = acc_ref[1] * jnp.exp2(lane_top - m)
    lse = m + jnp.log2(jnp.sum(lane_sum, axis=1, keepdims=True))
    fpot_ref[...] = xn_ref[...] - (epsilon * LN2) * lse
    p1, p2, p3 = split3_kernel(ls_ref[...] * LOG2E - lse)
    xc_ref[...] = (xa + sel[1:2, :] + p1.astype(jnp.float32) * sel[2:3, :]
                   + p2.astype(jnp.float32) * sel[3:4, :]
                   + p3.astype(jnp.float32) * sel[4:5, :]).astype(jnp.bfloat16)

    def col_pass(ts):
        for slot, t in enumerate(ts):
            tb = pairs_ref[base + t]
            u = jnp.dot(xc_ref[...], tab_ref[tb], preferred_element_type=jnp.float32)
            sbuf[slot] = u
            cm = jnp.max(u, axis=0, keepdims=True)
            cs = jnp.sum(jnp.exp2(sbuf[slot] - cm), axis=0, keepdims=True)
            old = gtop_ref[tb]
            new = jnp.maximum(old, cm)
            gsum_ref[tb] = gsum_ref[tb] * jnp.exp2(old - new) + cs * jnp.exp2(cm - new)
            gtop_ref[tb] = new

    quads_of(col_pass)


def merge(tops, sums, axis):
    top = jnp.max(tops, axis=axis, keepdims=True)
    total = jnp.sum(sums * jnp.exp2(tops - top), axis=axis, keepdims=True)
    return top, total


def on_device(src_feat, tgt_feat, tgt_pot, log_src, log_tgt, pairs, counts):
    d = src_feat.shape[0]
    ns = src_feat.shape[1]
    nrb = ns // BLK
    npairs = pairs.shape[1]
    own_targets = tgt_feat.shape[1]
    ncols = lax.axis_size("cols")

    packed = jnp.concatenate([tgt_feat, tgt_pot[None, :], log_tgt[None, :]], axis=0)
    rowsp = packed.shape[0]
    nrows = lax.axis_size("rows")
    share = rowsp // nrows
    mine = lax.dynamic_slice_in_dim(packed, lax.axis_index("rows") * share, share, 0)
    spread = jnp.broadcast_to(mine[None], (ncols, share, own_targets))
    halves = lax.all_to_all(spread, "cols", 0, 0, tiled=True)
    other = lax.ppermute(halves, "rows", [(0, 1), (1, 0)])
    first = lax.axis_index("rows") == 0
    gathered = jnp.concatenate(
        [jnp.where(first, halves, other), jnp.where(first, other, halves)], axis=1)
    nt = ncols * own_targets
    tblocks = nt // BLK
    blocks = jnp.transpose(
        gathered.reshape(ncols, rowsp, own_targets // BLK, BLK), (0, 2, 1, 3)).reshape(tblocks, rowsp, BLK)

    col = jnp.arange(KP, dtype=jnp.int32)[None, :]
    comp = jnp.arange(d, dtype=jnp.int32)[:, None]
    def place(starts):
        hit = jnp.zeros((d, KP), bool)
        for s in starts:
            hit = hit | (col == comp + s)
        return hit.astype(jnp.bfloat16)
    expand = jnp.stack([place([0, d]), place([2 * d]), place([])])
    k0 = 3 * d
    sel = jnp.stack([
        ((col[0] >= k0) & (col[0] < k0 + 3)),
        ((col[0] >= k0 + 3) & (col[0] < k0 + 6)),
        col[0] == k0 + 6, col[0] == k0 + 7, col[0] == k0 + 8,
        col[0] < 0, col[0] < 0, col[0] < 0,
    ]).astype(jnp.float32)

    kept = (nrb // 2) * BLK
    kept_blocks = nrb // 2
    swap = [(0, 1), (1, 0)]
    feats = jnp.concatenate([src_feat, log_src[None, :]], axis=0)
    feats = jnp.concatenate([feats[:, :kept], lax.ppermute(feats[:, kept:], "rows", swap)], axis=1)
    lists = jnp.concatenate([pairs, counts[:, None]], axis=1)
    lists = jnp.concatenate([lists[:kept_blocks], lax.ppermute(lists[kept_blocks:], "rows", swap)], axis=0)
    src_feat = feats[:d]
    pairs = lists[:, :npairs]
    counts = lists[:, npairs]
    xt = jnp.transpose(src_feat)
    xn = jnp.sum(src_feat * src_feat, axis=0)[:, None]
    ls = feats[d][:, None]

    grid_spec = pltpu.PrefetchScalarGridSpec(
        num_scalar_prefetch=2,
        grid=(nrb,),
        in_specs=[
            pl.BlockSpec((BLK, d), lambda b, pr, ct: (b, 0)),
            pl.BlockSpec((BLK, 1), lambda b, pr, ct: (b, 0)),
            pl.BlockSpec((BLK, 1), lambda b, pr, ct: (b, 0)),
            pl.BlockSpec((3, d, KP), lambda b, pr, ct: (0, 0, 0)),
            pl.BlockSpec((8, KP), lambda b, pr, ct: (0, 0)),
            pl.BlockSpec((tblocks, rowsp, BLK), lambda b, pr, ct: (0, 0, 0)),
        ],
        out_specs=[
            pl.BlockSpec((BLK, 1), lambda b, pr, ct: (b, 0)),
            pl.BlockSpec((tblocks, 1, BLK), lambda b, pr, ct: (0, 0, 0)),
            pl.BlockSpec((tblocks, 1, BLK), lambda b, pr, ct: (0, 0, 0)),
        ],
        scratch_shapes=[pltpu.VMEM((4, BLK, BLK), jnp.float32),
                        pltpu.VMEM((BLK, KP), jnp.bfloat16),
                        pltpu.VMEM((BLK, KP), jnp.bfloat16),
                        pltpu.VMEM((2, BLK, LANE), jnp.float32),
                        pltpu.VMEM((tblocks, KP, BLK), jnp.bfloat16)],
    )
    fpot, gtop, gsum = pl.pallas_call(
        functools.partial(sinkhorn_kernel, npairs, d),
        grid_spec=grid_spec,
        out_shape=[
            jax.ShapeDtypeStruct((ns, 1), jnp.float32),
            jax.ShapeDtypeStruct((tblocks, 1, BLK), jnp.float32),
            jax.ShapeDtypeStruct((tblocks, 1, BLK), jnp.float32),
        ],
        compiler_params=pltpu.CompilerParams(
            dimension_semantics=("arbitrary",), vmem_limit_bytes=100 * 1024 * 1024),
    )(pairs.reshape(-1), counts, xt, xn, ls, expand, sel, blocks)

    done = fpot.reshape(-1)
    src_pot = jnp.concatenate([done[:kept], lax.ppermute(done[kept:], "rows", swap)])
    parts = jnp.stack([gtop.reshape(ncols, own_targets), gsum.reshape(ncols, own_targets)], axis=1)
    mine = lax.all_to_all(parts, "cols", 0, 0, tiled=True)
    top, total = merge(mine[:, 0, :], mine[:, 1, :], 0)
    here = jnp.concatenate([top, total], axis=0)
    there = lax.ppermute(here, "rows", [(0, 1), (1, 0)])
    both = jnp.stack([jnp.where(first, here, there), jnp.where(first, there, here)])
    top, total = merge(both[:, 0, :], both[:, 1, :], 0)
    new_tgt_pot = (-epsilon * LN2) * (top[0] + jnp.log2(total[0]))
    return (src_pot, new_tgt_pot)


def solution(mesh):
    placed = (
        P(None, ("parts", "rows", "cols")),
        P(None, ("parts", "cols")),
        P(("parts", "cols")),
        P(("parts", "rows", "cols")),
        P(("parts", "cols")),
        P(("parts", "rows", "cols"), None),
        P(("parts", "rows", "cols")),
    )
    return jax.shard_map(
        on_device,
        mesh=mesh,
        in_specs=placed,
        out_specs=(P(("parts", "rows", "cols")), P(("parts", "cols"))),
        check_vma=False,
    )
```

```python
import functools

import jax
import jax.numpy as jnp
from jax import lax
from jax.experimental import pallas as pl
from jax.experimental.pallas import tpu as pltpu
from jax.sharding import PartitionSpec as P

BLK = 256
KP = 128
LANE = 128

epsilon = 0.1
NEG = -1e30
LOG2E = 1.4426950408889634
LN2 = 0.6931471805599453


def split3(v):
    first = lax.reduce_precision(v, exponent_bits=8, mantissa_bits=7)
    rest = v - first
    second = lax.reduce_precision(rest, exponent_bits=8, mantissa_bits=7)
    third = rest - second
    return (first.astype(jnp.bfloat16), second.astype(jnp.bfloat16),
            third.astype(jnp.bfloat16))


def split3_kernel(v):
    first = v.astype(jnp.bfloat16)
    rest = v - first.astype(jnp.float32)
    second = rest.astype(jnp.bfloat16)
    third = (rest - second.astype(jnp.float32)).astype(jnp.bfloat16)
    return first, second, third


def build_table(d, blocks_ref, tab_ref):
    scale = 2.0 * LOG2E / epsilon
    slot_row = lax.broadcasted_iota(jnp.int32, (16, BLK), 0)
    used = 3 * d + 16

    def one(tb, carry):
        blk = blocks_ref[tb]
        y = blk[0:d, :]
        yn = jnp.sum(y * y, axis=0, keepdims=True)
        tp = blk[d:d + 1, :]
        lt = blk[d + 1:d + 2, :]
        acol = (lt + (tp - yn) / epsilon) * LOG2E
        ccol = (-yn / epsilon) * LOG2E
        y1, y2, y3 = split3_kernel(y * scale)
        for k, piece in enumerate([y1, y2, y1]):
            tab_ref[tb, k * d:(k + 1) * d, :] = piece
        slot = jnp.zeros((16, BLK), jnp.float32)
        pieces = list(split3_kernel(acol)) + list(split3_kernel(ccol))
        for k, piece in enumerate(pieces):
            slot = jnp.where(slot_row == k, piece.astype(jnp.float32), slot)
        slot = jnp.where((slot_row >= 6) & (slot_row < 9), 1.0, slot)
        tab_ref[tb, 3 * d:used, :] = slot.astype(jnp.bfloat16)
        tab_ref[tb, used:KP, :] = jnp.zeros((KP - used, BLK), jnp.bfloat16)
        return carry

    lax.fori_loop(0, tab_ref.shape[0], one, 0)


def sinkhorn_kernel(npairs, d, pairs_ref, counts_ref, xt_ref, expand_ref, sel_ref,
                    blocks_ref, fpot_ref, gtop_ref, gsum_ref, sbuf, xr_ref, xc_ref, acc_ref, tab_ref):
    b = pl.program_id(0)

    @pl.when(b == 0)
    def _init():
        gtop_ref[...] = jnp.full(gtop_ref.shape, NEG, jnp.float32)
        gsum_ref[...] = jnp.zeros(gsum_ref.shape, jnp.float32)
        build_table(d, blocks_ref, tab_ref)

    cnt = counts_ref[b]
    base = b * npairs
    xfull = xt_ref[...]
    xs = xfull[:, :d]
    ls = xfull[:, d:d + 1]
    xn = jnp.sum(xs * xs, axis=1, keepdims=True)
    x1, x2, x3 = split3_kernel(xs)
    xa = (jnp.dot(x1, expand_ref[0], preferred_element_type=jnp.float32)
          + jnp.dot(x2, expand_ref[1], preferred_element_type=jnp.float32)
          + jnp.dot(x3, expand_ref[2], preferred_element_type=jnp.float32))
    sel = sel_ref[...]
    xr_ref[...] = (xa + sel[0:1, :]).astype(jnp.bfloat16)
    acc_ref[0] = jnp.full((BLK, LANE), NEG, jnp.float32)
    acc_ref[1] = jnp.zeros((BLK, LANE), jnp.float32)

    def pairs_of(body):
        def two(k, carry):
            body([2 * k, 2 * k + 1])
            return carry

        lax.fori_loop(0, cnt // 2, two, 0)

        @pl.when(cnt % 2 == 1)
        def _last():
            body([cnt - 1])

    def quads_of(body):
        def four(k, carry):
            body([4 * k + i for i in range(4)])
            return carry

        lax.fori_loop(0, cnt // 4, four, 0)
        done = cnt - cnt % 4

        @pl.when(cnt % 4 >= 2)
        def _pair():
            body([done, done + 1])

        @pl.when(cnt % 2 == 1)
        def _last():
            body([cnt - 1])

    def row_pass(ts):
        halves = []
        for t in ts:
            s = jnp.dot(xr_ref[...], tab_ref[pairs_ref[base + t]], preferred_element_type=jnp.float32)
            halves += [s[:, :LANE], s[:, LANE:]]
        old = acc_ref[0]
        new = old
        for h in halves:
            new = jnp.maximum(new, h)
        total = acc_ref[1] * jnp.exp2(old - new)
        for h in halves:
            total = total + jnp.exp2(h - new)
        acc_ref[0] = new
        acc_ref[1] = total

    pairs_of(row_pass)
    lane_top = acc_ref[0]
    m = jnp.max(lane_top, axis=1, keepdims=True)
    lane_sum = acc_ref[1] * jnp.exp2(lane_top - m)
    lse = m + jnp.log2(jnp.sum(lane_sum, axis=1, keepdims=True))
    fpot_ref[...] = xn - (epsilon * LN2) * lse
    p1, p2, p3 = split3_kernel(ls * LOG2E - lse)
    xc_ref[...] = (xa + sel[1:2, :] + p1.astype(jnp.float32) * sel[2:3, :]
                   + p2.astype(jnp.float32) * sel[3:4, :]
                   + p3.astype(jnp.float32) * sel[4:5, :]).astype(jnp.bfloat16)

    def col_pass(ts):
        for slot, t in enumerate(ts):
            tb = pairs_ref[base + t]
            u = jnp.dot(xc_ref[...], tab_ref[tb], preferred_element_type=jnp.float32)
            sbuf[slot] = u
            cm = jnp.max(u, axis=0, keepdims=True)
            cs = jnp.sum(jnp.exp2(sbuf[slot] - cm), axis=0, keepdims=True)
            old = gtop_ref[tb]
            new = jnp.maximum(old, cm)
            gsum_ref[tb] = gsum_ref[tb] * jnp.exp2(old - new) + cs * jnp.exp2(cm - new)
            gtop_ref[tb] = new

    quads_of(col_pass)


def merge(tops, sums, axis):
    top = jnp.max(tops, axis=axis, keepdims=True)
    total = jnp.sum(sums * jnp.exp2(tops - top), axis=axis, keepdims=True)
    return top, total


def on_device(src_feat, tgt_feat, tgt_pot, log_src, log_tgt, pairs, counts):
    d = src_feat.shape[0]
    ns = src_feat.shape[1]
    nrb = ns // BLK
    npairs = pairs.shape[1]
    own_targets = tgt_feat.shape[1]
    ncols = lax.axis_size("cols")

    packed = jnp.concatenate([tgt_feat, tgt_pot[None, :], log_tgt[None, :]], axis=0)
    rowsp = packed.shape[0]
    nrows = lax.axis_size("rows")
    share = rowsp // nrows
    mine = lax.dynamic_slice_in_dim(packed, lax.axis_index("rows") * share, share, 0)
    spread = jnp.broadcast_to(mine[None], (ncols, share, own_targets))
    halves = lax.all_to_all(spread, "cols", 0, 0, tiled=True)
    other = lax.ppermute(halves, "rows", [(0, 1), (1, 0)])
    first = lax.axis_index("rows") == 0
    gathered = jnp.concatenate(
        [jnp.where(first, halves, other), jnp.where(first, other, halves)], axis=1)
    nt = ncols * own_targets
    tblocks = nt // BLK
    blocks = jnp.transpose(
        gathered.reshape(ncols, rowsp, own_targets // BLK, BLK), (0, 2, 1, 3)).reshape(tblocks, rowsp, BLK)

    col = jnp.arange(KP, dtype=jnp.int32)[None, :]
    comp = jnp.arange(d, dtype=jnp.int32)[:, None]
    def place(starts):
        hit = jnp.zeros((d, KP), bool)
        for s in starts:
            hit = hit | (col == comp + s)
        return hit.astype(jnp.bfloat16)
    expand = jnp.stack([place([0, d]), place([2 * d]), place([])])
    k0 = 3 * d
    sel = jnp.stack([
        ((col[0] >= k0) & (col[0] < k0 + 3)),
        ((col[0] >= k0 + 3) & (col[0] < k0 + 6)),
        col[0] == k0 + 6, col[0] == k0 + 7, col[0] == k0 + 8,
        col[0] < 0, col[0] < 0, col[0] < 0,
    ]).astype(jnp.float32)

    kept = (nrb // 2) * BLK
    kept_blocks = nrb // 2
    swap = [(0, 1), (1, 0)]
    feats = jnp.concatenate([src_feat, log_src[None, :]], axis=0)
    feats = jnp.concatenate([feats[:, :kept], lax.ppermute(feats[:, kept:], "rows", swap)], axis=1)
    lists = jnp.concatenate([pairs, counts[:, None]], axis=1)
    lists = jnp.concatenate([lists[:kept_blocks], lax.ppermute(lists[kept_blocks:], "rows", swap)], axis=0)
    src_feat = feats[:d]
    pairs = lists[:, :npairs]
    counts = lists[:, npairs]
    xt = jnp.transpose(feats)

    grid_spec = pltpu.PrefetchScalarGridSpec(
        num_scalar_prefetch=2,
        grid=(nrb,),
        in_specs=[
            pl.BlockSpec((BLK, d + 1), lambda b, pr, ct: (b, 0)),
            pl.BlockSpec((3, d, KP), lambda b, pr, ct: (0, 0, 0)),
            pl.BlockSpec((8, KP), lambda b, pr, ct: (0, 0)),
            pl.BlockSpec((tblocks, rowsp, BLK), lambda b, pr, ct: (0, 0, 0)),
        ],
        out_specs=[
            pl.BlockSpec((BLK, 1), lambda b, pr, ct: (b, 0)),
            pl.BlockSpec((tblocks, 1, BLK), lambda b, pr, ct: (0, 0, 0)),
            pl.BlockSpec((tblocks, 1, BLK), lambda b, pr, ct: (0, 0, 0)),
        ],
        scratch_shapes=[pltpu.VMEM((4, BLK, BLK), jnp.float32),
                        pltpu.VMEM((BLK, KP), jnp.bfloat16),
                        pltpu.VMEM((BLK, KP), jnp.bfloat16),
                        pltpu.VMEM((2, BLK, LANE), jnp.float32),
                        pltpu.VMEM((tblocks, KP, BLK), jnp.bfloat16)],
    )
    fpot, gtop, gsum = pl.pallas_call(
        functools.partial(sinkhorn_kernel, npairs, d),
        grid_spec=grid_spec,
        out_shape=[
            jax.ShapeDtypeStruct((ns, 1), jnp.float32),
            jax.ShapeDtypeStruct((tblocks, 1, BLK), jnp.float32),
            jax.ShapeDtypeStruct((tblocks, 1, BLK), jnp.float32),
        ],
        compiler_params=pltpu.CompilerParams(
            dimension_semantics=("arbitrary",), vmem_limit_bytes=100 * 1024 * 1024),
    )(pairs.reshape(-1), counts, xt, expand, sel, blocks)

    done = fpot.reshape(-1)
    src_pot = jnp.concatenate([done[:kept], lax.ppermute(done[kept:], "rows", swap)])
    parts = jnp.stack([gtop.reshape(ncols, own_targets), gsum.reshape(ncols, own_targets)], axis=1)
    mine = lax.all_to_all(parts, "cols", 0, 0, tiled=True)
    top, total = merge(mine[:, 0, :], mine[:, 1, :], 0)
    here = jnp.concatenate([top, total], axis=0)
    there = lax.ppermute(here, "rows", [(0, 1), (1, 0)])
    both = jnp.stack([jnp.where(first, here, there), jnp.where(first, there, here)])
    top, total = merge(both[:, 0, :], both[:, 1, :], 0)
    new_tgt_pot = (-epsilon * LN2) * (top[0] + jnp.log2(total[0]))
    return (src_pot, new_tgt_pot)


def solution(mesh):
    placed = (
        P(None, ("parts", "rows", "cols")),
        P(None, ("parts", "cols")),
        P(("parts", "cols")),
        P(("parts", "rows", "cols")),
        P(("parts", "cols")),
        P(("parts", "rows", "cols"), None),
        P(("parts", "rows", "cols")),
    )
    return jax.shard_map(
        on_device,
        mesh=mesh,
        in_specs=placed,
        out_specs=(P(("parts", "rows", "cols")), P(("parts", "cols"))),
        check_vma=False,
    )
```

```python
import functools

import jax
import jax.numpy as jnp
from jax import lax
from jax.experimental import pallas as pl
from jax.experimental.pallas import tpu as pltpu
from jax.sharding import PartitionSpec as P

BLK = 256
KP = 128
LANE = 128

epsilon = 0.1
NEG = -1e30
LOG2E = 1.4426950408889634
LN2 = 0.6931471805599453


def split3(v):
    first = lax.reduce_precision(v, exponent_bits=8, mantissa_bits=7)
    rest = v - first
    second = lax.reduce_precision(rest, exponent_bits=8, mantissa_bits=7)
    third = rest - second
    return (first.astype(jnp.bfloat16), second.astype(jnp.bfloat16),
            third.astype(jnp.bfloat16))


def split3_kernel(v):
    first = v.astype(jnp.bfloat16)
    rest = v - first.astype(jnp.float32)
    second = rest.astype(jnp.bfloat16)
    third = (rest - second.astype(jnp.float32)).astype(jnp.bfloat16)
    return first, second, third


def build_table(d, blocks_ref, tab_ref):
    scale = 2.0 * LOG2E / epsilon
    slot_row = lax.broadcasted_iota(jnp.int32, (16, BLK), 0)
    used = 3 * d + 16

    def one(tb, carry):
        blk = blocks_ref[tb]
        y = blk[0:d, :]
        yn = jnp.sum(y * y, axis=0, keepdims=True)
        tp = blk[d:d + 1, :]
        lt = blk[d + 1:d + 2, :]
        acol = (lt + (tp - yn) / epsilon) * LOG2E
        ccol = (-yn / epsilon) * LOG2E
        y1, y2, y3 = split3_kernel(y * scale)
        for k, piece in enumerate([y1, y2, y1]):
            tab_ref[tb, k * d:(k + 1) * d, :] = piece
        slot = jnp.zeros((16, BLK), jnp.float32)
        pieces = list(split3_kernel(acol)) + list(split3_kernel(ccol))
        for k, piece in enumerate(pieces):
            slot = jnp.where(slot_row == k, piece.astype(jnp.float32), slot)
        slot = jnp.where((slot_row >= 6) & (slot_row < 9), 1.0, slot)
        tab_ref[tb, 3 * d:used, :] = slot.astype(jnp.bfloat16)
        tab_ref[tb, used:KP, :] = jnp.zeros((KP - used, BLK), jnp.bfloat16)
        return carry

    lax.fori_loop(0, tab_ref.shape[0], one, 0)


def sinkhorn_kernel(npairs, d, pairs_ref, counts_ref, xt_ref, expand_ref, sel_ref,
                    blocks_ref, fpot_ref, gtop_ref, gsum_ref, sbuf, xr_ref, xc_ref, acc_ref, tab_ref):
    b = pl.program_id(0)

    @pl.when(b == 0)
    def _init():
        gtop_ref[...] = jnp.full(gtop_ref.shape, NEG, jnp.float32)
        gsum_ref[...] = jnp.zeros(gsum_ref.shape, jnp.float32)
        build_table(d, blocks_ref, tab_ref)

    cnt = counts_ref[b]
    base = b * npairs
    xfull = xt_ref[...]
    xs = xfull[:, :d]
    ls = xfull[:, d:d + 1]
    xn = jnp.sum(xs * xs, axis=1, keepdims=True)
    x1, x2, x3 = split3_kernel(xs)
    xa = (jnp.dot(x1, expand_ref[0], preferred_element_type=jnp.float32)
          + jnp.dot(x2, expand_ref[1], preferred_element_type=jnp.float32)
          + jnp.dot(x3, expand_ref[2], preferred_element_type=jnp.float32))
    sel = sel_ref[...]
    xr_ref[...] = (xa + sel[0:1, :]).astype(jnp.bfloat16)
    acc_ref[0] = jnp.full((BLK, LANE), NEG, jnp.float32)
    acc_ref[1] = jnp.zeros((BLK, LANE), jnp.float32)

    def pairs_of(body):
        def two(k, carry):
            body([2 * k, 2 * k + 1])
            return carry

        lax.fori_loop(0, cnt // 2, two, 0)

        @pl.when(cnt % 2 == 1)
        def _last():
            body([cnt - 1])

    def quads_of(body):
        def four(k, carry):
            body([4 * k + i for i in range(4)])
            return carry

        lax.fori_loop(0, cnt // 4, four, 0)
        done = cnt - cnt % 4

        @pl.when(cnt % 4 >= 2)
        def _pair():
            body([done, done + 1])

        @pl.when(cnt % 2 == 1)
        def _last():
            body([cnt - 1])

    def row_pass(ts):
        halves = []
        for t in ts:
            s = jnp.dot(xr_ref[...], tab_ref[pairs_ref[base + t]], preferred_element_type=jnp.float32)
            halves += [s[:, :LANE], s[:, LANE:]]
        old = acc_ref[0]
        new = old
        for h in halves:
            new = jnp.maximum(new, h)
        total = acc_ref[1] * jnp.exp2(old - new)
        for h in halves:
            total = total + jnp.exp2(h - new)
        acc_ref[0] = new
        acc_ref[1] = total

    pairs_of(row_pass)
    lane_top = acc_ref[0]
    m = jnp.max(lane_top, axis=1, keepdims=True)
    lane_sum = acc_ref[1] * jnp.exp2(lane_top - m)
    lse = m + jnp.log2(jnp.sum(lane_sum, axis=1, keepdims=True))
    fpot_ref[...] = xn - (epsilon * LN2) * lse
    p1, p2, p3 = split3_kernel(ls * LOG2E - lse)
    xc_ref[...] = (xa + sel[1:2, :] + p1.astype(jnp.float32) * sel[2:3, :]
                   + p2.astype(jnp.float32) * sel[3:4, :]
                   + p3.astype(jnp.float32) * sel[4:5, :]).astype(jnp.bfloat16)

    def col_pass(ts):
        for slot, t in enumerate(ts):
            tb = pairs_ref[base + t]
            u = jnp.dot(xc_ref[...], tab_ref[tb], preferred_element_type=jnp.float32)
            sbuf[slot] = u
            cm = jnp.max(u, axis=0, keepdims=True)
            cs = jnp.sum(jnp.exp2(sbuf[slot] - cm), axis=0, keepdims=True)
            old = gtop_ref[tb]
            new = jnp.maximum(old, cm)
            gsum_ref[tb] = gsum_ref[tb] * jnp.exp2(old - new) + cs * jnp.exp2(cm - new)
            gtop_ref[tb] = new

    quads_of(col_pass)


def merge(tops, sums, axis):
    top = jnp.max(tops, axis=axis, keepdims=True)
    total = jnp.sum(sums * jnp.exp2(tops - top), axis=axis, keepdims=True)
    return top, total


def on_device(src_feat, tgt_feat, tgt_pot, log_src, log_tgt, pairs, counts):
    d = src_feat.shape[0]
    ns = src_feat.shape[1]
    nrb = ns // BLK
    npairs = pairs.shape[1]
    own_targets = tgt_feat.shape[1]
    ncols = lax.axis_size("cols")

    packed = jnp.concatenate([tgt_feat, tgt_pot[None, :], log_tgt[None, :]], axis=0)
    rowsp = packed.shape[0]
    nrows = lax.axis_size("rows")
    share = rowsp // nrows
    mine = lax.dynamic_slice_in_dim(packed, lax.axis_index("rows") * share, share, 0)
    halves = mine[None]
    col_index = lax.axis_index("cols")
    step = 1
    while step < ncols:
        partner = lax.ppermute(halves, "cols", [(i, i ^ step) for i in range(ncols)])
        low = (col_index & step) == 0
        halves = jnp.concatenate(
            [jnp.where(low, halves, partner), jnp.where(low, partner, halves)], axis=0)
        step *= 2
    other = lax.ppermute(halves, "rows", [(0, 1), (1, 0)])
    first = lax.axis_index("rows") == 0
    gathered = jnp.concatenate(
        [jnp.where(first, halves, other), jnp.where(first, other, halves)], axis=1)
    nt = ncols * own_targets
    tblocks = nt // BLK
    blocks = jnp.transpose(
        gathered.reshape(ncols, rowsp, own_targets // BLK, BLK), (0, 2, 1, 3)).reshape(tblocks, rowsp, BLK)

    col = jnp.arange(KP, dtype=jnp.int32)[None, :]
    comp = jnp.arange(d, dtype=jnp.int32)[:, None]
    def place(starts):
        hit = jnp.zeros((d, KP), bool)
        for s in starts:
            hit = hit | (col == comp + s)
        return hit.astype(jnp.bfloat16)
    expand = jnp.stack([place([0, d]), place([2 * d]), place([])])
    k0 = 3 * d
    sel = jnp.stack([
        ((col[0] >= k0) & (col[0] < k0 + 3)),
        ((col[0] >= k0 + 3) & (col[0] < k0 + 6)),
        col[0] == k0 + 6, col[0] == k0 + 7, col[0] == k0 + 8,
        col[0] < 0, col[0] < 0, col[0] < 0,
    ]).astype(jnp.float32)

    kept = (nrb // 2) * BLK
    kept_blocks = nrb // 2
    swap = [(0, 1), (1, 0)]
    feats = jnp.concatenate([src_feat, log_src[None, :]], axis=0)
    feats = jnp.concatenate([feats[:, :kept], lax.ppermute(feats[:, kept:], "rows", swap)], axis=1)
    lists = jnp.concatenate([pairs, counts[:, None]], axis=1)
    lists = jnp.concatenate([lists[:kept_blocks], lax.ppermute(lists[kept_blocks:], "rows", swap)], axis=0)
    src_feat = feats[:d]
    pairs = lists[:, :npairs]
    counts = lists[:, npairs]
    xt = jnp.transpose(feats)

    grid_spec = pltpu.PrefetchScalarGridSpec(
        num_scalar_prefetch=2,
        grid=(nrb,),
        in_specs=[
            pl.BlockSpec((BLK, d + 1), lambda b, pr, ct: (b, 0)),
            pl.BlockSpec((3, d, KP), lambda b, pr, ct: (0, 0, 0)),
            pl.BlockSpec((8, KP), lambda b, pr, ct: (0, 0)),
            pl.BlockSpec((tblocks, rowsp, BLK), lambda b, pr, ct: (0, 0, 0)),
        ],
        out_specs=[
            pl.BlockSpec((BLK, 1), lambda b, pr, ct: (b, 0)),
            pl.BlockSpec((tblocks, 1, BLK), lambda b, pr, ct: (0, 0, 0)),
            pl.BlockSpec((tblocks, 1, BLK), lambda b, pr, ct: (0, 0, 0)),
        ],
        scratch_shapes=[pltpu.VMEM((4, BLK, BLK), jnp.float32),
                        pltpu.VMEM((BLK, KP), jnp.bfloat16),
                        pltpu.VMEM((BLK, KP), jnp.bfloat16),
                        pltpu.VMEM((2, BLK, LANE), jnp.float32),
                        pltpu.VMEM((tblocks, KP, BLK), jnp.bfloat16)],
    )
    fpot, gtop, gsum = pl.pallas_call(
        functools.partial(sinkhorn_kernel, npairs, d),
        grid_spec=grid_spec,
        out_shape=[
            jax.ShapeDtypeStruct((ns, 1), jnp.float32),
            jax.ShapeDtypeStruct((tblocks, 1, BLK), jnp.float32),
            jax.ShapeDtypeStruct((tblocks, 1, BLK), jnp.float32),
        ],
        compiler_params=pltpu.CompilerParams(
            dimension_semantics=("arbitrary",), vmem_limit_bytes=100 * 1024 * 1024),
    )(pairs.reshape(-1), counts, xt, expand, sel, blocks)

    done = fpot.reshape(-1)
    src_pot = jnp.concatenate([done[:kept], lax.ppermute(done[kept:], "rows", swap)])
    parts = jnp.stack([gtop.reshape(ncols, own_targets), gsum.reshape(ncols, own_targets)], axis=1)
    mine = lax.all_to_all(parts, "cols", 0, 0, tiled=True)
    top, total = merge(mine[:, 0, :], mine[:, 1, :], 0)
    here = jnp.concatenate([top, total], axis=0)
    there = lax.ppermute(here, "rows", [(0, 1), (1, 0)])
    both = jnp.stack([jnp.where(first, here, there), jnp.where(first, there, here)])
    top, total = merge(both[:, 0, :], both[:, 1, :], 0)
    new_tgt_pot = (-epsilon * LN2) * (top[0] + jnp.log2(total[0]))
    return (src_pot, new_tgt_pot)


def solution(mesh):
    placed = (
        P(None, ("parts", "rows", "cols")),
        P(None, ("parts", "cols")),
        P(("parts", "cols")),
        P(("parts", "rows", "cols")),
        P(("parts", "cols")),
        P(("parts", "rows", "cols"), None),
        P(("parts", "rows", "cols")),
    )
    return jax.shard_map(
        on_device,
        mesh=mesh,
        in_specs=placed,
        out_specs=(P(("parts", "rows", "cols")), P(("parts", "cols"))),
        check_vma=False,
    )
```

```python
import functools

import jax
import jax.numpy as jnp
from jax import lax
from jax.experimental import pallas as pl
from jax.experimental.pallas import tpu as pltpu
from jax.sharding import PartitionSpec as P

BLK = 256
KP = 128
LANE = 128

epsilon = 0.1
NEG = -1e30
LOG2E = 1.4426950408889634
LN2 = 0.6931471805599453


def split3(v):
    first = lax.reduce_precision(v, exponent_bits=8, mantissa_bits=7)
    rest = v - first
    second = lax.reduce_precision(rest, exponent_bits=8, mantissa_bits=7)
    third = rest - second
    return (first.astype(jnp.bfloat16), second.astype(jnp.bfloat16),
            third.astype(jnp.bfloat16))


def split3_kernel(v):
    first = v.astype(jnp.bfloat16)
    rest = v - first.astype(jnp.float32)
    second = rest.astype(jnp.bfloat16)
    third = (rest - second.astype(jnp.float32)).astype(jnp.bfloat16)
    return first, second, third


def build_table(d, blocks_ref, tab_ref):
    scale = 2.0 * LOG2E / epsilon
    slot_row = lax.broadcasted_iota(jnp.int32, (16, BLK), 0)
    used = 3 * d + 16

    def one(tb, carry):
        blk = blocks_ref[tb]
        y = blk[0:d, :]
        yn = jnp.sum(y * y, axis=0, keepdims=True)
        tp = blk[d:d + 1, :]
        lt = blk[d + 1:d + 2, :]
        acol = (lt + (tp - yn) / epsilon) * LOG2E
        ccol = (-yn / epsilon) * LOG2E
        y1, y2, y3 = split3_kernel(y * scale)
        for k, piece in enumerate([y1, y2, y1]):
            tab_ref[tb, k * d:(k + 1) * d, :] = piece
        slot = jnp.zeros((16, BLK), jnp.float32)
        pieces = list(split3_kernel(acol)) + list(split3_kernel(ccol))
        for k, piece in enumerate(pieces):
            slot = jnp.where(slot_row == k, piece.astype(jnp.float32), slot)
        slot = jnp.where((slot_row >= 6) & (slot_row < 9), 1.0, slot)
        tab_ref[tb, 3 * d:used, :] = slot.astype(jnp.bfloat16)
        tab_ref[tb, used:KP, :] = jnp.zeros((KP - used, BLK), jnp.bfloat16)
        return carry

    lax.fori_loop(0, tab_ref.shape[0], one, 0)


def sinkhorn_kernel(npairs, d, pairs_ref, counts_ref, xt_ref, expand_ref, sel_ref,
                    blocks_ref, fpot_ref, gtop_ref, gsum_ref, sbuf, xr_ref, xc_ref, acc_ref, tab_ref):
    b = pl.program_id(0)

    @pl.when(b == 0)
    def _init():
        gtop_ref[...] = jnp.full(gtop_ref.shape, NEG, jnp.float32)
        gsum_ref[...] = jnp.zeros(gsum_ref.shape, jnp.float32)
        build_table(d, blocks_ref, tab_ref)

    cnt = counts_ref[b]
    base = b * npairs
    xfull = xt_ref[...]
    xs = xfull[:, :d]
    ls = xfull[:, d:d + 1]
    xn = jnp.sum(xs * xs, axis=1, keepdims=True)
    x1, x2, x3 = split3_kernel(xs)
    xa = (jnp.dot(x1, expand_ref[0], preferred_element_type=jnp.float32)
          + jnp.dot(x2, expand_ref[1], preferred_element_type=jnp.float32)
          + jnp.dot(x3, expand_ref[2], preferred_element_type=jnp.float32))
    sel = sel_ref[...]
    xr_ref[...] = (xa + sel[0:1, :]).astype(jnp.bfloat16)
    acc_ref[0] = jnp.full((BLK, LANE), NEG, jnp.float32)
    acc_ref[1] = jnp.zeros((BLK, LANE), jnp.float32)

    def pairs_of(body):
        def two(k, carry):
            body([2 * k, 2 * k + 1])
            return carry

        lax.fori_loop(0, cnt // 2, two, 0)

        @pl.when(cnt % 2 == 1)
        def _last():
            body([cnt - 1])

    def quads_of(body):
        def four(k, carry):
            body([4 * k + i for i in range(4)])
            return carry

        lax.fori_loop(0, cnt // 4, four, 0)
        done = cnt - cnt % 4

        @pl.when(cnt % 4 >= 2)
        def _pair():
            body([done, done + 1])

        @pl.when(cnt % 2 == 1)
        def _last():
            body([cnt - 1])

    def row_pass(ts):
        halves = []
        for t in ts:
            s = jnp.dot(xr_ref[...], tab_ref[pairs_ref[base + t]], preferred_element_type=jnp.float32)
            halves += [s[:, :LANE], s[:, LANE:]]
        old = acc_ref[0]
        new = old
        for h in halves:
            new = jnp.maximum(new, h)
        total = acc_ref[1] * jnp.exp2(old - new)
        for h in halves:
            total = total + jnp.exp2(h - new)
        acc_ref[0] = new
        acc_ref[1] = total

    pairs_of(row_pass)
    lane_top = acc_ref[0]
    m = jnp.max(lane_top, axis=1, keepdims=True)
    lane_sum = acc_ref[1] * jnp.exp2(lane_top - m)
    lse = m + jnp.log2(jnp.sum(lane_sum, axis=1, keepdims=True))
    fpot_ref[...] = xn - (epsilon * LN2) * lse
    p1, p2, p3 = split3_kernel(ls * LOG2E - lse)
    xc_ref[...] = (xa + sel[1:2, :] + p1.astype(jnp.float32) * sel[2:3, :]
                   + p2.astype(jnp.float32) * sel[3:4, :]
                   + p3.astype(jnp.float32) * sel[4:5, :]).astype(jnp.bfloat16)

    def col_pass(ts):
        for slot, t in enumerate(ts):
            tb = pairs_ref[base + t]
            u = jnp.dot(xc_ref[...], tab_ref[tb], preferred_element_type=jnp.float32)
            sbuf[slot] = u
            cm = jnp.max(u, axis=0, keepdims=True)
            cs = jnp.sum(jnp.exp2(sbuf[slot] - cm), axis=0, keepdims=True)
            old = gtop_ref[tb]
            new = jnp.maximum(old, cm)
            gsum_ref[tb] = gsum_ref[tb] * jnp.exp2(old - new) + cs * jnp.exp2(cm - new)
            gtop_ref[tb] = new

    quads_of(col_pass)


def merge(tops, sums, axis):
    top = jnp.max(tops, axis=axis, keepdims=True)
    total = jnp.sum(sums * jnp.exp2(tops - top), axis=axis, keepdims=True)
    return top, total


def on_device(src_feat, tgt_feat, tgt_pot, log_src, log_tgt, pairs, counts):
    d = src_feat.shape[0]
    ns = src_feat.shape[1]
    nrb = ns // BLK
    npairs = pairs.shape[1]
    own_targets = tgt_feat.shape[1]
    ncols = lax.axis_size("cols")

    packed = jnp.concatenate([tgt_feat, tgt_pot[None, :], log_tgt[None, :]], axis=0)
    rowsp = packed.shape[0]
    nrows = lax.axis_size("rows")
    share = rowsp // nrows
    mine = lax.dynamic_slice_in_dim(packed, lax.axis_index("rows") * share, share, 0)
    halves = mine[None]
    col_index = lax.axis_index("cols")
    nbits = ncols.bit_length() - 1
    for bit in reversed(range(nbits)):
        step = 1 << bit
        partner = lax.ppermute(halves, "cols", [(i, i ^ step) for i in range(ncols)])
        low = (col_index & step) == 0
        halves = jnp.concatenate(
            [jnp.where(low, halves, partner), jnp.where(low, partner, halves)], axis=0)
    halves = jnp.transpose(
        halves.reshape((2,) * nbits + (share, own_targets)),
        tuple(reversed(range(nbits))) + (nbits, nbits + 1)).reshape(ncols, share, own_targets)
    other = lax.ppermute(halves, "rows", [(0, 1), (1, 0)])
    first = lax.axis_index("rows") == 0
    gathered = jnp.concatenate(
        [jnp.where(first, halves, other), jnp.where(first, other, halves)], axis=1)
    nt = ncols * own_targets
    tblocks = nt // BLK
    blocks = jnp.transpose(
        gathered.reshape(ncols, rowsp, own_targets // BLK, BLK), (0, 2, 1, 3)).reshape(tblocks, rowsp, BLK)

    col = jnp.arange(KP, dtype=jnp.int32)[None, :]
    comp = jnp.arange(d, dtype=jnp.int32)[:, None]
    def place(starts):
        hit = jnp.zeros((d, KP), bool)
        for s in starts:
            hit = hit | (col == comp + s)
        return hit.astype(jnp.bfloat16)
    expand = jnp.stack([place([0, d]), place([2 * d]), place([])])
    k0 = 3 * d
    sel = jnp.stack([
        ((col[0] >= k0) & (col[0] < k0 + 3)),
        ((col[0] >= k0 + 3) & (col[0] < k0 + 6)),
        col[0] == k0 + 6, col[0] == k0 + 7, col[0] == k0 + 8,
        col[0] < 0, col[0] < 0, col[0] < 0,
    ]).astype(jnp.float32)

    kept = (nrb // 2) * BLK
    kept_blocks = nrb // 2
    swap = [(0, 1), (1, 0)]
    feats = jnp.concatenate([src_feat, log_src[None, :]], axis=0)
    feats = jnp.concatenate([feats[:, :kept], lax.ppermute(feats[:, kept:], "rows", swap)], axis=1)
    lists = jnp.concatenate([pairs, counts[:, None]], axis=1)
    lists = jnp.concatenate([lists[:kept_blocks], lax.ppermute(lists[kept_blocks:], "rows", swap)], axis=0)
    src_feat = feats[:d]
    pairs = lists[:, :npairs]
    counts = lists[:, npairs]
    xt = jnp.transpose(feats)

    grid_spec = pltpu.PrefetchScalarGridSpec(
        num_scalar_prefetch=2,
        grid=(nrb,),
        in_specs=[
            pl.BlockSpec((BLK, d + 1), lambda b, pr, ct: (b, 0)),
            pl.BlockSpec((3, d, KP), lambda b, pr, ct: (0, 0, 0)),
            pl.BlockSpec((8, KP), lambda b, pr, ct: (0, 0)),
            pl.BlockSpec((tblocks, rowsp, BLK), lambda b, pr, ct: (0, 0, 0)),
        ],
        out_specs=[
            pl.BlockSpec((BLK, 1), lambda b, pr, ct: (b, 0)),
            pl.BlockSpec((tblocks, 1, BLK), lambda b, pr, ct: (0, 0, 0)),
            pl.BlockSpec((tblocks, 1, BLK), lambda b, pr, ct: (0, 0, 0)),
        ],
        scratch_shapes=[pltpu.VMEM((4, BLK, BLK), jnp.float32),
                        pltpu.VMEM((BLK, KP), jnp.bfloat16),
                        pltpu.VMEM((BLK, KP), jnp.bfloat16),
                        pltpu.VMEM((2, BLK, LANE), jnp.float32),
                        pltpu.VMEM((tblocks, KP, BLK), jnp.bfloat16)],
    )
    fpot, gtop, gsum = pl.pallas_call(
        functools.partial(sinkhorn_kernel, npairs, d),
        grid_spec=grid_spec,
        out_shape=[
            jax.ShapeDtypeStruct((ns, 1), jnp.float32),
            jax.ShapeDtypeStruct((tblocks, 1, BLK), jnp.float32),
            jax.ShapeDtypeStruct((tblocks, 1, BLK), jnp.float32),
        ],
        compiler_params=pltpu.CompilerParams(
            dimension_semantics=("arbitrary",), vmem_limit_bytes=100 * 1024 * 1024),
    )(pairs.reshape(-1), counts, xt, expand, sel, blocks)

    done = fpot.reshape(-1)
    src_pot = jnp.concatenate([done[:kept], lax.ppermute(done[kept:], "rows", swap)])
    parts = jnp.stack([gtop.reshape(ncols, own_targets), gsum.reshape(ncols, own_targets)], axis=1)
    mine = lax.all_to_all(parts, "cols", 0, 0, tiled=True)
    top, total = merge(mine[:, 0, :], mine[:, 1, :], 0)
    here = jnp.concatenate([top, total], axis=0)
    there = lax.ppermute(here, "rows", [(0, 1), (1, 0)])
    both = jnp.stack([jnp.where(first, here, there), jnp.where(first, there, here)])
    top, total = merge(both[:, 0, :], both[:, 1, :], 0)
    new_tgt_pot = (-epsilon * LN2) * (top[0] + jnp.log2(total[0]))
    return (src_pot, new_tgt_pot)


def solution(mesh):
    placed = (
        P(None, ("parts", "rows", "cols")),
        P(None, ("parts", "cols")),
        P(("parts", "cols")),
        P(("parts", "rows", "cols")),
        P(("parts", "cols")),
        P(("parts", "rows", "cols"), None),
        P(("parts", "rows", "cols")),
    )
    return jax.shard_map(
        on_device,
        mesh=mesh,
        in_specs=placed,
        out_specs=(P(("parts", "rows", "cols")), P(("parts", "cols"))),
        check_vma=False,
    )
```

```python
import functools

import jax
import jax.numpy as jnp
from jax import lax
from jax.experimental import pallas as pl
from jax.experimental.pallas import tpu as pltpu
from jax.sharding import PartitionSpec as P

BLK = 256
KP = 128
LANE = 128

epsilon = 0.1
NEG = -1e30
LOG2E = 1.4426950408889634
LN2 = 0.6931471805599453


def split3(v):
    first = lax.reduce_precision(v, exponent_bits=8, mantissa_bits=7)
    rest = v - first
    second = lax.reduce_precision(rest, exponent_bits=8, mantissa_bits=7)
    third = rest - second
    return (first.astype(jnp.bfloat16), second.astype(jnp.bfloat16),
            third.astype(jnp.bfloat16))


def split3_kernel(v):
    first = v.astype(jnp.bfloat16)
    rest = v - first.astype(jnp.float32)
    second = rest.astype(jnp.bfloat16)
    third = (rest - second.astype(jnp.float32)).astype(jnp.bfloat16)
    return first, second, third


def build_table(d, blocks_ref, tab_ref):
    scale = 2.0 * LOG2E / epsilon
    slot_row = lax.broadcasted_iota(jnp.int32, (16, BLK), 0)
    used = 3 * d + 16

    def one(tb, carry):
        blk = blocks_ref[tb]
        y = blk[0:d, :]
        yn = jnp.sum(y * y, axis=0, keepdims=True)
        tp = blk[d:d + 1, :]
        lt = blk[d + 1:d + 2, :]
        acol = (lt + (tp - yn) / epsilon) * LOG2E
        ccol = (-yn / epsilon) * LOG2E
        y1, y2, y3 = split3_kernel(y * scale)
        for k, piece in enumerate([y1, y2, y1]):
            tab_ref[tb, k * d:(k + 1) * d, :] = piece
        slot = jnp.zeros((16, BLK), jnp.float32)
        pieces = list(split3_kernel(acol)) + list(split3_kernel(ccol))
        for k, piece in enumerate(pieces):
            slot = jnp.where(slot_row == k, piece.astype(jnp.float32), slot)
        slot = jnp.where((slot_row >= 6) & (slot_row < 9), 1.0, slot)
        tab_ref[tb, 3 * d:used, :] = slot.astype(jnp.bfloat16)
        tab_ref[tb, used:KP, :] = jnp.zeros((KP - used, BLK), jnp.bfloat16)
        return carry

    lax.fori_loop(0, tab_ref.shape[0], one, 0)


def sinkhorn_kernel(npairs, d, pairs_ref, counts_ref, xt_ref, expand_ref, sel_ref,
                    blocks_ref, fpot_ref, gtop_ref, gsum_ref, sbuf, xr_ref, xc_ref, acc_ref, tab_ref):
    b = pl.program_id(0)

    @pl.when(b == 0)
    def _init():
        gtop_ref[...] = jnp.full(gtop_ref.shape, NEG, jnp.float32)
        gsum_ref[...] = jnp.zeros(gsum_ref.shape, jnp.float32)
        build_table(d, blocks_ref, tab_ref)

    cnt = counts_ref[b]
    base = b * npairs
    xfull = xt_ref[...]
    xs = xfull[:, :d]
    ls = xfull[:, d:d + 1]
    xn = jnp.sum(xs * xs, axis=1, keepdims=True)
    x1, x2, x3 = split3_kernel(xs)
    xa = (jnp.dot(x1, expand_ref[0], preferred_element_type=jnp.float32)
          + jnp.dot(x2, expand_ref[1], preferred_element_type=jnp.float32)
          + jnp.dot(x3, expand_ref[2], preferred_element_type=jnp.float32))
    sel = sel_ref[...]
    xr_ref[...] = (xa + sel[0:1, :]).astype(jnp.bfloat16)
    for a in range(2):
        acc_ref[2 * a] = jnp.full((BLK, LANE), NEG, jnp.float32)
        acc_ref[2 * a + 1] = jnp.zeros((BLK, LANE), jnp.float32)

    def pairs_of(body):
        def two(k, carry):
            body([2 * k, 2 * k + 1])
            return carry

        lax.fori_loop(0, cnt // 2, two, 0)

        @pl.when(cnt % 2 == 1)
        def _last():
            body([cnt - 1])

    def quads_of(body):
        def four(k, carry):
            body([4 * k + i for i in range(4)])
            return carry

        lax.fori_loop(0, cnt // 4, four, 0)
        done = cnt - cnt % 4

        @pl.when(cnt % 4 >= 2)
        def _pair():
            body([done, done + 1])

        @pl.when(cnt % 2 == 1)
        def _last():
            body([cnt - 1])

    def row_update(ts, a):
        halves = []
        for t in ts:
            s = jnp.dot(xr_ref[...], tab_ref[pairs_ref[base + t]], preferred_element_type=jnp.float32)
            halves += [s[:, :LANE], s[:, LANE:]]
        old = acc_ref[2 * a]
        new = old
        for h in halves:
            new = jnp.maximum(new, h)
        total = acc_ref[2 * a + 1] * jnp.exp2(old - new)
        for h in halves:
            total = total + jnp.exp2(h - new)
        acc_ref[2 * a] = new
        acc_ref[2 * a + 1] = total

    def row_pass(ts):
        row_update(ts[:2], 0)
        if len(ts) > 2:
            row_update(ts[2:], 1)

    quads_of(row_pass)
    top_a = acc_ref[0]
    top_b = acc_ref[2]
    lane_top = jnp.maximum(top_a, top_b)
    m = jnp.max(lane_top, axis=1, keepdims=True)
    lane_sum = (acc_ref[1] * jnp.exp2(top_a - m) + acc_ref[3] * jnp.exp2(top_b - m))
    lse = m + jnp.log2(jnp.sum(lane_sum, axis=1, keepdims=True))
    fpot_ref[...] = xn - (epsilon * LN2) * lse
    p1, p2, p3 = split3_kernel(ls * LOG2E - lse)
    xc_ref[...] = (xa + sel[1:2, :] + p1.astype(jnp.float32) * sel[2:3, :]
                   + p2.astype(jnp.float32) * sel[3:4, :]
                   + p3.astype(jnp.float32) * sel[4:5, :]).astype(jnp.bfloat16)

    def col_pass(ts):
        for slot, t in enumerate(ts):
            tb = pairs_ref[base + t]
            u = jnp.dot(xc_ref[...], tab_ref[tb], preferred_element_type=jnp.float32)
            sbuf[slot] = u
            cm = jnp.max(u, axis=0, keepdims=True)
            cs = jnp.sum(jnp.exp2(sbuf[slot] - cm), axis=0, keepdims=True)
            old = gtop_ref[tb]
            new = jnp.maximum(old, cm)
            gsum_ref[tb] = gsum_ref[tb] * jnp.exp2(old - new) + cs * jnp.exp2(cm - new)
            gtop_ref[tb] = new

    quads_of(col_pass)


def merge(tops, sums, axis):
    top = jnp.max(tops, axis=axis, keepdims=True)
    total = jnp.sum(sums * jnp.exp2(tops - top), axis=axis, keepdims=True)
    return top, total


def on_device(src_feat, tgt_feat, tgt_pot, log_src, log_tgt, pairs, counts):
    d = src_feat.shape[0]
    ns = src_feat.shape[1]
    nrb = ns // BLK
    npairs = pairs.shape[1]
    own_targets = tgt_feat.shape[1]
    ncols = lax.axis_size("cols")

    packed = jnp.concatenate([tgt_feat, tgt_pot[None, :], log_tgt[None, :]], axis=0)
    rowsp = packed.shape[0]
    nrows = lax.axis_size("rows")
    share = rowsp // nrows
    mine = lax.dynamic_slice_in_dim(packed, lax.axis_index("rows") * share, share, 0)
    halves = mine[None]
    col_index = lax.axis_index("cols")
    nbits = ncols.bit_length() - 1
    for bit in reversed(range(nbits)):
        step = 1 << bit
        partner = lax.ppermute(halves, "cols", [(i, i ^ step) for i in range(ncols)])
        low = (col_index & step) == 0
        halves = jnp.concatenate(
            [jnp.where(low, halves, partner), jnp.where(low, partner, halves)], axis=0)
    halves = jnp.transpose(
        halves.reshape((2,) * nbits + (share, own_targets)),
        tuple(reversed(range(nbits))) + (nbits, nbits + 1)).reshape(ncols, share, own_targets)
    other = lax.ppermute(halves, "rows", [(0, 1), (1, 0)])
    first = lax.axis_index("rows") == 0
    gathered = jnp.concatenate(
        [jnp.where(first, halves, other), jnp.where(first, other, halves)], axis=1)
    nt = ncols * own_targets
    tblocks = nt // BLK
    blocks = jnp.transpose(
        gathered.reshape(ncols, rowsp, own_targets // BLK, BLK), (0, 2, 1, 3)).reshape(tblocks, rowsp, BLK)

    col = jnp.arange(KP, dtype=jnp.int32)[None, :]
    comp = jnp.arange(d, dtype=jnp.int32)[:, None]
    def place(starts):
        hit = jnp.zeros((d, KP), bool)
        for s in starts:
            hit = hit | (col == comp + s)
        return hit.astype(jnp.bfloat16)
    expand = jnp.stack([place([0, d]), place([2 * d]), place([])])
    k0 = 3 * d
    sel = jnp.stack([
        ((col[0] >= k0) & (col[0] < k0 + 3)),
        ((col[0] >= k0 + 3) & (col[0] < k0 + 6)),
        col[0] == k0 + 6, col[0] == k0 + 7, col[0] == k0 + 8,
        col[0] < 0, col[0] < 0, col[0] < 0,
    ]).astype(jnp.float32)

    kept = (nrb // 2) * BLK
    kept_blocks = nrb // 2
    swap = [(0, 1), (1, 0)]
    feats = jnp.concatenate([src_feat, log_src[None, :]], axis=0)
    feats = jnp.concatenate([feats[:, :kept], lax.ppermute(feats[:, kept:], "rows", swap)], axis=1)
    lists = jnp.concatenate([pairs, counts[:, None]], axis=1)
    lists = jnp.concatenate([lists[:kept_blocks], lax.ppermute(lists[kept_blocks:], "rows", swap)], axis=0)
    src_feat = feats[:d]
    pairs = lists[:, :npairs]
    counts = lists[:, npairs]
    xt = jnp.transpose(feats)

    grid_spec = pltpu.PrefetchScalarGridSpec(
        num_scalar_prefetch=2,
        grid=(nrb,),
        in_specs=[
            pl.BlockSpec((BLK, d + 1), lambda b, pr, ct: (b, 0)),
            pl.BlockSpec((3, d, KP), lambda b, pr, ct: (0, 0, 0)),
            pl.BlockSpec((8, KP), lambda b, pr, ct: (0, 0)),
            pl.BlockSpec((tblocks, rowsp, BLK), lambda b, pr, ct: (0, 0, 0)),
        ],
        out_specs=[
            pl.BlockSpec((BLK, 1), lambda b, pr, ct: (b, 0)),
            pl.BlockSpec((tblocks, 1, BLK), lambda b, pr, ct: (0, 0, 0)),
            pl.BlockSpec((tblocks, 1, BLK), lambda b, pr, ct: (0, 0, 0)),
        ],
        scratch_shapes=[pltpu.VMEM((4, BLK, BLK), jnp.float32),
                        pltpu.VMEM((BLK, KP), jnp.bfloat16),
                        pltpu.VMEM((BLK, KP), jnp.bfloat16),
                        pltpu.VMEM((4, BLK, LANE), jnp.float32),
                        pltpu.VMEM((tblocks, KP, BLK), jnp.bfloat16)],
    )
    fpot, gtop, gsum = pl.pallas_call(
        functools.partial(sinkhorn_kernel, npairs, d),
        grid_spec=grid_spec,
        out_shape=[
            jax.ShapeDtypeStruct((ns, 1), jnp.float32),
            jax.ShapeDtypeStruct((tblocks, 1, BLK), jnp.float32),
            jax.ShapeDtypeStruct((tblocks, 1, BLK), jnp.float32),
        ],
        compiler_params=pltpu.CompilerParams(
            dimension_semantics=("arbitrary",), vmem_limit_bytes=100 * 1024 * 1024),
    )(pairs.reshape(-1), counts, xt, expand, sel, blocks)

    done = fpot.reshape(-1)
    src_pot = jnp.concatenate([done[:kept], lax.ppermute(done[kept:], "rows", swap)])
    parts = jnp.stack([gtop.reshape(ncols, own_targets), gsum.reshape(ncols, own_targets)], axis=1)
    mine = lax.all_to_all(parts, "cols", 0, 0, tiled=True)
    top, total = merge(mine[:, 0, :], mine[:, 1, :], 0)
    here = jnp.concatenate([top, total], axis=0)
    there = lax.ppermute(here, "rows", [(0, 1), (1, 0)])
    both = jnp.stack([jnp.where(first, here, there), jnp.where(first, there, here)])
    top, total = merge(both[:, 0, :], both[:, 1, :], 0)
    new_tgt_pot = (-epsilon * LN2) * (top[0] + jnp.log2(total[0]))
    return (src_pot, new_tgt_pot)


def solution(mesh):
    placed = (
        P(None, ("parts", "rows", "cols")),
        P(None, ("parts", "cols")),
        P(("parts", "cols")),
        P(("parts", "rows", "cols")),
        P(("parts", "cols")),
        P(("parts", "rows", "cols"), None),
        P(("parts", "rows", "cols")),
    )
    return jax.shard_map(
        on_device,
        mesh=mesh,
        in_specs=placed,
        out_specs=(P(("parts", "rows", "cols")), P(("parts", "cols"))),
        check_vma=False,
    )
```

```python
import functools

import jax
import jax.numpy as jnp
from jax import lax
from jax.experimental import pallas as pl
from jax.experimental.pallas import tpu as pltpu
from jax.sharding import PartitionSpec as P

BLK = 256
KP = 128
LANE = 128

epsilon = 0.1
NEG = -1e30
LOG2E = 1.4426950408889634
LN2 = 0.6931471805599453


def split3(v):
    first = lax.reduce_precision(v, exponent_bits=8, mantissa_bits=7)
    rest = v - first
    second = lax.reduce_precision(rest, exponent_bits=8, mantissa_bits=7)
    third = rest - second
    return (first.astype(jnp.bfloat16), second.astype(jnp.bfloat16),
            third.astype(jnp.bfloat16))


def split3_kernel(v):
    first = v.astype(jnp.bfloat16)
    rest = v - first.astype(jnp.float32)
    second = rest.astype(jnp.bfloat16)
    third = (rest - second.astype(jnp.float32)).astype(jnp.bfloat16)
    return first, second, third


def build_table(d, nbits, blocks_ref, tab_ref):
    scale = 2.0 * LOG2E / epsilon
    slot_row = lax.broadcasted_iota(jnp.int32, (16, BLK), 0)
    used = 3 * d + 16
    per_col = blocks_ref.shape[2] // BLK

    def one(pos, carry):
        src = 0
        for i in range(nbits):
            src = src + ((pos >> i) & 1) * (1 << (nbits - 1 - i))
        for q in range(per_col):
            blk = blocks_ref[pos, :, q * BLK:(q + 1) * BLK]
            tb = src * per_col + q
            y = blk[0:d, :]
            yn = jnp.sum(y * y, axis=0, keepdims=True)
            tp = blk[d:d + 1, :]
            lt = blk[d + 1:d + 2, :]
            acol = (lt + (tp - yn) / epsilon) * LOG2E
            ccol = (-yn / epsilon) * LOG2E
            y1, y2, y3 = split3_kernel(y * scale)
            for k, piece in enumerate([y1, y2, y1]):
                tab_ref[tb, k * d:(k + 1) * d, :] = piece
            slot = jnp.zeros((16, BLK), jnp.float32)
            pieces = list(split3_kernel(acol)) + list(split3_kernel(ccol))
            for k, piece in enumerate(pieces):
                slot = jnp.where(slot_row == k, piece.astype(jnp.float32), slot)
            slot = jnp.where((slot_row >= 6) & (slot_row < 9), 1.0, slot)
            tab_ref[tb, 3 * d:used, :] = slot.astype(jnp.bfloat16)
            tab_ref[tb, used:KP, :] = jnp.zeros((KP - used, BLK), jnp.bfloat16)
        return carry

    lax.fori_loop(0, blocks_ref.shape[0], one, 0)


def sinkhorn_kernel(npairs, d, nbits, pairs_ref, counts_ref, xt_ref, expand_ref, sel_ref,
                    blocks_ref, fpot_ref, gtop_ref, gsum_ref, sbuf, xr_ref, xc_ref, acc_ref, tab_ref):
    b = pl.program_id(0)

    @pl.when(b == 0)
    def _init():
        gtop_ref[...] = jnp.full(gtop_ref.shape, NEG, jnp.float32)
        gsum_ref[...] = jnp.zeros(gsum_ref.shape, jnp.float32)
        build_table(d, nbits, blocks_ref, tab_ref)

    cnt = counts_ref[b]
    base = b * npairs
    xfull = xt_ref[...]
    xs = xfull[:, :d]
    ls = xfull[:, d:d + 1]
    xn = jnp.sum(xs * xs, axis=1, keepdims=True)
    x1, x2, x3 = split3_kernel(xs)
    xa = (jnp.dot(x1, expand_ref[0], preferred_element_type=jnp.float32)
          + jnp.dot(x2, expand_ref[1], preferred_element_type=jnp.float32)
          + jnp.dot(x3, expand_ref[2], preferred_element_type=jnp.float32))
    sel = sel_ref[...]
    xr_ref[...] = (xa + sel[0:1, :]).astype(jnp.bfloat16)
    for a in range(2):
        acc_ref[2 * a] = jnp.full((BLK, LANE), NEG, jnp.float32)
        acc_ref[2 * a + 1] = jnp.zeros((BLK, LANE), jnp.float32)

    def pairs_of(body):
        def two(k, carry):
            body([2 * k, 2 * k + 1])
            return carry

        lax.fori_loop(0, cnt // 2, two, 0)

        @pl.when(cnt % 2 == 1)
        def _last():
            body([cnt - 1])

    def quads_of(body):
        def four(k, carry):
            body([4 * k + i for i in range(4)])
            return carry

        lax.fori_loop(0, cnt // 4, four, 0)
        done = cnt - cnt % 4

        @pl.when(cnt % 4 >= 2)
        def _pair():
            body([done, done + 1])

        @pl.when(cnt % 2 == 1)
        def _last():
            body([cnt - 1])

    def row_update(ts, a):
        halves = []
        for t in ts:
            s = jnp.dot(xr_ref[...], tab_ref[pairs_ref[base + t]], preferred_element_type=jnp.float32)
            halves += [s[:, :LANE], s[:, LANE:]]
        old = acc_ref[2 * a]
        new = old
        for h in halves:
            new = jnp.maximum(new, h)
        total = acc_ref[2 * a + 1] * jnp.exp2(old - new)
        for h in halves:
            total = total + jnp.exp2(h - new)
        acc_ref[2 * a] = new
        acc_ref[2 * a + 1] = total

    def row_pass(ts):
        row_update(ts[:2], 0)
        if len(ts) > 2:
            row_update(ts[2:], 1)

    quads_of(row_pass)
    top_a = acc_ref[0]
    top_b = acc_ref[2]
    lane_top = jnp.maximum(top_a, top_b)
    m = jnp.max(lane_top, axis=1, keepdims=True)
    lane_sum = (acc_ref[1] * jnp.exp2(top_a - m) + acc_ref[3] * jnp.exp2(top_b - m))
    lse = m + jnp.log2(jnp.sum(lane_sum, axis=1, keepdims=True))
    fpot_ref[...] = xn - (epsilon * LN2) * lse
    p1, p2, p3 = split3_kernel(ls * LOG2E - lse)
    xc_ref[...] = (xa + sel[1:2, :] + p1.astype(jnp.float32) * sel[2:3, :]
                   + p2.astype(jnp.float32) * sel[3:4, :]
                   + p3.astype(jnp.float32) * sel[4:5, :]).astype(jnp.bfloat16)

    def col_pass(ts):
        for slot, t in enumerate(ts):
            tb = pairs_ref[base + t]
            u = jnp.dot(xc_ref[...], tab_ref[tb], preferred_element_type=jnp.float32)
            sbuf[slot] = u
            cm = jnp.max(u, axis=0, keepdims=True)
            cs = jnp.sum(jnp.exp2(sbuf[slot] - cm), axis=0, keepdims=True)
            old = gtop_ref[tb]
            new = jnp.maximum(old, cm)
            gsum_ref[tb] = gsum_ref[tb] * jnp.exp2(old - new) + cs * jnp.exp2(cm - new)
            gtop_ref[tb] = new

    quads_of(col_pass)


def merge(tops, sums, axis):
    top = jnp.max(tops, axis=axis, keepdims=True)
    total = jnp.sum(sums * jnp.exp2(tops - top), axis=axis, keepdims=True)
    return top, total


def on_device(src_feat, tgt_feat, tgt_pot, log_src, log_tgt, pairs, counts):
    d = src_feat.shape[0]
    ns = src_feat.shape[1]
    nrb = ns // BLK
    npairs = pairs.shape[1]
    own_targets = tgt_feat.shape[1]
    ncols = lax.axis_size("cols")

    packed = jnp.concatenate([tgt_feat, tgt_pot[None, :], log_tgt[None, :]], axis=0)
    rowsp = packed.shape[0]
    nrows = lax.axis_size("rows")
    share = rowsp // nrows
    mine = lax.dynamic_slice_in_dim(packed, lax.axis_index("rows") * share, share, 0)
    halves = mine[None]
    col_index = lax.axis_index("cols")
    nbits = ncols.bit_length() - 1
    for bit in reversed(range(nbits)):
        step = 1 << bit
        partner = lax.ppermute(halves, "cols", [(i, i ^ step) for i in range(ncols)])
        low = (col_index & step) == 0
        halves = jnp.concatenate(
            [jnp.where(low, halves, partner), jnp.where(low, partner, halves)], axis=0)
    other = lax.ppermute(halves, "rows", [(0, 1), (1, 0)])
    first = lax.axis_index("rows") == 0
    gathered = jnp.concatenate(
        [jnp.where(first, halves, other), jnp.where(first, other, halves)], axis=1)
    nt = ncols * own_targets
    tblocks = nt // BLK

    col = jnp.arange(KP, dtype=jnp.int32)[None, :]
    comp = jnp.arange(d, dtype=jnp.int32)[:, None]
    def place(starts):
        hit = jnp.zeros((d, KP), bool)
        for s in starts:
            hit = hit | (col == comp + s)
        return hit.astype(jnp.bfloat16)
    expand = jnp.stack([place([0, d]), place([2 * d]), place([])])
    k0 = 3 * d
    sel = jnp.stack([
        ((col[0] >= k0) & (col[0] < k0 + 3)),
        ((col[0] >= k0 + 3) & (col[0] < k0 + 6)),
        col[0] == k0 + 6, col[0] == k0 + 7, col[0] == k0 + 8,
        col[0] < 0, col[0] < 0, col[0] < 0,
    ]).astype(jnp.float32)

    kept = (nrb // 2) * BLK
    kept_blocks = nrb // 2
    swap = [(0, 1), (1, 0)]
    feats = jnp.concatenate([src_feat, log_src[None, :]], axis=0)
    feats = jnp.concatenate([feats[:, :kept], lax.ppermute(feats[:, kept:], "rows", swap)], axis=1)
    lists = jnp.concatenate([pairs, counts[:, None]], axis=1)
    lists = jnp.concatenate([lists[:kept_blocks], lax.ppermute(lists[kept_blocks:], "rows", swap)], axis=0)
    src_feat = feats[:d]
    pairs = lists[:, :npairs]
    counts = lists[:, npairs]
    xt = jnp.transpose(feats)

    grid_spec = pltpu.PrefetchScalarGridSpec(
        num_scalar_prefetch=2,
        grid=(nrb,),
        in_specs=[
            pl.BlockSpec((BLK, d + 1), lambda b, pr, ct: (b, 0)),
            pl.BlockSpec((3, d, KP), lambda b, pr, ct: (0, 0, 0)),
            pl.BlockSpec((8, KP), lambda b, pr, ct: (0, 0)),
            pl.BlockSpec((ncols, rowsp, own_targets), lambda b, pr, ct: (0, 0, 0)),
        ],
        out_specs=[
            pl.BlockSpec((BLK, 1), lambda b, pr, ct: (b, 0)),
            pl.BlockSpec((tblocks, 1, BLK), lambda b, pr, ct: (0, 0, 0)),
            pl.BlockSpec((tblocks, 1, BLK), lambda b, pr, ct: (0, 0, 0)),
        ],
        scratch_shapes=[pltpu.VMEM((4, BLK, BLK), jnp.float32),
                        pltpu.VMEM((BLK, KP), jnp.bfloat16),
                        pltpu.VMEM((BLK, KP), jnp.bfloat16),
                        pltpu.VMEM((4, BLK, LANE), jnp.float32),
                        pltpu.VMEM((tblocks, KP, BLK), jnp.bfloat16)],
    )
    fpot, gtop, gsum = pl.pallas_call(
        functools.partial(sinkhorn_kernel, npairs, d, nbits),
        grid_spec=grid_spec,
        out_shape=[
            jax.ShapeDtypeStruct((ns, 1), jnp.float32),
            jax.ShapeDtypeStruct((tblocks, 1, BLK), jnp.float32),
            jax.ShapeDtypeStruct((tblocks, 1, BLK), jnp.float32),
        ],
        compiler_params=pltpu.CompilerParams(
            dimension_semantics=("arbitrary",), vmem_limit_bytes=100 * 1024 * 1024),
    )(pairs.reshape(-1), counts, xt, expand, sel, gathered)

    done = fpot.reshape(-1)
    src_pot = jnp.concatenate([done[:kept], lax.ppermute(done[kept:], "rows", swap)])
    parts = jnp.stack([gtop.reshape(ncols, own_targets), gsum.reshape(ncols, own_targets)], axis=1)
    mine = lax.all_to_all(parts, "cols", 0, 0, tiled=True)
    top, total = merge(mine[:, 0, :], mine[:, 1, :], 0)
    here = jnp.concatenate([top, total], axis=0)
    there = lax.ppermute(here, "rows", [(0, 1), (1, 0)])
    both = jnp.stack([jnp.where(first, here, there), jnp.where(first, there, here)])
    top, total = merge(both[:, 0, :], both[:, 1, :], 0)
    new_tgt_pot = (-epsilon * LN2) * (top[0] + jnp.log2(total[0]))
    return (src_pot, new_tgt_pot)


def solution(mesh):
    placed = (
        P(None, ("parts", "rows", "cols")),
        P(None, ("parts", "cols")),
        P(("parts", "cols")),
        P(("parts", "rows", "cols")),
        P(("parts", "cols")),
        P(("parts", "rows", "cols"), None),
        P(("parts", "rows", "cols")),
    )
    return jax.shard_map(
        on_device,
        mesh=mesh,
        in_specs=placed,
        out_specs=(P(("parts", "rows", "cols")), P(("parts", "cols"))),
        check_vma=False,
    )
```

```python
import functools

import jax
import jax.numpy as jnp
from jax import lax
from jax.experimental import pallas as pl
from jax.experimental.pallas import tpu as pltpu
from jax.sharding import PartitionSpec as P

BLK = 256
KP = 128
LANE = 128

epsilon = 0.1
NEG = -1e30
LOG2E = 1.4426950408889634
LN2 = 0.6931471805599453


def split3(v):
    first = lax.reduce_precision(v, exponent_bits=8, mantissa_bits=7)
    rest = v - first
    second = lax.reduce_precision(rest, exponent_bits=8, mantissa_bits=7)
    third = rest - second
    return (first.astype(jnp.bfloat16), second.astype(jnp.bfloat16),
            third.astype(jnp.bfloat16))


def split3_kernel(v):
    first = v.astype(jnp.bfloat16)
    rest = v - first.astype(jnp.float32)
    second = rest.astype(jnp.bfloat16)
    third = (rest - second.astype(jnp.float32)).astype(jnp.bfloat16)
    return first, second, third


def build_table(d, nbits, blocks_ref, tab_ref):
    scale = 2.0 * LOG2E / epsilon
    slot_row = lax.broadcasted_iota(jnp.int32, (16, BLK), 0)
    used = 3 * d + 16
    per_col = blocks_ref.shape[2] // BLK

    def one(pos, carry):
        src = 0
        for i in range(nbits):
            src = src + ((pos >> i) & 1) * (1 << (nbits - 1 - i))
        for q in range(per_col):
            blk = blocks_ref[pos, :, q * BLK:(q + 1) * BLK]
            tb = src * per_col + q
            y = blk[0:d, :]
            yn = jnp.sum(y * y, axis=0, keepdims=True)
            tp = blk[d:d + 1, :]
            lt = blk[d + 1:d + 2, :]
            acol = (lt + (tp - yn) / epsilon) * LOG2E
            ccol = (-yn / epsilon) * LOG2E
            y1, y2, y3 = split3_kernel(y * scale)
            for k, piece in enumerate([y1, y2, y1]):
                tab_ref[tb, k * d:(k + 1) * d, :] = piece
            slot = jnp.zeros((16, BLK), jnp.float32)
            pieces = list(split3_kernel(acol)) + list(split3_kernel(ccol))
            for k, piece in enumerate(pieces):
                slot = jnp.where(slot_row == k, piece.astype(jnp.float32), slot)
            slot = jnp.where((slot_row >= 6) & (slot_row < 9), 1.0, slot)
            tab_ref[tb, 3 * d:used, :] = slot.astype(jnp.bfloat16)
            tab_ref[tb, used:KP, :] = jnp.zeros((KP - used, BLK), jnp.bfloat16)
        return carry

    lax.fori_loop(0, blocks_ref.shape[0], one, 0)


def sinkhorn_kernel(npairs, d, nbits, pairs_ref, counts_ref, xt_ref, expand_ref, sel_ref,
                    blocks_ref, fpot_ref, gtop_ref, gsum_ref, sbuf, xr_ref, xc_ref, acc_ref, tab_ref):
    b = pl.program_id(0)

    @pl.when(b == 0)
    def _init():
        gtop_ref[...] = jnp.full(gtop_ref.shape, NEG, jnp.float32)
        gsum_ref[...] = jnp.zeros(gsum_ref.shape, jnp.float32)
        build_table(d, nbits, blocks_ref, tab_ref)

    cnt = counts_ref[b]
    base = b * npairs
    xfull = xt_ref[...]
    xs = xfull[:, :d]
    ls = xfull[:, d:d + 1]
    xn = jnp.sum(xs * xs, axis=1, keepdims=True)
    x1, x2, x3 = split3_kernel(xs)
    xa = (jnp.dot(x1, expand_ref[0], preferred_element_type=jnp.float32)
          + jnp.dot(x2, expand_ref[1], preferred_element_type=jnp.float32)
          + jnp.dot(x3, expand_ref[2], preferred_element_type=jnp.float32))
    sel = sel_ref[...]
    xr_ref[...] = (xa + sel[0:1, :]).astype(jnp.bfloat16)
    for a in range(2):
        acc_ref[2 * a] = jnp.full((BLK, LANE), NEG, jnp.float32)
        acc_ref[2 * a + 1] = jnp.zeros((BLK, LANE), jnp.float32)

    def pairs_of(body):
        def two(k, carry):
            body([2 * k, 2 * k + 1])
            return carry

        lax.fori_loop(0, cnt // 2, two, 0)

        @pl.when(cnt % 2 == 1)
        def _last():
            body([cnt - 1])

    def quads_of(body):
        def four(k, carry):
            body([4 * k + i for i in range(4)])
            return carry

        lax.fori_loop(0, cnt // 4, four, 0)
        done = cnt - cnt % 4

        @pl.when(cnt % 4 >= 2)
        def _pair():
            body([done, done + 1])

        @pl.when(cnt % 2 == 1)
        def _last():
            body([cnt - 1])

    def row_update(ts, a):
        halves = []
        for t in ts:
            s = jnp.dot(xr_ref[...], tab_ref[pairs_ref[base + t]], preferred_element_type=jnp.float32)
            halves += [s[:, :LANE], s[:, LANE:]]
        old = acc_ref[2 * a]
        new = old
        for h in halves:
            new = jnp.maximum(new, h)
        total = acc_ref[2 * a + 1] * jnp.exp2(old - new)
        for h in halves:
            total = total + jnp.exp2(h - new)
        acc_ref[2 * a] = new
        acc_ref[2 * a + 1] = total

    def row_pass(ts):
        row_update(ts[:2], 0)
        if len(ts) > 2:
            row_update(ts[2:], 1)

    quads_of(row_pass)
    top_a = acc_ref[0]
    top_b = acc_ref[2]
    lane_top = jnp.maximum(top_a, top_b)
    m = jnp.max(lane_top, axis=1, keepdims=True)
    lane_sum = (acc_ref[1] * jnp.exp2(top_a - m) + acc_ref[3] * jnp.exp2(top_b - m))
    lse = m + jnp.log2(jnp.sum(lane_sum, axis=1, keepdims=True))
    fpot_ref[...] = xn - (epsilon * LN2) * lse
    p1, p2, p3 = split3_kernel(ls * LOG2E - lse)
    xc_ref[...] = (xa + sel[1:2, :] + p1.astype(jnp.float32) * sel[2:3, :]
                   + p2.astype(jnp.float32) * sel[3:4, :]
                   + p3.astype(jnp.float32) * sel[4:5, :]).astype(jnp.bfloat16)

    def col_pass(ts):
        for slot, t in enumerate(ts):
            tb = pairs_ref[base + t]
            u = jnp.dot(xc_ref[...], tab_ref[tb], preferred_element_type=jnp.float32)
            sbuf[slot] = u
            cm = jnp.max(u, axis=0, keepdims=True)
            cs = jnp.sum(jnp.exp2(sbuf[slot] - cm), axis=0, keepdims=True)
            old = gtop_ref[tb]
            new = jnp.maximum(old, cm)
            gsum_ref[tb] = gsum_ref[tb] * jnp.exp2(old - new) + cs * jnp.exp2(cm - new)
            gtop_ref[tb] = new

    quads_of(col_pass)


def merge(tops, sums, axis):
    top = jnp.max(tops, axis=axis, keepdims=True)
    total = jnp.sum(sums * jnp.exp2(tops - top), axis=axis, keepdims=True)
    return top, total


def on_device(src_feat, tgt_feat, tgt_pot, log_src, log_tgt, pairs, counts):
    d = src_feat.shape[0]
    ns = src_feat.shape[1]
    nrb = ns // BLK
    npairs = pairs.shape[1]
    own_targets = tgt_feat.shape[1]
    ncols = lax.axis_size("cols")

    packed = jnp.concatenate([tgt_feat, tgt_pot[None, :], log_tgt[None, :]], axis=0)
    rowsp = packed.shape[0]
    nrows = lax.axis_size("rows")
    share = rowsp // nrows
    mine = lax.dynamic_slice_in_dim(packed, lax.axis_index("rows") * share, share, 0)
    halves = mine[None]
    col_index = lax.axis_index("cols")
    nbits = ncols.bit_length() - 1
    for bit in reversed(range(nbits)):
        step = 1 << bit
        partner = lax.ppermute(halves, "cols", [(i, i ^ step) for i in range(ncols)])
        low = (col_index & step) == 0
        halves = jnp.concatenate(
            [jnp.where(low, halves, partner), jnp.where(low, partner, halves)], axis=0)
    other = lax.ppermute(halves, "rows", [(0, 1), (1, 0)])
    first = lax.axis_index("rows") == 0
    gathered = jnp.concatenate(
        [jnp.where(first, halves, other), jnp.where(first, other, halves)], axis=1)
    nt = ncols * own_targets
    tblocks = nt // BLK

    col = jnp.arange(KP, dtype=jnp.int32)[None, :]
    comp = jnp.arange(d, dtype=jnp.int32)[:, None]
    def place(starts):
        hit = jnp.zeros((d, KP), bool)
        for s in starts:
            hit = hit | (col == comp + s)
        return hit.astype(jnp.bfloat16)
    expand = jnp.stack([place([0, d]), place([2 * d]), place([])])
    k0 = 3 * d
    sel = jnp.stack([
        ((col[0] >= k0) & (col[0] < k0 + 3)),
        ((col[0] >= k0 + 3) & (col[0] < k0 + 6)),
        col[0] == k0 + 6, col[0] == k0 + 7, col[0] == k0 + 8,
        col[0] < 0, col[0] < 0, col[0] < 0,
    ]).astype(jnp.float32)

    kept = (nrb // 2) * BLK
    kept_blocks = nrb // 2
    swap = [(0, 1), (1, 0)]
    feats = jnp.transpose(jnp.concatenate([src_feat, log_src[None, :]], axis=0))
    xt = jnp.concatenate([feats[:kept], lax.ppermute(feats[kept:], "rows", swap)], axis=0)
    lists = jnp.concatenate([pairs, counts[:, None]], axis=1)
    lists = jnp.concatenate([lists[:kept_blocks], lax.ppermute(lists[kept_blocks:], "rows", swap)], axis=0)
    pairs = lists[:, :npairs]
    counts = lists[:, npairs]

    grid_spec = pltpu.PrefetchScalarGridSpec(
        num_scalar_prefetch=2,
        grid=(nrb,),
        in_specs=[
            pl.BlockSpec((BLK, d + 1), lambda b, pr, ct: (b, 0)),
            pl.BlockSpec((3, d, KP), lambda b, pr, ct: (0, 0, 0)),
            pl.BlockSpec((8, KP), lambda b, pr, ct: (0, 0)),
            pl.BlockSpec((ncols, rowsp, own_targets), lambda b, pr, ct: (0, 0, 0)),
        ],
        out_specs=[
            pl.BlockSpec((BLK, 1), lambda b, pr, ct: (b, 0)),
            pl.BlockSpec((tblocks, 1, BLK), lambda b, pr, ct: (0, 0, 0)),
            pl.BlockSpec((tblocks, 1, BLK), lambda b, pr, ct: (0, 0, 0)),
        ],
        scratch_shapes=[pltpu.VMEM((4, BLK, BLK), jnp.float32),
                        pltpu.VMEM((BLK, KP), jnp.bfloat16),
                        pltpu.VMEM((BLK, KP), jnp.bfloat16),
                        pltpu.VMEM((4, BLK, LANE), jnp.float32),
                        pltpu.VMEM((tblocks, KP, BLK), jnp.bfloat16)],
    )
    fpot, gtop, gsum = pl.pallas_call(
        functools.partial(sinkhorn_kernel, npairs, d, nbits),
        grid_spec=grid_spec,
        out_shape=[
            jax.ShapeDtypeStruct((ns, 1), jnp.float32),
            jax.ShapeDtypeStruct((tblocks, 1, BLK), jnp.float32),
            jax.ShapeDtypeStruct((tblocks, 1, BLK), jnp.float32),
        ],
        compiler_params=pltpu.CompilerParams(
            dimension_semantics=("arbitrary",), vmem_limit_bytes=100 * 1024 * 1024),
    )(pairs.reshape(-1), counts, xt, expand, sel, gathered)

    done = fpot.reshape(-1)
    src_pot = jnp.concatenate([done[:kept], lax.ppermute(done[kept:], "rows", swap)])
    parts = jnp.stack([gtop.reshape(ncols, own_targets), gsum.reshape(ncols, own_targets)], axis=1)
    mine = lax.all_to_all(parts, "cols", 0, 0, tiled=True)
    top, total = merge(mine[:, 0, :], mine[:, 1, :], 0)
    here = jnp.concatenate([top, total], axis=0)
    there = lax.ppermute(here, "rows", [(0, 1), (1, 0)])
    both = jnp.stack([jnp.where(first, here, there), jnp.where(first, there, here)])
    top, total = merge(both[:, 0, :], both[:, 1, :], 0)
    new_tgt_pot = (-epsilon * LN2) * (top[0] + jnp.log2(total[0]))
    return (src_pot, new_tgt_pot)


def solution(mesh):
    placed = (
        P(None, ("parts", "rows", "cols")),
        P(None, ("parts", "cols")),
        P(("parts", "cols")),
        P(("parts", "rows", "cols")),
        P(("parts", "cols")),
        P(("parts", "rows", "cols"), None),
        P(("parts", "rows", "cols")),
    )
    return jax.shard_map(
        on_device,
        mesh=mesh,
        in_specs=placed,
        out_specs=(P(("parts", "rows", "cols")), P(("parts", "cols"))),
        check_vma=False,
    )
```

```python
import functools

import jax
import jax.numpy as jnp
from jax import lax
from jax.experimental import pallas as pl
from jax.experimental.pallas import tpu as pltpu
from jax.sharding import PartitionSpec as P

BLK = 256
KP = 128
LANE = 128

epsilon = 0.1
NEG = -1e30
LOG2E = 1.4426950408889634
LN2 = 0.6931471805599453


def split3(v):
    first = lax.reduce_precision(v, exponent_bits=8, mantissa_bits=7)
    rest = v - first
    second = lax.reduce_precision(rest, exponent_bits=8, mantissa_bits=7)
    third = rest - second
    return (first.astype(jnp.bfloat16), second.astype(jnp.bfloat16),
            third.astype(jnp.bfloat16))


def split3_kernel(v):
    first = v.astype(jnp.bfloat16)
    rest = v - first.astype(jnp.float32)
    second = rest.astype(jnp.bfloat16)
    third = (rest - second.astype(jnp.float32)).astype(jnp.bfloat16)
    return first, second, third


def build_table(d, nbits, blocks_ref, tab_ref):
    scale = 2.0 * LOG2E / epsilon
    slot_row = lax.broadcasted_iota(jnp.int32, (16, BLK), 0)
    used = 3 * d + 16
    per_col = blocks_ref.shape[2] // BLK

    def one(pos, carry):
        src = 0
        for i in range(nbits):
            src = src + ((pos >> i) & 1) * (1 << (nbits - 1 - i))
        for q in range(per_col):
            blk = blocks_ref[pos, :, q * BLK:(q + 1) * BLK]
            tb = src * per_col + q
            y = blk[0:d, :]
            yn = jnp.sum(y * y, axis=0, keepdims=True)
            tp = blk[d:d + 1, :]
            lt = blk[d + 1:d + 2, :]
            acol = (lt + (tp - yn) / epsilon) * LOG2E
            ccol = (-yn / epsilon) * LOG2E
            y1, y2, y3 = split3_kernel(y * scale)
            for k, piece in enumerate([y1, y2, y1]):
                tab_ref[tb, k * d:(k + 1) * d, :] = piece
            slot = jnp.zeros((16, BLK), jnp.float32)
            pieces = list(split3_kernel(acol)) + list(split3_kernel(ccol))
            for k, piece in enumerate(pieces):
                slot = jnp.where(slot_row == k, piece.astype(jnp.float32), slot)
            slot = jnp.where((slot_row >= 6) & (slot_row < 9), 1.0, slot)
            tab_ref[tb, 3 * d:used, :] = slot.astype(jnp.bfloat16)
            tab_ref[tb, used:KP, :] = jnp.zeros((KP - used, BLK), jnp.bfloat16)
        return carry

    lax.fori_loop(0, blocks_ref.shape[0], one, 0)


def sinkhorn_kernel(npairs, d, nbits, pairs_ref, counts_ref, xt_ref, expand_ref, sel_ref,
                    blocks_ref, fpot_ref, gtop_ref, gsum_ref, sbuf, xr_ref, xc_ref, acc_ref, tab_ref):
    b = pl.program_id(0)

    @pl.when(b == 0)
    def _init():
        gtop_ref[...] = jnp.full(gtop_ref.shape, NEG, jnp.float32)
        gsum_ref[...] = jnp.zeros(gsum_ref.shape, jnp.float32)
        build_table(d, nbits, blocks_ref, tab_ref)

    cnt = counts_ref[b]
    base = b * npairs
    xfull = xt_ref[...]
    xs = xfull[:, :d]
    ls = xfull[:, d:d + 1]
    xn = jnp.sum(xs * xs, axis=1, keepdims=True)
    x1, x2, x3 = split3_kernel(xs)
    xa = (jnp.dot(x1, expand_ref[0], preferred_element_type=jnp.float32)
          + jnp.dot(x2, expand_ref[1], preferred_element_type=jnp.float32)
          + jnp.dot(x3, expand_ref[2], preferred_element_type=jnp.float32))
    sel = sel_ref[...]
    xr_ref[...] = (xa + sel[0:1, :]).astype(jnp.bfloat16)
    for a in range(2):
        acc_ref[2 * a] = jnp.full((BLK, LANE), NEG, jnp.float32)
        acc_ref[2 * a + 1] = jnp.zeros((BLK, LANE), jnp.float32)

    def pairs_of(body):
        def two(k, carry):
            body([2 * k, 2 * k + 1])
            return carry

        lax.fori_loop(0, cnt // 2, two, 0)

        @pl.when(cnt % 2 == 1)
        def _last():
            body([cnt - 1])

    def quads_of(body):
        def four(k, carry):
            body([4 * k + i for i in range(4)])
            return carry

        lax.fori_loop(0, cnt // 4, four, 0)
        done = cnt - cnt % 4

        @pl.when(cnt % 4 >= 2)
        def _pair():
            body([done, done + 1])

        @pl.when(cnt % 2 == 1)
        def _last():
            body([cnt - 1])

    def row_update(ts, a):
        halves = []
        for t in ts:
            s = jnp.dot(xr_ref[...], tab_ref[pairs_ref[base + t]], preferred_element_type=jnp.float32)
            halves += [s[:, :LANE], s[:, LANE:]]
        old = acc_ref[2 * a]
        new = old
        for h in halves:
            new = jnp.maximum(new, h)
        total = acc_ref[2 * a + 1] * jnp.exp2(old - new)
        for h in halves:
            total = total + jnp.exp2(h - new)
        acc_ref[2 * a] = new
        acc_ref[2 * a + 1] = total

    def row_pass(ts):
        row_update(ts[:2], 0)
        if len(ts) > 2:
            row_update(ts[2:], 1)

    quads_of(row_pass)
    top_a = acc_ref[0]
    top_b = acc_ref[2]
    lane_top = jnp.maximum(top_a, top_b)
    m = jnp.max(lane_top, axis=1, keepdims=True)
    lane_sum = (acc_ref[1] * jnp.exp2(top_a - m) + acc_ref[3] * jnp.exp2(top_b - m))
    lse = m + jnp.log2(jnp.sum(lane_sum, axis=1, keepdims=True))
    fpot_ref[...] = xn - (epsilon * LN2) * lse
    p1, p2, p3 = split3_kernel(ls * LOG2E - lse)
    xc_ref[...] = (xa + sel[1:2, :] + p1.astype(jnp.float32) * sel[2:3, :]
                   + p2.astype(jnp.float32) * sel[3:4, :]
                   + p3.astype(jnp.float32) * sel[4:5, :]).astype(jnp.bfloat16)

    def col_pass(ts):
        for slot, t in enumerate(ts):
            tb = pairs_ref[base + t]
            u = jnp.dot(xc_ref[...], tab_ref[tb], preferred_element_type=jnp.float32)
            sbuf[slot] = u
            cm = jnp.max(u, axis=0, keepdims=True)
            cs = jnp.sum(jnp.exp2(sbuf[slot] - cm), axis=0, keepdims=True)
            old = gtop_ref[tb]
            new = jnp.maximum(old, cm)
            gsum_ref[tb] = gsum_ref[tb] * jnp.exp2(old - new) + cs * jnp.exp2(cm - new)
            gtop_ref[tb] = new

    def octets_of(body):
        def eight(k, carry):
            body([8 * k + i for i in range(8)])
            return carry

        lax.fori_loop(0, cnt // 8, eight, 0)
        rest = cnt % 8
        start4 = cnt - rest

        @pl.when(rest >= 4)
        def _four():
            body([start4 + i for i in range(4)])

        start2 = start4 + (rest // 4) * 4

        @pl.when(rest % 4 >= 2)
        def _pair():
            body([start2, start2 + 1])

        @pl.when(cnt % 2 == 1)
        def _last():
            body([cnt - 1])

    octets_of(col_pass)


def merge(tops, sums, axis):
    top = jnp.max(tops, axis=axis, keepdims=True)
    total = jnp.sum(sums * jnp.exp2(tops - top), axis=axis, keepdims=True)
    return top, total


def on_device(src_feat, tgt_feat, tgt_pot, log_src, log_tgt, pairs, counts):
    d = src_feat.shape[0]
    ns = src_feat.shape[1]
    nrb = ns // BLK
    npairs = pairs.shape[1]
    own_targets = tgt_feat.shape[1]
    ncols = lax.axis_size("cols")

    packed = jnp.concatenate([tgt_feat, tgt_pot[None, :], log_tgt[None, :]], axis=0)
    rowsp = packed.shape[0]
    nrows = lax.axis_size("rows")
    share = rowsp // nrows
    mine = lax.dynamic_slice_in_dim(packed, lax.axis_index("rows") * share, share, 0)
    halves = mine[None]
    col_index = lax.axis_index("cols")
    nbits = ncols.bit_length() - 1
    for bit in reversed(range(nbits)):
        step = 1 << bit
        partner = lax.ppermute(halves, "cols", [(i, i ^ step) for i in range(ncols)])
        low = (col_index & step) == 0
        halves = jnp.concatenate(
            [jnp.where(low, halves, partner), jnp.where(low, partner, halves)], axis=0)
    other = lax.ppermute(halves, "rows", [(0, 1), (1, 0)])
    first = lax.axis_index("rows") == 0
    gathered = jnp.concatenate(
        [jnp.where(first, halves, other), jnp.where(first, other, halves)], axis=1)
    nt = ncols * own_targets
    tblocks = nt // BLK

    col = jnp.arange(KP, dtype=jnp.int32)[None, :]
    comp = jnp.arange(d, dtype=jnp.int32)[:, None]
    def place(starts):
        hit = jnp.zeros((d, KP), bool)
        for s in starts:
            hit = hit | (col == comp + s)
        return hit.astype(jnp.bfloat16)
    expand = jnp.stack([place([0, d]), place([2 * d]), place([])])
    k0 = 3 * d
    sel = jnp.stack([
        ((col[0] >= k0) & (col[0] < k0 + 3)),
        ((col[0] >= k0 + 3) & (col[0] < k0 + 6)),
        col[0] == k0 + 6, col[0] == k0 + 7, col[0] == k0 + 8,
        col[0] < 0, col[0] < 0, col[0] < 0,
    ]).astype(jnp.float32)

    kept = (nrb // 2) * BLK
    kept_blocks = nrb // 2
    swap = [(0, 1), (1, 0)]
    feats = jnp.concatenate([src_feat, log_src[None, :]], axis=0)
    feats = jnp.concatenate([feats[:, :kept], lax.ppermute(feats[:, kept:], "rows", swap)], axis=1)
    lists = jnp.concatenate([pairs, counts[:, None]], axis=1)
    lists = jnp.concatenate([lists[:kept_blocks], lax.ppermute(lists[kept_blocks:], "rows", swap)], axis=0)
    src_feat = feats[:d]
    pairs = lists[:, :npairs]
    counts = lists[:, npairs]
    xt = jnp.transpose(feats)

    grid_spec = pltpu.PrefetchScalarGridSpec(
        num_scalar_prefetch=2,
        grid=(nrb,),
        in_specs=[
            pl.BlockSpec((BLK, d + 1), lambda b, pr, ct: (b, 0)),
            pl.BlockSpec((3, d, KP), lambda b, pr, ct: (0, 0, 0)),
            pl.BlockSpec((8, KP), lambda b, pr, ct: (0, 0)),
            pl.BlockSpec((ncols, rowsp, own_targets), lambda b, pr, ct: (0, 0, 0)),
        ],
        out_specs=[
            pl.BlockSpec((BLK, 1), lambda b, pr, ct: (b, 0)),
            pl.BlockSpec((tblocks, 1, BLK), lambda b, pr, ct: (0, 0, 0)),
            pl.BlockSpec((tblocks, 1, BLK), lambda b, pr, ct: (0, 0, 0)),
        ],
        scratch_shapes=[pltpu.VMEM((8, BLK, BLK), jnp.float32),
                        pltpu.VMEM((BLK, KP), jnp.bfloat16),
                        pltpu.VMEM((BLK, KP), jnp.bfloat16),
                        pltpu.VMEM((4, BLK, LANE), jnp.float32),
                        pltpu.VMEM((tblocks, KP, BLK), jnp.bfloat16)],
    )
    fpot, gtop, gsum = pl.pallas_call(
        functools.partial(sinkhorn_kernel, npairs, d, nbits),
        grid_spec=grid_spec,
        out_shape=[
            jax.ShapeDtypeStruct((ns, 1), jnp.float32),
            jax.ShapeDtypeStruct((tblocks, 1, BLK), jnp.float32),
            jax.ShapeDtypeStruct((tblocks, 1, BLK), jnp.float32),
        ],
        compiler_params=pltpu.CompilerParams(
            dimension_semantics=("arbitrary",), vmem_limit_bytes=100 * 1024 * 1024),
    )(pairs.reshape(-1), counts, xt, expand, sel, gathered)

    done = fpot.reshape(-1)
    src_pot = jnp.concatenate([done[:kept], lax.ppermute(done[kept:], "rows", swap)])
    parts = jnp.stack([gtop.reshape(ncols, own_targets), gsum.reshape(ncols, own_targets)], axis=1)
    mine = lax.all_to_all(parts, "cols", 0, 0, tiled=True)
    top, total = merge(mine[:, 0, :], mine[:, 1, :], 0)
    here = jnp.concatenate([top, total], axis=0)
    there = lax.ppermute(here, "rows", [(0, 1), (1, 0)])
    both = jnp.stack([jnp.where(first, here, there), jnp.where(first, there, here)])
    top, total = merge(both[:, 0, :], both[:, 1, :], 0)
    new_tgt_pot = (-epsilon * LN2) * (top[0] + jnp.log2(total[0]))
    return (src_pot, new_tgt_pot)


def solution(mesh):
    placed = (
        P(None, ("parts", "rows", "cols")),
        P(None, ("parts", "cols")),
        P(("parts", "cols")),
        P(("parts", "rows", "cols")),
        P(("parts", "cols")),
        P(("parts", "rows", "cols"), None),
        P(("parts", "rows", "cols")),
    )
    return jax.shard_map(
        on_device,
        mesh=mesh,
        in_specs=placed,
        out_specs=(P(("parts", "rows", "cols")), P(("parts", "cols"))),
        check_vma=False,
    )
```

```python
import functools

import jax
import jax.numpy as jnp
from jax import lax
from jax.experimental import pallas as pl
from jax.experimental.pallas import tpu as pltpu
from jax.sharding import PartitionSpec as P

BLK = 256
KP = 128
LANE = 128

epsilon = 0.1
NEG = -1e30
LOG2E = 1.4426950408889634
LN2 = 0.6931471805599453


def split3(v):
    first = lax.reduce_precision(v, exponent_bits=8, mantissa_bits=7)
    rest = v - first
    second = lax.reduce_precision(rest, exponent_bits=8, mantissa_bits=7)
    third = rest - second
    return (first.astype(jnp.bfloat16), second.astype(jnp.bfloat16),
            third.astype(jnp.bfloat16))


def split3_kernel(v):
    first = v.astype(jnp.bfloat16)
    rest = v - first.astype(jnp.float32)
    second = rest.astype(jnp.bfloat16)
    third = (rest - second.astype(jnp.float32)).astype(jnp.bfloat16)
    return first, second, third


def build_table(d, nbits, blocks_ref, tab_ref):
    scale = 2.0 * LOG2E / epsilon
    slot_row = lax.broadcasted_iota(jnp.int32, (16, BLK), 0)
    used = 3 * d + 16
    per_col = blocks_ref.shape[2] // BLK

    def one(pos, carry):
        src = 0
        for i in range(nbits):
            src = src + ((pos >> i) & 1) * (1 << (nbits - 1 - i))
        for q in range(per_col):
            blk = blocks_ref[pos, :, q * BLK:(q + 1) * BLK]
            tb = src * per_col + q
            y = blk[0:d, :]
            yn = jnp.sum(y * y, axis=0, keepdims=True)
            tp = blk[d:d + 1, :]
            lt = blk[d + 1:d + 2, :]
            acol = (lt + (tp - yn) / epsilon) * LOG2E
            ccol = (-yn / epsilon) * LOG2E
            y1, y2, y3 = split3_kernel(y * scale)
            for k, piece in enumerate([y1, y2, y1]):
                tab_ref[tb, k * d:(k + 1) * d, :] = piece
            slot = jnp.zeros((16, BLK), jnp.float32)
            pieces = list(split3_kernel(acol)) + list(split3_kernel(ccol))
            for k, piece in enumerate(pieces):
                slot = jnp.where(slot_row == k, piece.astype(jnp.float32), slot)
            slot = jnp.where((slot_row >= 6) & (slot_row < 9), 1.0, slot)
            tab_ref[tb, 3 * d:used, :] = slot.astype(jnp.bfloat16)
            tab_ref[tb, used:KP, :] = jnp.zeros((KP - used, BLK), jnp.bfloat16)
        return carry

    lax.fori_loop(0, blocks_ref.shape[0], one, 0)


def sinkhorn_kernel(npairs, d, nbits, pairs_ref, counts_ref, xt_ref, expand_ref, sel_ref,
                    blocks_ref, fpot_ref, gtop_ref, gsum_ref, sbuf, xr_ref, xc_ref, acc_ref, tab_ref):
    b = pl.program_id(0)

    @pl.when(b == 0)
    def _init():
        gtop_ref[...] = jnp.full(gtop_ref.shape, NEG, jnp.float32)
        gsum_ref[...] = jnp.zeros(gsum_ref.shape, jnp.float32)
        build_table(d, nbits, blocks_ref, tab_ref)

    cnt = counts_ref[b]
    base = b * npairs
    xfull = xt_ref[...]
    xs = xfull[:, :d]
    ls = xfull[:, d:d + 1]
    xn = jnp.sum(xs * xs, axis=1, keepdims=True)
    x1, x2, x3 = split3_kernel(xs)
    xa = (jnp.dot(x1, expand_ref[0], preferred_element_type=jnp.float32)
          + jnp.dot(x2, expand_ref[1], preferred_element_type=jnp.float32)
          + jnp.dot(x3, expand_ref[2], preferred_element_type=jnp.float32))
    sel = sel_ref[...]
    xr_ref[...] = (xa + sel[0:1, :]).astype(jnp.bfloat16)
    for a in range(4):
        acc_ref[2 * a] = jnp.full((BLK, LANE), NEG, jnp.float32)
        acc_ref[2 * a + 1] = jnp.zeros((BLK, LANE), jnp.float32)

    def pairs_of(body):
        def two(k, carry):
            body([2 * k, 2 * k + 1])
            return carry

        lax.fori_loop(0, cnt // 2, two, 0)

        @pl.when(cnt % 2 == 1)
        def _last():
            body([cnt - 1])

    def quads_of(body):
        def four(k, carry):
            body([4 * k + i for i in range(4)])
            return carry

        lax.fori_loop(0, cnt // 4, four, 0)
        done = cnt - cnt % 4

        @pl.when(cnt % 4 >= 2)
        def _pair():
            body([done, done + 1])

        @pl.when(cnt % 2 == 1)
        def _last():
            body([cnt - 1])

    def row_update(ts, a):
        halves = []
        for t in ts:
            s = jnp.dot(xr_ref[...], tab_ref[pairs_ref[base + t]], preferred_element_type=jnp.float32)
            halves += [s[:, :LANE], s[:, LANE:]]
        old = acc_ref[2 * a]
        new = old
        for h in halves:
            new = jnp.maximum(new, h)
        total = acc_ref[2 * a + 1] * jnp.exp2(old - new)
        for h in halves:
            total = total + jnp.exp2(h - new)
        acc_ref[2 * a] = new
        acc_ref[2 * a + 1] = total

    def row_pass(ts):
        for a in range(0, len(ts), 2):
            row_update(ts[a:a + 2], a // 2)

    def col_pass(ts):
        for slot, t in enumerate(ts):
            tb = pairs_ref[base + t]
            u = jnp.dot(xc_ref[...], tab_ref[tb], preferred_element_type=jnp.float32)
            sbuf[slot] = u
            cm = jnp.max(u, axis=0, keepdims=True)
            cs = jnp.sum(jnp.exp2(sbuf[slot] - cm), axis=0, keepdims=True)
            old = gtop_ref[tb]
            new = jnp.maximum(old, cm)
            gsum_ref[tb] = gsum_ref[tb] * jnp.exp2(old - new) + cs * jnp.exp2(cm - new)
            gtop_ref[tb] = new

    def octets_of(body):
        def eight(k, carry):
            body([8 * k + i for i in range(8)])
            return carry

        lax.fori_loop(0, cnt // 8, eight, 0)
        rest = cnt % 8
        start4 = cnt - rest

        @pl.when(rest >= 4)
        def _four():
            body([start4 + i for i in range(4)])

        start2 = start4 + (rest // 4) * 4

        @pl.when(rest % 4 >= 2)
        def _pair():
            body([start2, start2 + 1])

        @pl.when(cnt % 2 == 1)
        def _last():
            body([cnt - 1])

    octets_of(row_pass)
    tops = [acc_ref[2 * a] for a in range(4)]
    lane_top = tops[0]
    for t in tops[1:]:
        lane_top = jnp.maximum(lane_top, t)
    m = jnp.max(lane_top, axis=1, keepdims=True)
    lane_sum = acc_ref[1] * jnp.exp2(tops[0] - m)
    for a in range(1, 4):
        lane_sum = lane_sum + acc_ref[2 * a + 1] * jnp.exp2(tops[a] - m)
    lse = m + jnp.log2(jnp.sum(lane_sum, axis=1, keepdims=True))
    fpot_ref[...] = xn - (epsilon * LN2) * lse
    p1, p2, p3 = split3_kernel(ls * LOG2E - lse)
    xc_ref[...] = (xa + sel[1:2, :] + p1.astype(jnp.float32) * sel[2:3, :]
                   + p2.astype(jnp.float32) * sel[3:4, :]
                   + p3.astype(jnp.float32) * sel[4:5, :]).astype(jnp.bfloat16)

    octets_of(col_pass)


def merge(tops, sums, axis):
    top = jnp.max(tops, axis=axis, keepdims=True)
    total = jnp.sum(sums * jnp.exp2(tops - top), axis=axis, keepdims=True)
    return top, total


def on_device(src_feat, tgt_feat, tgt_pot, log_src, log_tgt, pairs, counts):
    d = src_feat.shape[0]
    ns = src_feat.shape[1]
    nrb = ns // BLK
    npairs = pairs.shape[1]
    own_targets = tgt_feat.shape[1]
    ncols = lax.axis_size("cols")

    packed = jnp.concatenate([tgt_feat, tgt_pot[None, :], log_tgt[None, :]], axis=0)
    rowsp = packed.shape[0]
    nrows = lax.axis_size("rows")
    share = rowsp // nrows
    mine = lax.dynamic_slice_in_dim(packed, lax.axis_index("rows") * share, share, 0)
    halves = mine[None]
    col_index = lax.axis_index("cols")
    nbits = ncols.bit_length() - 1
    for bit in reversed(range(nbits)):
        step = 1 << bit
        partner = lax.ppermute(halves, "cols", [(i, i ^ step) for i in range(ncols)])
        low = (col_index & step) == 0
        halves = jnp.concatenate(
            [jnp.where(low, halves, partner), jnp.where(low, partner, halves)], axis=0)
    other = lax.ppermute(halves, "rows", [(0, 1), (1, 0)])
    first = lax.axis_index("rows") == 0
    gathered = jnp.concatenate(
        [jnp.where(first, halves, other), jnp.where(first, other, halves)], axis=1)
    nt = ncols * own_targets
    tblocks = nt // BLK

    col = jnp.arange(KP, dtype=jnp.int32)[None, :]
    comp = jnp.arange(d, dtype=jnp.int32)[:, None]
    def place(starts):
        hit = jnp.zeros((d, KP), bool)
        for s in starts:
            hit = hit | (col == comp + s)
        return hit.astype(jnp.bfloat16)
    expand = jnp.stack([place([0, d]), place([2 * d]), place([])])
    k0 = 3 * d
    sel = jnp.stack([
        ((col[0] >= k0) & (col[0] < k0 + 3)),
        ((col[0] >= k0 + 3) & (col[0] < k0 + 6)),
        col[0] == k0 + 6, col[0] == k0 + 7, col[0] == k0 + 8,
        col[0] < 0, col[0] < 0, col[0] < 0,
    ]).astype(jnp.float32)

    kept = (nrb // 2) * BLK
    kept_blocks = nrb // 2
    swap = [(0, 1), (1, 0)]
    feats = jnp.concatenate([src_feat, log_src[None, :]], axis=0)
    feats = jnp.concatenate([feats[:, :kept], lax.ppermute(feats[:, kept:], "rows", swap)], axis=1)
    lists = jnp.concatenate([pairs, counts[:, None]], axis=1)
    lists = jnp.concatenate([lists[:kept_blocks], lax.ppermute(lists[kept_blocks:], "rows", swap)], axis=0)
    src_feat = feats[:d]
    pairs = lists[:, :npairs]
    counts = lists[:, npairs]
    xt = jnp.transpose(feats)

    grid_spec = pltpu.PrefetchScalarGridSpec(
        num_scalar_prefetch=2,
        grid=(nrb,),
        in_specs=[
            pl.BlockSpec((BLK, d + 1), lambda b, pr, ct: (b, 0)),
            pl.BlockSpec((3, d, KP), lambda b, pr, ct: (0, 0, 0)),
            pl.BlockSpec((8, KP), lambda b, pr, ct: (0, 0)),
            pl.BlockSpec((ncols, rowsp, own_targets), lambda b, pr, ct: (0, 0, 0)),
        ],
        out_specs=[
            pl.BlockSpec((BLK, 1), lambda b, pr, ct: (b, 0)),
            pl.BlockSpec((tblocks, 1, BLK), lambda b, pr, ct: (0, 0, 0)),
            pl.BlockSpec((tblocks, 1, BLK), lambda b, pr, ct: (0, 0, 0)),
        ],
        scratch_shapes=[pltpu.VMEM((8, BLK, BLK), jnp.float32),
                        pltpu.VMEM((BLK, KP), jnp.bfloat16),
                        pltpu.VMEM((BLK, KP), jnp.bfloat16),
                        pltpu.VMEM((8, BLK, LANE), jnp.float32),
                        pltpu.VMEM((tblocks, KP, BLK), jnp.bfloat16)],
    )
    fpot, gtop, gsum = pl.pallas_call(
        functools.partial(sinkhorn_kernel, npairs, d, nbits),
        grid_spec=grid_spec,
        out_shape=[
            jax.ShapeDtypeStruct((ns, 1), jnp.float32),
            jax.ShapeDtypeStruct((tblocks, 1, BLK), jnp.float32),
            jax.ShapeDtypeStruct((tblocks, 1, BLK), jnp.float32),
        ],
        compiler_params=pltpu.CompilerParams(
            dimension_semantics=("arbitrary",), vmem_limit_bytes=100 * 1024 * 1024),
    )(pairs.reshape(-1), counts, xt, expand, sel, gathered)

    done = fpot.reshape(-1)
    src_pot = jnp.concatenate([done[:kept], lax.ppermute(done[kept:], "rows", swap)])
    parts = jnp.stack([gtop.reshape(ncols, own_targets), gsum.reshape(ncols, own_targets)], axis=1)
    mine = lax.all_to_all(parts, "cols", 0, 0, tiled=True)
    top, total = merge(mine[:, 0, :], mine[:, 1, :], 0)
    here = jnp.concatenate([top, total], axis=0)
    there = lax.ppermute(here, "rows", [(0, 1), (1, 0)])
    both = jnp.stack([jnp.where(first, here, there), jnp.where(first, there, here)])
    top, total = merge(both[:, 0, :], both[:, 1, :], 0)
    new_tgt_pot = (-epsilon * LN2) * (top[0] + jnp.log2(total[0]))
    return (src_pot, new_tgt_pot)


def solution(mesh):
    placed = (
        P(None, ("parts", "rows", "cols")),
        P(None, ("parts", "cols")),
        P(("parts", "cols")),
        P(("parts", "rows", "cols")),
        P(("parts", "cols")),
        P(("parts", "rows", "cols"), None),
        P(("parts", "rows", "cols")),
    )
    return jax.shard_map(
        on_device,
        mesh=mesh,
        in_specs=placed,
        out_specs=(P(("parts", "rows", "cols")), P(("parts", "cols"))),
        check_vma=False,
    )
```

```python
import functools

import jax
import jax.numpy as jnp
from jax import lax
from jax.experimental import pallas as pl
from jax.experimental.pallas import tpu as pltpu
from jax.sharding import PartitionSpec as P

BLK = 256
KP = 128
LANE = 128

epsilon = 0.1
NEG = -1e30
LOG2E = 1.4426950408889634
LN2 = 0.6931471805599453


def split3(v):
    first = lax.reduce_precision(v, exponent_bits=8, mantissa_bits=7)
    rest = v - first
    second = lax.reduce_precision(rest, exponent_bits=8, mantissa_bits=7)
    third = rest - second
    return (first.astype(jnp.bfloat16), second.astype(jnp.bfloat16),
            third.astype(jnp.bfloat16))


def split3_kernel(v):
    first = v.astype(jnp.bfloat16)
    rest = v - first.astype(jnp.float32)
    second = rest.astype(jnp.bfloat16)
    third = (rest - second.astype(jnp.float32)).astype(jnp.bfloat16)
    return first, second, third


def build_table(d, nbits, blocks_ref, tab_ref):
    scale = 2.0 * LOG2E / epsilon
    slot_row = lax.broadcasted_iota(jnp.int32, (16, BLK), 0)
    used = 3 * d + 16
    per_col = blocks_ref.shape[2] // BLK

    def one(pos, carry):
        src = 0
        for i in range(nbits):
            src = src + ((pos >> i) & 1) * (1 << (nbits - 1 - i))
        for q in range(per_col):
            blk = blocks_ref[pos, :, q * BLK:(q + 1) * BLK]
            tb = src * per_col + q
            y = blk[0:d, :]
            yn = jnp.sum(y * y, axis=0, keepdims=True)
            tp = blk[d:d + 1, :]
            lt = blk[d + 1:d + 2, :]
            acol = (lt + (tp - yn) / epsilon) * LOG2E
            ccol = (-yn / epsilon) * LOG2E
            y1, y2, y3 = split3_kernel(y * scale)
            for k, piece in enumerate([y1, y2, y1]):
                tab_ref[tb, k * d:(k + 1) * d, :] = piece
            slot = jnp.zeros((16, BLK), jnp.float32)
            pieces = list(split3_kernel(acol)) + list(split3_kernel(ccol))
            for k, piece in enumerate(pieces):
                slot = jnp.where(slot_row == k, piece.astype(jnp.float32), slot)
            slot = jnp.where((slot_row >= 6) & (slot_row < 9), 1.0, slot)
            tab_ref[tb, 3 * d:used, :] = slot.astype(jnp.bfloat16)
            tab_ref[tb, used:KP, :] = jnp.zeros((KP - used, BLK), jnp.bfloat16)
        return carry

    lax.fori_loop(0, blocks_ref.shape[0], one, 0)


def sinkhorn_kernel(npairs, d, nbits, pairs_ref, counts_ref, xt_ref, expand_ref, sel_ref,
                    blocks_ref, fpot_ref, gtop_ref, gsum_ref, sbuf, xr_ref, xc_ref, acc_ref, tab_ref):
    b = pl.program_id(0)

    @pl.when(b == 0)
    def _init():
        gtop_ref[...] = jnp.full(gtop_ref.shape, NEG, jnp.float32)
        gsum_ref[...] = jnp.zeros(gsum_ref.shape, jnp.float32)
        build_table(d, nbits, blocks_ref, tab_ref)

    cnt = counts_ref[b]
    base = b * npairs
    xfull = xt_ref[...]
    xs = xfull[:, :d]
    ls = xfull[:, d:d + 1]
    xn = jnp.sum(xs * xs, axis=1, keepdims=True)
    x1, x2, x3 = split3_kernel(xs)
    xa = (jnp.dot(x1, expand_ref[0], preferred_element_type=jnp.float32)
          + jnp.dot(x2, expand_ref[1], preferred_element_type=jnp.float32)
          + jnp.dot(x3, expand_ref[2], preferred_element_type=jnp.float32))
    sel = sel_ref[...]
    xr_ref[...] = (xa + sel[0:1, :]).astype(jnp.bfloat16)
    for a in range(4):
        acc_ref[2 * a] = jnp.full((BLK, LANE), NEG, jnp.float32)
        acc_ref[2 * a + 1] = jnp.zeros((BLK, LANE), jnp.float32)

    def pairs_of(body):
        def two(k, carry):
            body([2 * k, 2 * k + 1])
            return carry

        lax.fori_loop(0, cnt // 2, two, 0)

        @pl.when(cnt % 2 == 1)
        def _last():
            body([cnt - 1])

    def quads_of(body):
        def four(k, carry):
            body([4 * k + i for i in range(4)])
            return carry

        lax.fori_loop(0, cnt // 4, four, 0)
        done = cnt - cnt % 4

        @pl.when(cnt % 4 >= 2)
        def _pair():
            body([done, done + 1])

        @pl.when(cnt % 2 == 1)
        def _last():
            body([cnt - 1])

    def row_update(ts, a):
        halves = []
        for t in ts:
            s = jnp.dot(xr_ref[...], tab_ref[pairs_ref[base + t]], preferred_element_type=jnp.float32)
            halves += [s[:, :LANE], s[:, LANE:]]
        old = acc_ref[2 * a]
        new = old
        for h in halves:
            new = jnp.maximum(new, h)
        total = acc_ref[2 * a + 1] * jnp.exp2(old - new)
        for h in halves:
            total = total + jnp.exp2(h - new)
        acc_ref[2 * a] = new
        acc_ref[2 * a + 1] = total

    def row_pass(ts):
        for a in range(0, len(ts), 2):
            row_update(ts[a:a + 2], a // 2)

    def col_pass(ts):
        for slot, t in enumerate(ts):
            tb = pairs_ref[base + t]
            u = jnp.dot(xc_ref[...], tab_ref[tb], preferred_element_type=jnp.float32)
            sbuf[slot] = u
            cm = jnp.max(u, axis=0, keepdims=True)
            cs = jnp.sum(jnp.exp2(sbuf[slot] - cm), axis=0, keepdims=True)
            old = gtop_ref[tb]
            new = jnp.maximum(old, cm)
            gsum_ref[tb] = gsum_ref[tb] * jnp.exp2(old - new) + cs * jnp.exp2(cm - new)
            gtop_ref[tb] = new

    def octets_of(body):
        def eight(k, carry):
            body([8 * k + i for i in range(8)])
            return carry

        lax.fori_loop(0, cnt // 8, eight, 0)
        rest = cnt % 8
        start4 = cnt - rest

        @pl.when(rest >= 4)
        def _four():
            body([start4 + i for i in range(4)])

        start2 = start4 + (rest // 4) * 4

        @pl.when(rest % 4 >= 2)
        def _pair():
            body([start2, start2 + 1])

        @pl.when(cnt % 2 == 1)
        def _last():
            body([cnt - 1])

    octets_of(row_pass)
    tops = [acc_ref[2 * a] for a in range(4)]
    lane_top = tops[0]
    for t in tops[1:]:
        lane_top = jnp.maximum(lane_top, t)
    m = jnp.max(lane_top, axis=1, keepdims=True)
    lane_sum = acc_ref[1] * jnp.exp2(tops[0] - m)
    for a in range(1, 4):
        lane_sum = lane_sum + acc_ref[2 * a + 1] * jnp.exp2(tops[a] - m)
    lse = m + jnp.log2(jnp.sum(lane_sum, axis=1, keepdims=True))
    fpot_ref[...] = xn - (epsilon * LN2) * lse
    p1, p2, p3 = split3_kernel(ls * LOG2E - lse)
    xc_ref[...] = (xa + sel[1:2, :] + p1.astype(jnp.float32) * sel[2:3, :]
                   + p2.astype(jnp.float32) * sel[3:4, :]
                   + p3.astype(jnp.float32) * sel[4:5, :]).astype(jnp.bfloat16)

    def dozens_of(body):
        def twelve(k, carry):
            body([12 * k + i for i in range(12)])
            return carry

        lax.fori_loop(0, cnt // 12, twelve, 0)
        start = cnt - cnt % 12
        for size in (8, 4, 2, 1):
            left = cnt - start

            @pl.when(left >= size)
            def _part(start=start, size=size):
                body([start + i for i in range(size)])

            start = start + jnp.where(left >= size, size, 0)

    dozens_of(col_pass)


def merge(tops, sums, axis):
    top = jnp.max(tops, axis=axis, keepdims=True)
    total = jnp.sum(sums * jnp.exp2(tops - top), axis=axis, keepdims=True)
    return top, total


def on_device(src_feat, tgt_feat, tgt_pot, log_src, log_tgt, pairs, counts):
    d = src_feat.shape[0]
    ns = src_feat.shape[1]
    nrb = ns // BLK
    npairs = pairs.shape[1]
    own_targets = tgt_feat.shape[1]
    ncols = lax.axis_size("cols")

    packed = jnp.concatenate([tgt_feat, tgt_pot[None, :], log_tgt[None, :]], axis=0)
    rowsp = packed.shape[0]
    nrows = lax.axis_size("rows")
    share = rowsp // nrows
    mine = lax.dynamic_slice_in_dim(packed, lax.axis_index("rows") * share, share, 0)
    halves = mine[None]
    col_index = lax.axis_index("cols")
    nbits = ncols.bit_length() - 1
    for bit in reversed(range(nbits)):
        step = 1 << bit
        partner = lax.ppermute(halves, "cols", [(i, i ^ step) for i in range(ncols)])
        low = (col_index & step) == 0
        halves = jnp.concatenate(
            [jnp.where(low, halves, partner), jnp.where(low, partner, halves)], axis=0)
    other = lax.ppermute(halves, "rows", [(0, 1), (1, 0)])
    first = lax.axis_index("rows") == 0
    gathered = jnp.concatenate(
        [jnp.where(first, halves, other), jnp.where(first, other, halves)], axis=1)
    nt = ncols * own_targets
    tblocks = nt // BLK

    col = jnp.arange(KP, dtype=jnp.int32)[None, :]
    comp = jnp.arange(d, dtype=jnp.int32)[:, None]
    def place(starts):
        hit = jnp.zeros((d, KP), bool)
        for s in starts:
            hit = hit | (col == comp + s)
        return hit.astype(jnp.bfloat16)
    expand = jnp.stack([place([0, d]), place([2 * d]), place([])])
    k0 = 3 * d
    sel = jnp.stack([
        ((col[0] >= k0) & (col[0] < k0 + 3)),
        ((col[0] >= k0 + 3) & (col[0] < k0 + 6)),
        col[0] == k0 + 6, col[0] == k0 + 7, col[0] == k0 + 8,
        col[0] < 0, col[0] < 0, col[0] < 0,
    ]).astype(jnp.float32)

    kept = (nrb // 2) * BLK
    kept_blocks = nrb // 2
    swap = [(0, 1), (1, 0)]
    feats = jnp.concatenate([src_feat, log_src[None, :]], axis=0)
    feats = jnp.concatenate([feats[:, :kept], lax.ppermute(feats[:, kept:], "rows", swap)], axis=1)
    lists = jnp.concatenate([pairs, counts[:, None]], axis=1)
    lists = jnp.concatenate([lists[:kept_blocks], lax.ppermute(lists[kept_blocks:], "rows", swap)], axis=0)
    src_feat = feats[:d]
    pairs = lists[:, :npairs]
    counts = lists[:, npairs]
    xt = jnp.transpose(feats)

    grid_spec = pltpu.PrefetchScalarGridSpec(
        num_scalar_prefetch=2,
        grid=(nrb,),
        in_specs=[
            pl.BlockSpec((BLK, d + 1), lambda b, pr, ct: (b, 0)),
            pl.BlockSpec((3, d, KP), lambda b, pr, ct: (0, 0, 0)),
            pl.BlockSpec((8, KP), lambda b, pr, ct: (0, 0)),
            pl.BlockSpec((ncols, rowsp, own_targets), lambda b, pr, ct: (0, 0, 0)),
        ],
        out_specs=[
            pl.BlockSpec((BLK, 1), lambda b, pr, ct: (b, 0)),
            pl.BlockSpec((tblocks, 1, BLK), lambda b, pr, ct: (0, 0, 0)),
            pl.BlockSpec((tblocks, 1, BLK), lambda b, pr, ct: (0, 0, 0)),
        ],
        scratch_shapes=[pltpu.VMEM((12, BLK, BLK), jnp.float32),
                        pltpu.VMEM((BLK, KP), jnp.bfloat16),
                        pltpu.VMEM((BLK, KP), jnp.bfloat16),
                        pltpu.VMEM((8, BLK, LANE), jnp.float32),
                        pltpu.VMEM((tblocks, KP, BLK), jnp.bfloat16)],
    )
    fpot, gtop, gsum = pl.pallas_call(
        functools.partial(sinkhorn_kernel, npairs, d, nbits),
        grid_spec=grid_spec,
        out_shape=[
            jax.ShapeDtypeStruct((ns, 1), jnp.float32),
            jax.ShapeDtypeStruct((tblocks, 1, BLK), jnp.float32),
            jax.ShapeDtypeStruct((tblocks, 1, BLK), jnp.float32),
        ],
        compiler_params=pltpu.CompilerParams(
            dimension_semantics=("arbitrary",), vmem_limit_bytes=100 * 1024 * 1024),
    )(pairs.reshape(-1), counts, xt, expand, sel, gathered)

    done = fpot.reshape(-1)
    src_pot = jnp.concatenate([done[:kept], lax.ppermute(done[kept:], "rows", swap)])
    parts = jnp.stack([gtop.reshape(ncols, own_targets), gsum.reshape(ncols, own_targets)], axis=1)
    mine = lax.all_to_all(parts, "cols", 0, 0, tiled=True)
    top, total = merge(mine[:, 0, :], mine[:, 1, :], 0)
    here = jnp.concatenate([top, total], axis=0)
    there = lax.ppermute(here, "rows", [(0, 1), (1, 0)])
    both = jnp.stack([jnp.where(first, here, there), jnp.where(first, there, here)])
    top, total = merge(both[:, 0, :], both[:, 1, :], 0)
    new_tgt_pot = (-epsilon * LN2) * (top[0] + jnp.log2(total[0]))
    return (src_pot, new_tgt_pot)


def solution(mesh):
    placed = (
        P(None, ("parts", "rows", "cols")),
        P(None, ("parts", "cols")),
        P(("parts", "cols")),
        P(("parts", "rows", "cols")),
        P(("parts", "cols")),
        P(("parts", "rows", "cols"), None),
        P(("parts", "rows", "cols")),
    )
    return jax.shard_map(
        on_device,
        mesh=mesh,
        in_specs=placed,
        out_specs=(P(("parts", "rows", "cols")), P(("parts", "cols"))),
        check_vma=False,
    )
```

```python
import functools

import jax
import jax.numpy as jnp
from jax import lax
from jax.experimental import pallas as pl
from jax.experimental.pallas import tpu as pltpu
from jax.sharding import PartitionSpec as P

BLK = 256
KP = 128
LANE = 128

epsilon = 0.1
NEG = -1e30
LOG2E = 1.4426950408889634
LN2 = 0.6931471805599453


def split3(v):
    first = lax.reduce_precision(v, exponent_bits=8, mantissa_bits=7)
    rest = v - first
    second = lax.reduce_precision(rest, exponent_bits=8, mantissa_bits=7)
    third = rest - second
    return (first.astype(jnp.bfloat16), second.astype(jnp.bfloat16),
            third.astype(jnp.bfloat16))


def split3_kernel(v):
    first = v.astype(jnp.bfloat16)
    rest = v - first.astype(jnp.float32)
    second = rest.astype(jnp.bfloat16)
    third = (rest - second.astype(jnp.float32)).astype(jnp.bfloat16)
    return first, second, third


def build_table(d, nbits, blocks_ref, tab_ref):
    scale = 2.0 * LOG2E / epsilon
    slot_row = lax.broadcasted_iota(jnp.int32, (16, BLK), 0)
    used = 3 * d + 16
    per_col = blocks_ref.shape[2] // BLK

    def one(pos, carry):
        src = 0
        for i in range(nbits):
            src = src + ((pos >> i) & 1) * (1 << (nbits - 1 - i))
        for q in range(per_col):
            blk = blocks_ref[pos, :, q * BLK:(q + 1) * BLK]
            tb = src * per_col + q
            y = blk[0:d, :]
            yn = jnp.sum(y * y, axis=0, keepdims=True)
            tp = blk[d:d + 1, :]
            lt = blk[d + 1:d + 2, :]
            acol = (lt + (tp - yn) / epsilon) * LOG2E
            ccol = (-yn / epsilon) * LOG2E
            y1, y2, y3 = split3_kernel(y * scale)
            for k, piece in enumerate([y1, y2, y1]):
                tab_ref[tb, k * d:(k + 1) * d, :] = piece
            slot = jnp.zeros((16, BLK), jnp.float32)
            pieces = list(split3_kernel(acol)) + list(split3_kernel(ccol))
            for k, piece in enumerate(pieces):
                slot = jnp.where(slot_row == k, piece.astype(jnp.float32), slot)
            slot = jnp.where((slot_row >= 6) & (slot_row < 9), 1.0, slot)
            tab_ref[tb, 3 * d:used, :] = slot.astype(jnp.bfloat16)
            tab_ref[tb, used:KP, :] = jnp.zeros((KP - used, BLK), jnp.bfloat16)
        return carry

    lax.fori_loop(0, blocks_ref.shape[0], one, 0)


def sinkhorn_kernel(npairs, d, nbits, pairs_ref, counts_ref, xt_ref, expand_ref, sel_ref,
                    blocks_ref, fpot_ref, gtop_ref, gsum_ref, sbuf, xr_ref, xc_ref, acc_ref, tab_ref):
    b = pl.program_id(0)

    @pl.when(b == 0)
    def _init():
        gtop_ref[...] = jnp.full(gtop_ref.shape, NEG, jnp.float32)
        gsum_ref[...] = jnp.zeros(gsum_ref.shape, jnp.float32)
        build_table(d, nbits, blocks_ref, tab_ref)

    cnt = counts_ref[b]
    base = b * npairs
    xfull = xt_ref[...]
    xs = xfull[:, :d]
    ls = xfull[:, d:d + 1]
    xn = jnp.sum(xs * xs, axis=1, keepdims=True)
    x1, x2, x3 = split3_kernel(xs)
    xa = (jnp.dot(x1, expand_ref[0], preferred_element_type=jnp.float32)
          + jnp.dot(x2, expand_ref[1], preferred_element_type=jnp.float32)
          + jnp.dot(x3, expand_ref[2], preferred_element_type=jnp.float32))
    sel = sel_ref[...]
    xr_ref[...] = (xa + sel[0:1, :]).astype(jnp.bfloat16)
    for a in range(6):
        acc_ref[2 * a] = jnp.full((BLK, LANE), NEG, jnp.float32)
        acc_ref[2 * a + 1] = jnp.zeros((BLK, LANE), jnp.float32)

    def pairs_of(body):
        def two(k, carry):
            body([2 * k, 2 * k + 1])
            return carry

        lax.fori_loop(0, cnt // 2, two, 0)

        @pl.when(cnt % 2 == 1)
        def _last():
            body([cnt - 1])

    def quads_of(body):
        def four(k, carry):
            body([4 * k + i for i in range(4)])
            return carry

        lax.fori_loop(0, cnt // 4, four, 0)
        done = cnt - cnt % 4

        @pl.when(cnt % 4 >= 2)
        def _pair():
            body([done, done + 1])

        @pl.when(cnt % 2 == 1)
        def _last():
            body([cnt - 1])

    def row_update(ts, a):
        halves = []
        for t in ts:
            s = jnp.dot(xr_ref[...], tab_ref[pairs_ref[base + t]], preferred_element_type=jnp.float32)
            halves += [s[:, :LANE], s[:, LANE:]]
        old = acc_ref[2 * a]
        new = old
        for h in halves:
            new = jnp.maximum(new, h)
        total = acc_ref[2 * a + 1] * jnp.exp2(old - new)
        for h in halves:
            total = total + jnp.exp2(h - new)
        acc_ref[2 * a] = new
        acc_ref[2 * a + 1] = total

    def row_pass(ts):
        for a in range(0, len(ts), 2):
            row_update(ts[a:a + 2], a // 2)

    def col_pass(ts):
        for slot, t in enumerate(ts):
            tb = pairs_ref[base + t]
            u = jnp.dot(xc_ref[...], tab_ref[tb], preferred_element_type=jnp.float32)
            sbuf[slot] = u
            cm = jnp.max(u, axis=0, keepdims=True)
            cs = jnp.sum(jnp.exp2(sbuf[slot] - cm), axis=0, keepdims=True)
            old = gtop_ref[tb]
            new = jnp.maximum(old, cm)
            gsum_ref[tb] = gsum_ref[tb] * jnp.exp2(old - new) + cs * jnp.exp2(cm - new)
            gtop_ref[tb] = new

    def octets_of(body):
        def eight(k, carry):
            body([8 * k + i for i in range(8)])
            return carry

        lax.fori_loop(0, cnt // 8, eight, 0)
        rest = cnt % 8
        start4 = cnt - rest

        @pl.when(rest >= 4)
        def _four():
            body([start4 + i for i in range(4)])

        start2 = start4 + (rest // 4) * 4

        @pl.when(rest % 4 >= 2)
        def _pair():
            body([start2, start2 + 1])

        @pl.when(cnt % 2 == 1)
        def _last():
            body([cnt - 1])

    def dozens_of(body):
        def twelve(k, carry):
            body([12 * k + i for i in range(12)])
            return carry

        lax.fori_loop(0, cnt // 12, twelve, 0)
        start = cnt - cnt % 12
        for size in (8, 4, 2, 1):
            left = cnt - start

            @pl.when(left >= size)
            def _part(start=start, size=size):
                body([start + i for i in range(size)])

            start = start + jnp.where(left >= size, size, 0)

    dozens_of(row_pass)
    tops = [acc_ref[2 * a] for a in range(6)]
    lane_top = tops[0]
    for t in tops[1:]:
        lane_top = jnp.maximum(lane_top, t)
    m = jnp.max(lane_top, axis=1, keepdims=True)
    lane_sum = acc_ref[1] * jnp.exp2(tops[0] - m)
    for a in range(1, 6):
        lane_sum = lane_sum + acc_ref[2 * a + 1] * jnp.exp2(tops[a] - m)
    lse = m + jnp.log2(jnp.sum(lane_sum, axis=1, keepdims=True))
    fpot_ref[...] = xn - (epsilon * LN2) * lse
    p1, p2, p3 = split3_kernel(ls * LOG2E - lse)
    xc_ref[...] = (xa + sel[1:2, :] + p1.astype(jnp.float32) * sel[2:3, :]
                   + p2.astype(jnp.float32) * sel[3:4, :]
                   + p3.astype(jnp.float32) * sel[4:5, :]).astype(jnp.bfloat16)

    dozens_of(col_pass)


def merge(tops, sums, axis):
    top = jnp.max(tops, axis=axis, keepdims=True)
    total = jnp.sum(sums * jnp.exp2(tops - top), axis=axis, keepdims=True)
    return top, total


def on_device(src_feat, tgt_feat, tgt_pot, log_src, log_tgt, pairs, counts):
    d = src_feat.shape[0]
    ns = src_feat.shape[1]
    nrb = ns // BLK
    npairs = pairs.shape[1]
    own_targets = tgt_feat.shape[1]
    ncols = lax.axis_size("cols")

    packed = jnp.concatenate([tgt_feat, tgt_pot[None, :], log_tgt[None, :]], axis=0)
    rowsp = packed.shape[0]
    nrows = lax.axis_size("rows")
    share = rowsp // nrows
    mine = lax.dynamic_slice_in_dim(packed, lax.axis_index("rows") * share, share, 0)
    halves = mine[None]
    col_index = lax.axis_index("cols")
    nbits = ncols.bit_length() - 1
    for bit in reversed(range(nbits)):
        step = 1 << bit
        partner = lax.ppermute(halves, "cols", [(i, i ^ step) for i in range(ncols)])
        low = (col_index & step) == 0
        halves = jnp.concatenate(
            [jnp.where(low, halves, partner), jnp.where(low, partner, halves)], axis=0)
    other = lax.ppermute(halves, "rows", [(0, 1), (1, 0)])
    first = lax.axis_index("rows") == 0
    gathered = jnp.concatenate(
        [jnp.where(first, halves, other), jnp.where(first, other, halves)], axis=1)
    nt = ncols * own_targets
    tblocks = nt // BLK

    col = jnp.arange(KP, dtype=jnp.int32)[None, :]
    comp = jnp.arange(d, dtype=jnp.int32)[:, None]
    def place(starts):
        hit = jnp.zeros((d, KP), bool)
        for s in starts:
            hit = hit | (col == comp + s)
        return hit.astype(jnp.bfloat16)
    expand = jnp.stack([place([0, d]), place([2 * d]), place([])])
    k0 = 3 * d
    sel = jnp.stack([
        ((col[0] >= k0) & (col[0] < k0 + 3)),
        ((col[0] >= k0 + 3) & (col[0] < k0 + 6)),
        col[0] == k0 + 6, col[0] == k0 + 7, col[0] == k0 + 8,
        col[0] < 0, col[0] < 0, col[0] < 0,
    ]).astype(jnp.float32)

    kept = (nrb // 2) * BLK
    kept_blocks = nrb // 2
    swap = [(0, 1), (1, 0)]
    feats = jnp.concatenate([src_feat, log_src[None, :]], axis=0)
    feats = jnp.concatenate([feats[:, :kept], lax.ppermute(feats[:, kept:], "rows", swap)], axis=1)
    lists = jnp.concatenate([pairs, counts[:, None]], axis=1)
    lists = jnp.concatenate([lists[:kept_blocks], lax.ppermute(lists[kept_blocks:], "rows", swap)], axis=0)
    src_feat = feats[:d]
    pairs = lists[:, :npairs]
    counts = lists[:, npairs]
    xt = jnp.transpose(feats)

    grid_spec = pltpu.PrefetchScalarGridSpec(
        num_scalar_prefetch=2,
        grid=(nrb,),
        in_specs=[
            pl.BlockSpec((BLK, d + 1), lambda b, pr, ct: (b, 0)),
            pl.BlockSpec((3, d, KP), lambda b, pr, ct: (0, 0, 0)),
            pl.BlockSpec((8, KP), lambda b, pr, ct: (0, 0)),
            pl.BlockSpec((ncols, rowsp, own_targets), lambda b, pr, ct: (0, 0, 0)),
        ],
        out_specs=[
            pl.BlockSpec((BLK, 1), lambda b, pr, ct: (b, 0)),
            pl.BlockSpec((tblocks, 1, BLK), lambda b, pr, ct: (0, 0, 0)),
            pl.BlockSpec((tblocks, 1, BLK), lambda b, pr, ct: (0, 0, 0)),
        ],
        scratch_shapes=[pltpu.VMEM((12, BLK, BLK), jnp.float32),
                        pltpu.VMEM((BLK, KP), jnp.bfloat16),
                        pltpu.VMEM((BLK, KP), jnp.bfloat16),
                        pltpu.VMEM((12, BLK, LANE), jnp.float32),
                        pltpu.VMEM((tblocks, KP, BLK), jnp.bfloat16)],
    )
    fpot, gtop, gsum = pl.pallas_call(
        functools.partial(sinkhorn_kernel, npairs, d, nbits),
        grid_spec=grid_spec,
        out_shape=[
            jax.ShapeDtypeStruct((ns, 1), jnp.float32),
            jax.ShapeDtypeStruct((tblocks, 1, BLK), jnp.float32),
            jax.ShapeDtypeStruct((tblocks, 1, BLK), jnp.float32),
        ],
        compiler_params=pltpu.CompilerParams(
            dimension_semantics=("arbitrary",), vmem_limit_bytes=100 * 1024 * 1024),
    )(pairs.reshape(-1), counts, xt, expand, sel, gathered)

    done = fpot.reshape(-1)
    src_pot = jnp.concatenate([done[:kept], lax.ppermute(done[kept:], "rows", swap)])
    parts = jnp.stack([gtop.reshape(ncols, own_targets), gsum.reshape(ncols, own_targets)], axis=1)
    mine = lax.all_to_all(parts, "cols", 0, 0, tiled=True)
    top, total = merge(mine[:, 0, :], mine[:, 1, :], 0)
    here = jnp.concatenate([top, total], axis=0)
    there = lax.ppermute(here, "rows", [(0, 1), (1, 0)])
    both = jnp.stack([jnp.where(first, here, there), jnp.where(first, there, here)])
    top, total = merge(both[:, 0, :], both[:, 1, :], 0)
    new_tgt_pot = (-epsilon * LN2) * (top[0] + jnp.log2(total[0]))
    return (src_pot, new_tgt_pot)


def solution(mesh):
    placed = (
        P(None, ("parts", "rows", "cols")),
        P(None, ("parts", "cols")),
        P(("parts", "cols")),
        P(("parts", "rows", "cols")),
        P(("parts", "cols")),
        P(("parts", "rows", "cols"), None),
        P(("parts", "rows", "cols")),
    )
    return jax.shard_map(
        on_device,
        mesh=mesh,
        in_specs=placed,
        out_specs=(P(("parts", "rows", "cols")), P(("parts", "cols"))),
        check_vma=False,
    )
```
